32 devices in a mesh: groups: 2 (over x), seq: 16 (over z, y, core).
Axes of the slice: x: 2, y: 2, z: 4, core: 2. Of those that a mesh axis runs over, the one named last changes fastest.
Arguments:
- query_feats: bfloat16 [16384, 2560], P(('groups', 'seq')), parts along dimension 0, may hold values from -10 to 10
- key_feats: bfloat16 [16384, 2560], P(('groups', 'seq')), parts along dimension 0, may hold values from -10 to 10
- value_feats: bfloat16 [16384, 2560], P(('groups', 'seq')), parts along dimension 0, may hold values from -6 to 6
- owner_map: int32 [256], P('groups'), parts along dimension 0, may hold values from 0 to 15, as said below
- pattern: int32 [256, 23], P('groups'), parts along dimension 0, may hold values from 0 to 127, as said below
Outputs:
- attended: bfloat16 [16384, 2560], P(('groups', 'seq')), parts along dimension 0
- log_sums: float32 [32, 8, 1280], P(('groups', 'seq')), parts along dimension 0
The draws below stay inside these ranges and needn't reach their ends.
There are 2 independent parts, one for each index of `groups`. The reference program is written for one: setup_inputs(seed, part) draws one part's arguments, and reference() takes and returns one part's arrays. A program takes and returns all parts, laid end to end along the dimension named above; each array names one. Nothing has to cross between parts.
Inputs may be any that keep to these rules, and one draw needn't show every extreme that they name: `owner_map`: each device owns exactly 8 tiles. In every block of 32 consecutive tile numbers each device owns at least one tile and at most 2, and some device owns exactly 2. `pattern`: row t holds 23 different tiles: all 8 tiles owned by the owner of tile t, and 15 tiles owned by other devices. Over all query tiles owned by one device, the listed tiles of other devices are exactly one tile of each other device; at most 4 of them lie in one block of 32 consecutive tile numbers, and exactly 4 in every such block but one.
All inputs are finite; a program needn't handle non-finite values.
Results may differ from the reference program's by a relative error of at most 0.005.
Values may be sent and summed in bfloat16 or wider, within the bound.
No kernel may reach another device: no remote copies, remote signals or barrier semaphores. Data moves between devices by JAX's collectives and lax.ppermute only.
A program may use at most 192 MiB of HBM per device.

```python
import math
import jax
import jax.numpy as jnp
from jax import lax

HEADS = 20
HEAD_DIM = 128
CHANNELS = 2560
WIDTH = 64
HEIGHT = 8
BANDS = 4
PIECES = 32
TOKENS = 8192
TILES = 128
OWN = 8
SLOTS = 4
FAR_SEL = 15
SELECTED = 23
STRIDE = 1
N_SEQ = 16


def plan_tables(key):
    base_key = jax.random.fold_in(key, 7)
    class_count = TILES // PIECES
    device_order = jax.random.permutation(jax.random.fold_in(base_key, 1), N_SEQ).astype(jnp.int32)
    order_inverse = jnp.argsort(device_order).astype(jnp.int32)
    class_keys = jax.random.split(jax.random.fold_in(base_key, 2), class_count)
    shuffle = jax.vmap(lambda part_key: jax.random.permutation(part_key, PIECES))(class_keys).astype(jnp.int32)
    class_iota = jnp.arange(class_count, dtype=jnp.int32)
    position = class_iota[:, None] * PIECES + jnp.arange(PIECES, dtype=jnp.int32)[None, :]
    tile_at = class_iota[:, None] * PIECES + shuffle
    owners = jnp.zeros((TILES,), jnp.int32).at[tile_at.reshape(-1)].set(device_order[position.reshape(-1) % N_SEQ])
    user_ids = jnp.arange(N_SEQ, dtype=jnp.int32)
    band_keys = jax.random.split(jax.random.fold_in(base_key, 3), N_SEQ)
    band_of = (jax.vmap(lambda part_key: jax.random.permutation(part_key, N_SEQ))(band_keys) // SLOTS).astype(jnp.int32)
    first_place = (order_inverse[None, :] - band_of * PIECES) % N_SEQ
    place_counts = (PIECES - 1 - first_place) // N_SEQ + 1
    extra_step = jax.random.randint(jax.random.fold_in(base_key, 4), (N_SEQ, N_SEQ), 0, 1 << 20) % place_counts
    chosen_place = first_place + extra_step * N_SEQ
    far_tile = (band_of * PIECES + shuffle[band_of, chosen_place]).astype(jnp.int32)
    onehot = (owners[:, None] == user_ids[None, :]).astype(jnp.int32)
    running = jnp.cumsum(onehot, axis=0)
    own_rank = jnp.sum(onehot * running, axis=1) - 1
    slot_iota = jnp.arange(OWN, dtype=jnp.int32)
    tile_iota = jnp.arange(TILES, dtype=jnp.int32)
    match_rows = (owners[None, None, :] == user_ids[:, None, None]) & (own_rank[None, None, :] == slot_iota[None, :, None])
    own_list = jnp.sum(jnp.where(match_rows, tile_iota[None, None, :], 0), axis=2).astype(jnp.int32)
    other_keys = jax.random.split(jax.random.fold_in(base_key, 5), N_SEQ)
    other_perm = jax.vmap(lambda part_key: jax.random.permutation(part_key, N_SEQ - 1))(other_keys).astype(jnp.int32)
    others = (user_ids[:, None] + 1 + other_perm) % N_SEQ
    far_picks = (slot_iota[:, None] * STRIDE + jnp.arange(FAR_SEL, dtype=jnp.int32)[None, :]) % (N_SEQ - 1)
    far_owner = others[:, far_picks].reshape(N_SEQ, OWN * FAR_SEL)
    far_ids = jnp.take_along_axis(far_tile, far_owner, axis=1).reshape(N_SEQ, OWN, FAR_SEL)
    own_wide = jnp.broadcast_to(own_list[:, None, :], (N_SEQ, OWN, OWN))
    listed_rows = jnp.concatenate([own_wide, far_ids], axis=2)
    row_scores = jax.random.randint(jax.random.fold_in(base_key, 6), (N_SEQ, OWN, SELECTED), 0, 1 << 20) * SELECTED
    row_scores = row_scores + jnp.arange(SELECTED, dtype=jnp.int32)[None, None, :]
    row_order = jnp.argsort(row_scores, axis=2).astype(jnp.int32)
    listed_rows = jnp.take_along_axis(listed_rows, row_order, axis=2)
    listed = jnp.zeros((TILES, SELECTED), jnp.int32).at[own_list.reshape(-1)].set(listed_rows.reshape(N_SEQ * OWN, SELECTED))
    return (owners, listed.astype(jnp.int32))


def draw_owner_map(key, part):
    return plan_tables(key)[0]


def draw_pattern(key, part):
    return plan_tables(key)[1]


def feature_pair(key):
    base_key = jax.random.fold_in(key, 5)
    shape = (TOKENS, HEADS * HEAD_DIM)
    raw_query = jnp.clip(jax.random.normal(jax.random.fold_in(base_key, 1), shape, jnp.float32), -4.0, 4.0)
    raw_key = jnp.clip(jax.random.normal(jax.random.fold_in(base_key, 2), shape, jnp.float32), -4.0, 4.0)
    row_scale = jnp.exp(jax.random.uniform(jax.random.fold_in(base_key, 3), (TOKENS, HEADS, 1), jnp.float32, math.log(0.6), math.log(1.6)))
    query_out = 1.5 * (raw_query.reshape(TOKENS, HEADS, HEAD_DIM) * row_scale).reshape(shape)
    key_out = 1.5 * raw_key
    return (query_out, key_out)


def draw_query_feats(key, part):
    return feature_pair(key)[0].astype(jnp.bfloat16)


def draw_key_feats(key, part):
    return feature_pair(key)[1].astype(jnp.bfloat16)


def steps_of(stream_key, dims, cuts, smallest, largest):
    factor_of = 1.0
    for axis_at, blocks in cuts:
        steps = jax.random.uniform(jax.random.fold_in(jax.random.fold_in(stream_key, 6), axis_at), (blocks,), jnp.float32, smallest / len(cuts), largest / len(cuts))
        factor_of = factor_of * jnp.repeat(jnp.exp(steps), dims[axis_at] // blocks).reshape((-1,) + (1,) * (len(dims) - 1 - axis_at))
    return factor_of


def bell_draw(own_key, dims, spread, most, cuts=(), kind=jnp.bfloat16):
    drawn = jax.random.normal(own_key, dims, jnp.float32) * spread
    if len(cuts) > 0:
        drawn = steps_of(own_key, dims, cuts, -0.22, 0.18) * drawn
    return jnp.clip(drawn, min=-most, max=most).astype(kind)


def setup_inputs(seed: int = 0, part: int = 0) -> dict:
    splits = jax.random.split(jax.random.key(seed), 6)
    part_splits = jax.random.split(jax.random.fold_in(splits[5], part), 6)
    return {
        "query_feats": draw_query_feats(jax.random.fold_in(jax.random.fold_in(splits[5], part), 71), part),
        "key_feats": draw_key_feats(jax.random.fold_in(jax.random.fold_in(splits[5], part), 71), part),
        "value_feats": bell_draw(part_splits[2], (TOKENS, CHANNELS), 1.0, 6.0, ((0, 16),)),
        "owner_map": draw_owner_map(jax.random.fold_in(jax.random.fold_in(splits[5], part), 71), part),
        "pattern": draw_pattern(jax.random.fold_in(jax.random.fold_in(splits[5], part), 71), part),
    }


def tile_rows(matrix):
    channels = matrix.shape[1]
    shaped = matrix.reshape(BANDS, 4, HEIGHT // 4, 4, WIDTH // 4, 4, channels)
    return shaped.transpose(0, 2, 4, 1, 3, 5, 6).reshape(TILES, 64, channels)


def token_rows(tiled_rows):
    channels = tiled_rows.shape[2]
    shaped = tiled_rows.reshape(BANDS, HEIGHT // 4, WIDTH // 4, 4, 4, 4, channels)
    return shaped.transpose(0, 3, 1, 4, 2, 5, 6).reshape(TOKENS, channels)


def reference(query_feats, key_feats, value_feats, owner_map, pattern):
    score_scale = HEAD_DIM ** -0.5
    tile_query = tile_rows(query_feats)
    tile_key = tile_rows(key_feats)
    tile_value = tile_rows(value_feats)

    def attend_tile(packed):
        query_tile, listed = packed
        chosen_key = jnp.take(tile_key, listed, axis=0).reshape(SELECTED * 64, HEADS, HEAD_DIM).astype(jnp.float32)
        chosen_value = jnp.take(tile_value, listed, axis=0).reshape(SELECTED * 64, HEADS, HEAD_DIM).astype(jnp.float32)
        query_float = query_tile.reshape(64, HEADS, HEAD_DIM).astype(jnp.float32)
        scores = jnp.einsum("qhd,khd->hqk", query_float, chosen_key) * score_scale
        row_max = jnp.max(scores, axis=2, keepdims=True)
        log_total = row_max + jnp.log(jnp.sum(jnp.exp(scores - row_max), axis=2, keepdims=True))
        weights = jnp.exp(scores - log_total).astype(jnp.bfloat16)
        weights = lax.optimization_barrier(weights).astype(jnp.float32)
        mixed_rows = jnp.einsum("hqk,khd->qhd", weights, chosen_value).reshape(64, HEADS * HEAD_DIM)
        return mixed_rows.astype(jnp.bfloat16), log_total[:, :, 0]

    mixed_tiles, log_tiles = lax.map(attend_tile, (tile_query, pattern))
    attended = token_rows(mixed_tiles)
    devices = jnp.arange(N_SEQ, dtype=jnp.int32)
    onehot = (owner_map[:, None] == devices[None, :]).astype(jnp.int32)
    running = jnp.cumsum(onehot, axis=0)
    own_rank = (jnp.sum(onehot * running, axis=1) - 1).astype(jnp.int32)
    slot_iota = jnp.arange(OWN, dtype=jnp.int32)
    tile_iota = jnp.arange(TILES, dtype=jnp.int32)
    match_rows = (owner_map[None, None, :] == devices[:, None, None]) & (own_rank[None, None, :] == slot_iota[None, :, None])
    own_list = jnp.sum(jnp.where(match_rows, tile_iota[None, None, :], 0), axis=2).astype(jnp.int32)
    log_flat = log_tiles.reshape(TILES, HEADS * 64)
    log_sums = jnp.take(log_flat, own_list.reshape(-1), axis=0).reshape(N_SEQ, OWN, HEADS * 64)
    return attended, log_sums
```

```python
import jax
import jax.numpy as jnp
from jax import lax
from jax.sharding import PartitionSpec as P
from jax.experimental import pallas as pl

HEADS = 20
HEAD_DIM = 128
WIDTH = 64
FRAMES = 16


masked_score = -1e30


def frame_pieces(rows_in, strips):
    channels = rows_in.shape[1]
    shaped = rows_in.reshape(strips, 4, WIDTH // 4, 4, channels)
    return shaped.transpose(0, 2, 1, 3, 4).reshape(strips * (WIDTH // 4), 16, channels)


def frame_rows(pieces, strips):
    channels = pieces.shape[2]
    shaped = pieces.reshape(strips, WIDTH // 4, 4, 4, channels)
    return shaped.transpose(0, 2, 1, 3, 4).reshape(strips * 4 * WIDTH, channels)


def owner_tables(owner_map, group_size, piece_count):
    tile_count = owner_map.shape[0]
    devices = jnp.arange(group_size, dtype=jnp.int32)
    onehot = (owner_map[:, None] == devices[None, :]).astype(jnp.int32)
    running = jnp.cumsum(onehot, axis=0)
    own_rank = jnp.sum(onehot * running, axis=1) - 1
    by_class = owner_map.reshape(tile_count // piece_count, piece_count)
    local_iota = jnp.arange(piece_count, dtype=jnp.int32)
    earlier = (by_class[:, :, None] == by_class[:, None, :]) & (
        local_iota[None, None, :] < local_iota[None, :, None]
    )
    class_rank = jnp.sum(earlier.astype(jnp.int32), axis=2).reshape(tile_count)
    return (own_rank, class_rank)


def owned_tiles(owner_map, own_rank, device, own_count):
    tile_iota = jnp.arange(owner_map.shape[0], dtype=jnp.int32)
    slot_iota = jnp.arange(own_count, dtype=jnp.int32)
    match_rows = (owner_map[None, :] == device) & (own_rank[None, :] == slot_iota[:, None])
    return jnp.sum(jnp.where(match_rows, tile_iota[None, :], 0), axis=1)


def request_table(owner_map, pattern, group_size):
    devices = jnp.arange(group_size, dtype=jnp.int32)
    entry_owner = jnp.take(owner_map, pattern)
    foreign = entry_owner != owner_map[:, None]
    entry_hit = (entry_owner[:, :, None] == devices[None, None, :]) & foreign[:, :, None]
    per_tile = jnp.max(jnp.where(entry_hit, pattern[:, :, None], -1), axis=1)
    per_user = owner_map[None, :] == devices[:, None]
    return jnp.max(jnp.where(per_user[:, :, None], per_tile[None, :, :], -1), axis=1)


def supplier_of(tile_class, frame_slice, frame_devs):
    return (4 * (tile_class // frame_devs) + frame_slice) * frame_devs + tile_class % frame_devs


def expand_mask(block_mask):
    query_tiles = block_mask.shape[0]
    key_tiles = block_mask.shape[1]
    wide = jnp.broadcast_to(block_mask[:, None, :, None], (query_tiles, 64, key_tiles, 64))
    return wide.reshape(query_tiles * 64, key_tiles * 64)


def head_part(matrix, offset):
    return lax.dynamic_slice_in_dim(matrix, offset, HEAD_DIM, 1)


def head_scores(query_head, key_rows, offset, mask):
    key_head = head_part(key_rows, offset)
    scores = lax.dot_general(
        query_head, key_head, (((1,), (1,)), ((), ())), preferred_element_type=jnp.float32
    ) * HEAD_DIM ** (-0.5)
    return jnp.where(mask, scores, masked_score)


def attention_kernel(query_ref, key_ref, value_ref, mask_ref, out_ref, log_ref):
    scores = lax.dot_general(
        query_ref[...], key_ref[...], (((1,), (1,)), ((), ())), preferred_element_type=jnp.float32
    ) * HEAD_DIM ** (-0.5)
    scores = jnp.where(mask_ref[...] > 0, scores, masked_score)
    row_max = jnp.max(scores, axis=1, keepdims=True)
    log_total = row_max + jnp.log(jnp.sum(jnp.exp(scores - row_max), axis=1, keepdims=True))
    weights = jnp.exp(scores - log_total).astype(jnp.bfloat16)
    mixed = jnp.dot(weights, value_ref[...], preferred_element_type=jnp.float32)
    out_ref[...] = mixed.astype(out_ref.dtype)
    log_ref[...] = log_total


def attend_pooled(own_query, pool_key, pool_value, mask):
    rows, channels = own_query.shape
    pool = pool_key.shape[0]
    heads = channels // HEAD_DIM
    mask_values = mask.astype(jnp.float32)
    mixed_rows, head_logs = pl.pallas_call(
        attention_kernel,
        grid=(heads,),
        in_specs=[
            pl.BlockSpec((rows, HEAD_DIM), lambda h: (0, h)),
            pl.BlockSpec((pool, HEAD_DIM), lambda h: (0, h)),
            pl.BlockSpec((pool, HEAD_DIM), lambda h: (0, h)),
            pl.BlockSpec((rows, pool), lambda h: (0, 0)),
        ],
        out_specs=[
            pl.BlockSpec((rows, HEAD_DIM), lambda h: (0, h)),
            pl.BlockSpec((None, rows, 1), lambda h: (h, 0, 0)),
        ],
        out_shape=[
            jax.ShapeDtypeStruct((rows, channels), jnp.bfloat16),
            jax.ShapeDtypeStruct((heads, rows, 1), jnp.float32),
        ],
    )(own_query, pool_key, pool_value, mask_values)
    return mixed_rows, head_logs[:, :, 0]


def shards(query_feats, key_feats, value_feats, owner_map, pattern):
    group_size = lax.axis_size("seq")
    device = lax.axis_index("seq")
    channels = query_feats.shape[1]
    strips = query_feats.shape[0] // (4 * WIDTH)
    piece_count = strips * (WIDTH // 4)
    tile_count = owner_map.shape[0]
    own_count = tile_count // group_size
    capacity = (piece_count + group_size - 1) // group_size
    frame_devs = group_size // FRAMES
    devices = jnp.arange(group_size, dtype=jnp.int32)
    local_iota = jnp.arange(piece_count, dtype=jnp.int32)
    cap_iota = jnp.arange(capacity, dtype=jnp.int32)
    slice_iota = jnp.arange(4, dtype=jnp.int32)
    own_rank, class_rank = owner_tables(owner_map, group_size, piece_count)
    my_frame = device // frame_devs
    my_class = my_frame // 4 * frame_devs + device % frame_devs
    my_tiles = my_class * piece_count + local_iota
    my_owner = jnp.take(owner_map, my_tiles)
    my_slot = jnp.take(class_rank, my_tiles)
    send_hit = (my_owner[None, None, :] == devices[:, None, None]) & (
        my_slot[None, None, :] == cap_iota[None, :, None]
    )
    send_index = jnp.sum(jnp.where(send_hit, local_iota[None, None, :], 0), axis=2).reshape(-1)
    query_pieces = frame_pieces(query_feats, strips)
    key_pieces = frame_pieces(key_feats, strips)
    value_pieces = frame_pieces(value_feats, strips)
    sent_query = jnp.take(query_pieces, send_index, axis=0).reshape(
        group_size, capacity, 16, channels
    )
    sent_key = jnp.take(key_pieces, send_index, axis=0).reshape(group_size, capacity, 16, channels)
    sent_value = jnp.take(value_pieces, send_index, axis=0).reshape(
        group_size, capacity, 16, channels
    )
    got_query, got_key, got_value = (
        lax.all_to_all(sent_query, "seq", split_axis=0, concat_axis=0, tiled=True),
        lax.all_to_all(sent_key, "seq", split_axis=0, concat_axis=0, tiled=True),
        lax.all_to_all(sent_value, "seq", split_axis=0, concat_axis=0, tiled=True),
    )
    own_ids = owned_tiles(owner_map, own_rank, device, own_count)
    own_class = own_ids // piece_count
    own_slot = jnp.take(class_rank, own_ids)
    gather_rows = (
        supplier_of(own_class[:, None], slice_iota[None, :], frame_devs) * capacity
        + own_slot[:, None]
    ).reshape(-1)
    own_query = jnp.take(
        got_query.reshape(group_size * capacity, 16, channels), gather_rows, axis=0
    ).reshape(own_count * 64, channels)
    own_key = jnp.take(
        got_key.reshape(group_size * capacity, 16, channels), gather_rows, axis=0
    ).reshape(own_count * 64, channels)
    own_value = jnp.take(
        got_value.reshape(group_size * capacity, 16, channels), gather_rows, axis=0
    ).reshape(own_count * 64, channels)
    requests = request_table(owner_map, pattern, group_size)
    far_ids = jnp.take(requests, device, axis=0)
    asked_tiles = jnp.take(requests, device, axis=1)
    serve_index = jnp.take(own_rank, jnp.maximum(asked_tiles, 0))
    out_key = jnp.take(own_key.reshape(own_count, 64, channels), serve_index, axis=0)
    out_value = jnp.take(own_value.reshape(own_count, 64, channels), serve_index, axis=0)
    far_key, far_value = (
        lax.all_to_all(out_key, "seq", split_axis=0, concat_axis=0, tiled=True),
        lax.all_to_all(out_value, "seq", split_axis=0, concat_axis=0, tiled=True),
    )
    listed = jnp.take(pattern, own_ids, axis=0)
    near_mask = expand_mask(jnp.any(listed[:, :, None] == own_ids[None, None, :], axis=1))
    far_mask = expand_mask(jnp.any(listed[:, :, None] == far_ids[None, None, :], axis=1))
    far_key_rows = far_key.reshape(group_size * 64, channels)
    far_value_rows = far_value.reshape(group_size * 64, channels)
    pool_key = jnp.concatenate([own_key, far_key_rows], axis=0)
    pool_value = jnp.concatenate([own_value, far_value_rows], axis=0)
    pool_mask = jnp.concatenate([near_mask, far_mask], axis=1)
    mixed_rows, head_logs = attend_pooled(own_query, pool_key, pool_value, pool_mask)
    log_sums = (
        head_logs.reshape(HEADS, own_count, 64).transpose(1, 0, 2).reshape(1, own_count, HEADS * 64)
    )
    out_pieces = mixed_rows.reshape(own_count * 4, 16, channels)
    dest_frame = devices // frame_devs
    dest_class = dest_frame // 4 * frame_devs + devices % frame_devs
    dest_slice = dest_frame % 4
    own_iota = jnp.arange(own_count, dtype=jnp.int32)
    back_hit = (own_class[None, None, :] == dest_class[:, None, None]) & (
        own_slot[None, None, :] == cap_iota[None, :, None]
    )
    back_index = jnp.sum(
        jnp.where(back_hit, own_iota[None, None, :] * 4 + dest_slice[:, None, None], 0), axis=2
    ).reshape(-1)
    back_sent = jnp.take(out_pieces, back_index, axis=0).reshape(group_size, capacity, 16, channels)
    returned = lax.all_to_all(back_sent, "seq", split_axis=0, concat_axis=0, tiled=True)
    place_rows = my_owner * capacity + my_slot
    placed = jnp.take(returned.reshape(group_size * capacity, 16, channels), place_rows, axis=0)
    attended = frame_rows(placed, strips)
    return (attended, log_sums)


def solution(mesh):
    placed = (
        P(("groups", "seq"), None),
        P(("groups", "seq"), None),
        P(("groups", "seq"), None),
        P("groups"),
        P("groups", None),
    )
    return jax.shard_map(
        shards,
        mesh=mesh,
        in_specs=placed,
        out_specs=(P(("groups", "seq"), None), P(("groups", "seq"), None, None)),
        check_vma=False,
    )
```

```python
import jax
import jax.numpy as jnp
from jax import lax
from jax.sharding import PartitionSpec as P
from jax.experimental import pallas as pl

HEADS = 20
HEAD_DIM = 128
WIDTH = 64
FRAMES = 16


masked_score = -1e30


def frame_pieces(rows_in, strips):
    channels = rows_in.shape[1]
    shaped = rows_in.reshape(strips, 4, WIDTH // 4, 4, channels)
    return shaped.transpose(0, 2, 1, 3, 4).reshape(strips * (WIDTH // 4), 16, channels)


def frame_rows(pieces, strips):
    channels = pieces.shape[2]
    shaped = pieces.reshape(strips, WIDTH // 4, 4, 4, channels)
    return shaped.transpose(0, 2, 1, 3, 4).reshape(strips * 4 * WIDTH, channels)


def owner_tables(owner_map, group_size, piece_count):
    tile_count = owner_map.shape[0]
    devices = jnp.arange(group_size, dtype=jnp.int32)
    onehot = (owner_map[:, None] == devices[None, :]).astype(jnp.int32)
    running = jnp.cumsum(onehot, axis=0)
    own_rank = jnp.sum(onehot * running, axis=1) - 1
    by_class = owner_map.reshape(tile_count // piece_count, piece_count)
    local_iota = jnp.arange(piece_count, dtype=jnp.int32)
    earlier = (by_class[:, :, None] == by_class[:, None, :]) & (
        local_iota[None, None, :] < local_iota[None, :, None]
    )
    class_rank = jnp.sum(earlier.astype(jnp.int32), axis=2).reshape(tile_count)
    return (own_rank, class_rank)


def owned_tiles(owner_map, own_rank, device, own_count):
    tile_iota = jnp.arange(owner_map.shape[0], dtype=jnp.int32)
    slot_iota = jnp.arange(own_count, dtype=jnp.int32)
    match_rows = (owner_map[None, :] == device) & (own_rank[None, :] == slot_iota[:, None])
    return jnp.sum(jnp.where(match_rows, tile_iota[None, :], 0), axis=1)


def request_table(owner_map, pattern, group_size):
    devices = jnp.arange(group_size, dtype=jnp.int32)
    entry_owner = jnp.take(owner_map, pattern)
    foreign = entry_owner != owner_map[:, None]
    entry_hit = (entry_owner[:, :, None] == devices[None, None, :]) & foreign[:, :, None]
    per_tile = jnp.max(jnp.where(entry_hit, pattern[:, :, None], -1), axis=1)
    per_user = owner_map[None, :] == devices[:, None]
    return jnp.max(jnp.where(per_user[:, :, None], per_tile[None, :, :], -1), axis=1)


def supplier_of(tile_class, frame_slice, frame_devs):
    return (4 * (tile_class // frame_devs) + frame_slice) * frame_devs + tile_class % frame_devs


def expand_mask(block_mask):
    query_tiles = block_mask.shape[0]
    key_tiles = block_mask.shape[1]
    wide = jnp.broadcast_to(block_mask[:, None, :, None], (query_tiles, 64, key_tiles, 64))
    return wide.reshape(query_tiles * 64, key_tiles * 64)


def head_part(matrix, offset):
    return lax.dynamic_slice_in_dim(matrix, offset, HEAD_DIM, 1)


def head_scores(query_head, key_rows, offset, mask):
    key_head = head_part(key_rows, offset)
    scores = lax.dot_general(
        query_head, key_head, (((1,), (1,)), ((), ())), preferred_element_type=jnp.float32
    ) * HEAD_DIM ** (-0.5)
    return jnp.where(mask, scores, masked_score)


FAR_SLOTS = 4


def attention_kernel(
    query_ref, near_key_ref, near_value_ref, far_key_ref, far_value_ref, near_bias_ref,
    far_bias_ref, out_ref, log_ref
):
    query = query_ref[...]
    dims = (((1,), (1,)), ((), ()))
    scale = HEAD_DIM ** (-0.5)
    near_scores = lax.dot_general(
        query, near_key_ref[...], dims, preferred_element_type=jnp.float32
    ) * scale + near_bias_ref[...]
    far_scores = lax.dot_general(
        query, far_key_ref[...], dims, preferred_element_type=jnp.float32
    ) * scale + far_bias_ref[...]
    row_max = jnp.maximum(
        jnp.max(near_scores, axis=1, keepdims=True), jnp.max(far_scores, axis=1, keepdims=True)
    )
    near_exp = jnp.exp(near_scores - row_max)
    far_exp = jnp.exp(far_scores - row_max)
    total = jnp.sum(near_exp, axis=1, keepdims=True) + jnp.sum(far_exp, axis=1, keepdims=True)
    log_total = row_max + jnp.log(total)
    inverse = 1.0 / total
    near_weights = (near_exp * inverse).astype(jnp.bfloat16)
    far_weights = (far_exp * inverse).astype(jnp.bfloat16)
    mixed = jnp.dot(near_weights, near_value_ref[...], preferred_element_type=jnp.float32)
    mixed = mixed + jnp.dot(far_weights, far_value_ref[...], preferred_element_type=jnp.float32)
    out_ref[...] = mixed.astype(out_ref.dtype)
    log_ref[...] = log_total


def attend(query, near_key, near_value, far_key, far_value, near_bias, far_bias):
    rows, channels = query.shape
    near = near_key.shape[0]
    far = far_key.shape[0]
    heads = channels // HEAD_DIM
    return pl.pallas_call(
        attention_kernel,
        grid=(heads,),
        in_specs=[
            pl.BlockSpec((rows, HEAD_DIM), lambda h: (0, h)),
            pl.BlockSpec((near, HEAD_DIM), lambda h: (0, h)),
            pl.BlockSpec((near, HEAD_DIM), lambda h: (0, h)),
            pl.BlockSpec((far, HEAD_DIM), lambda h: (0, h)),
            pl.BlockSpec((far, HEAD_DIM), lambda h: (0, h)),
            pl.BlockSpec((rows, near), lambda h: (0, 0)),
            pl.BlockSpec((rows, far), lambda h: (0, 0)),
        ],
        out_specs=[
            pl.BlockSpec((rows, HEAD_DIM), lambda h: (0, h)),
            pl.BlockSpec((None, rows, 1), lambda h: (h, 0, 0)),
        ],
        out_shape=[
            jax.ShapeDtypeStruct((rows, channels), jnp.bfloat16),
            jax.ShapeDtypeStruct((heads, rows, 1), jnp.float32),
        ],
    )(query, near_key, near_value, far_key, far_value, near_bias, far_bias)


def class_of(devices, frame_devs):
    return devices // frame_devs // 4 * frame_devs + devices % frame_devs


def ranked_pick(candidates, wanted, slot_count):
    rank = jnp.cumsum(wanted.astype(jnp.int32), axis=-1) - 1
    slots = jnp.arange(slot_count, dtype=jnp.int32)
    hit = wanted[..., None] & (rank[..., None] == slots)
    picked = jnp.sum(jnp.where(hit, candidates[..., None], 0), axis=-2)
    return picked, jnp.any(hit, axis=-2)


def shards(query_feats, key_feats, value_feats, owner_map, pattern):
    group_size = lax.axis_size("seq")
    device = lax.axis_index("seq")
    local_rows, channels = query_feats.shape
    strips = local_rows // (4 * WIDTH)
    blocks = WIDTH // 4
    piece_count = strips * blocks
    tile_count = owner_map.shape[0]
    own_count = tile_count // group_size
    capacity = (piece_count + group_size - 1) // group_size
    frame_devs = group_size // FRAMES
    devices = jnp.arange(group_size, dtype=jnp.int32)
    local_iota = jnp.arange(piece_count, dtype=jnp.int32)
    cap_iota = jnp.arange(capacity, dtype=jnp.int32)
    slice_iota = jnp.arange(4, dtype=jnp.int32)
    token_iota = jnp.arange(16, dtype=jnp.int32)

    def piece_rows(pieces):
        strip = pieces // blocks
        column = pieces % blocks
        return (
            strip[..., None] * (4 * WIDTH)
            + (token_iota // 4) * WIDTH
            + column[..., None] * 4
            + token_iota % 4
        )

    own_rank, class_rank = owner_tables(owner_map, group_size, piece_count)
    my_class = class_of(device, frame_devs)
    my_tiles = my_class * piece_count + local_iota
    my_owner = jnp.take(owner_map, my_tiles)
    my_slot = jnp.take(class_rank, my_tiles)
    send_hit = (my_owner[None, None, :] == devices[:, None, None]) & (
        my_slot[None, None, :] == cap_iota[None, :, None]
    )
    send_index = jnp.sum(jnp.where(send_hit, local_iota[None, None, :], 0), axis=2)
    own_send_rows = piece_rows(send_index).reshape(-1)
    requests = request_table(owner_map, pattern, group_size)
    wanted = (requests >= 0) & (requests // piece_count == my_class)
    far_send_piece, _ = ranked_pick(requests % piece_count, wanted, FAR_SLOTS)
    far_send_rows = piece_rows(far_send_piece).reshape(-1)
    own_shape = (group_size, capacity * 16, channels)
    far_shape = (group_size, FAR_SLOTS * 16, channels)
    sent_query = jnp.take(query_feats, own_send_rows, axis=0).reshape(own_shape)
    sent_key = jnp.take(key_feats, own_send_rows, axis=0).reshape(own_shape)
    sent_value = jnp.take(value_feats, own_send_rows, axis=0).reshape(own_shape)
    sent_far_key = jnp.take(key_feats, far_send_rows, axis=0).reshape(far_shape)
    sent_far_value = jnp.take(value_feats, far_send_rows, axis=0).reshape(far_shape)

    def exchange(sent):
        got = lax.all_to_all(sent, "seq", split_axis=0, concat_axis=0, tiled=True)
        return got.reshape(-1, channels)

    got_query = exchange(sent_query)
    got_key = exchange(sent_key)
    got_value = exchange(sent_value)
    got_far_key = exchange(sent_far_key)
    got_far_value = exchange(sent_far_value)
    source_class = class_of(devices, frame_devs)
    class_tiles = source_class[:, None] * piece_count + local_iota[None, :]
    mine = jnp.take(owner_map, class_tiles) == device
    near_hit = mine[:, None, :] & (jnp.take(class_rank, class_tiles)[:, None, :] == cap_iota[None, :, None])
    near_tile = jnp.sum(jnp.where(near_hit, class_tiles[:, None, :], 0), axis=2)
    near_tile_rows = jnp.broadcast_to(near_tile[:, :, None], (group_size, capacity, 16)).reshape(-1)
    my_requests = jnp.take(requests, device, axis=0)
    far_wanted = (my_requests[None, :] >= 0) & (my_requests[None, :] // piece_count == source_class[:, None])
    far_tile, far_valid = ranked_pick(
        jnp.broadcast_to(my_requests[None, :], (group_size, group_size)), far_wanted, FAR_SLOTS
    )
    far_tile = jnp.where(far_valid, far_tile, -1)
    far_tile_rows = jnp.broadcast_to(far_tile[:, :, None], (group_size, FAR_SLOTS, 16)).reshape(-1)
    own_ids = owned_tiles(owner_map, own_rank, device, own_count)
    listed = jnp.take(pattern, own_ids, axis=0)
    near_ok = jnp.any(listed[:, :, None] == near_tile_rows[None, None, :], axis=1)
    far_ok = jnp.any(listed[:, :, None] == far_tile_rows[None, None, :], axis=1)
    query_own = jnp.take(own_rank, near_tile_rows)
    near_bias = jnp.where(jnp.take(near_ok, query_own, axis=0), 0.0, masked_score).astype(jnp.float32)
    far_bias = jnp.where(jnp.take(far_ok, query_own, axis=0), 0.0, masked_score).astype(jnp.float32)
    mixed_rows, head_logs = attend(
        got_query, got_key, got_value, got_far_key, got_far_value, near_bias, far_bias
    )
    own_class = own_ids // piece_count
    own_slot = jnp.take(class_rank, own_ids)
    gather_rows = (
        supplier_of(own_class[:, None], slice_iota[None, :], frame_devs) * capacity
        + own_slot[:, None]
    )
    log_rows = (gather_rows[:, :, None] * 16 + token_iota).reshape(-1)
    heads = channels // HEAD_DIM
    log_sums = (
        jnp.take(head_logs[:, :, 0], log_rows, axis=1)
        .reshape(heads, own_count, 64)
        .transpose(1, 0, 2)
        .reshape(1, own_count, heads * 64)
    )
    returned = exchange(mixed_rows.reshape(own_shape))
    local_iota_rows = jnp.arange(local_rows, dtype=jnp.int32)
    strip = local_iota_rows // (4 * WIDTH)
    height = local_iota_rows % (4 * WIDTH) // WIDTH
    column = local_iota_rows % WIDTH
    piece = strip * blocks + column // 4
    token = height * 4 + column % 4
    back_rows = (jnp.take(my_owner, piece) * capacity + jnp.take(my_slot, piece)) * 16 + token
    attended = jnp.take(returned, back_rows, axis=0)
    return (attended, log_sums)


def solution(mesh):
    placed = (
        P(("groups", "seq"), None),
        P(("groups", "seq"), None),
        P(("groups", "seq"), None),
        P("groups"),
        P("groups", None),
    )
    return jax.shard_map(
        shards,
        mesh=mesh,
        in_specs=placed,
        out_specs=(P(("groups", "seq"), None), P(("groups", "seq"), None, None)),
        check_vma=False,
    )
```

```python
import jax
import jax.numpy as jnp
from jax import lax
from jax.sharding import PartitionSpec as P
from jax.experimental import pallas as pl

HEADS = 20
HEAD_DIM = 128
WIDTH = 64
FRAMES = 16


masked_score = -1e30


def frame_pieces(rows_in, strips):
    channels = rows_in.shape[1]
    shaped = rows_in.reshape(strips, 4, WIDTH // 4, 4, channels)
    return shaped.transpose(0, 2, 1, 3, 4).reshape(strips * (WIDTH // 4), 16, channels)


def frame_rows(pieces, strips):
    channels = pieces.shape[2]
    shaped = pieces.reshape(strips, WIDTH // 4, 4, 4, channels)
    return shaped.transpose(0, 2, 1, 3, 4).reshape(strips * 4 * WIDTH, channels)


def owner_tables(owner_map, group_size, piece_count):
    tile_count = owner_map.shape[0]
    devices = jnp.arange(group_size, dtype=jnp.int32)
    onehot = (owner_map[:, None] == devices[None, :]).astype(jnp.int32)
    running = jnp.cumsum(onehot, axis=0)
    own_rank = jnp.sum(onehot * running, axis=1) - 1
    by_class = owner_map.reshape(tile_count // piece_count, piece_count)
    local_iota = jnp.arange(piece_count, dtype=jnp.int32)
    earlier = (by_class[:, :, None] == by_class[:, None, :]) & (
        local_iota[None, None, :] < local_iota[None, :, None]
    )
    class_rank = jnp.sum(earlier.astype(jnp.int32), axis=2).reshape(tile_count)
    return (own_rank, class_rank)


def owned_tiles(owner_map, own_rank, device, own_count):
    tile_iota = jnp.arange(owner_map.shape[0], dtype=jnp.int32)
    slot_iota = jnp.arange(own_count, dtype=jnp.int32)
    match_rows = (owner_map[None, :] == device) & (own_rank[None, :] == slot_iota[:, None])
    return jnp.sum(jnp.where(match_rows, tile_iota[None, :], 0), axis=1)


def request_table(owner_map, pattern, group_size):
    devices = jnp.arange(group_size, dtype=jnp.int32)
    entry_owner = jnp.take(owner_map, pattern)
    foreign = entry_owner != owner_map[:, None]
    entry_hit = (entry_owner[:, :, None] == devices[None, None, :]) & foreign[:, :, None]
    per_tile = jnp.max(jnp.where(entry_hit, pattern[:, :, None], -1), axis=1)
    per_user = owner_map[None, :] == devices[:, None]
    return jnp.max(jnp.where(per_user[:, :, None], per_tile[None, :, :], -1), axis=1)


def supplier_of(tile_class, frame_slice, frame_devs):
    return (4 * (tile_class // frame_devs) + frame_slice) * frame_devs + tile_class % frame_devs


def expand_mask(block_mask):
    query_tiles = block_mask.shape[0]
    key_tiles = block_mask.shape[1]
    wide = jnp.broadcast_to(block_mask[:, None, :, None], (query_tiles, 64, key_tiles, 64))
    return wide.reshape(query_tiles * 64, key_tiles * 64)


def head_part(matrix, offset):
    return lax.dynamic_slice_in_dim(matrix, offset, HEAD_DIM, 1)


def head_scores(query_head, key_rows, offset, mask):
    key_head = head_part(key_rows, offset)
    scores = lax.dot_general(
        query_head, key_head, (((1,), (1,)), ((), ())), preferred_element_type=jnp.float32
    ) * HEAD_DIM ** (-0.5)
    return jnp.where(mask, scores, masked_score)


FAR_SLOTS = 4
HEAD_CHUNKS = 2


def attention_kernel(
    far_key_ref, far_value_ref, query_ref, near_key_ref, near_value_ref, near_bias_ref,
    far_bias_ref, out_ref, log_ref
):
    def flat(ref):
        block = ref[...]
        return block.reshape(block.shape[0] * block.shape[1], block.shape[2])

    query = flat(query_ref)
    dims = (((1,), (1,)), ((), ()))
    scale = HEAD_DIM ** (-0.5)
    near_scores = lax.dot_general(
        query, flat(near_key_ref), dims, preferred_element_type=jnp.float32
    ) * scale + near_bias_ref[...]
    far_scores = lax.dot_general(
        query, flat(far_key_ref), dims, preferred_element_type=jnp.float32
    ) * scale + far_bias_ref[...]
    row_max = jnp.maximum(
        jnp.max(near_scores, axis=1, keepdims=True), jnp.max(far_scores, axis=1, keepdims=True)
    )
    near_exp = jnp.exp(near_scores - row_max)
    far_exp = jnp.exp(far_scores - row_max)
    total = jnp.sum(near_exp, axis=1, keepdims=True) + jnp.sum(far_exp, axis=1, keepdims=True)
    log_total = row_max + jnp.log(total)
    inverse = 1.0 / total
    near_weights = (near_exp * inverse).astype(jnp.bfloat16)
    far_weights = (far_exp * inverse).astype(jnp.bfloat16)
    mixed = jnp.dot(near_weights, flat(near_value_ref), preferred_element_type=jnp.float32)
    mixed = mixed + jnp.dot(far_weights, flat(far_value_ref), preferred_element_type=jnp.float32)
    out_ref[...] = mixed.astype(out_ref.dtype).reshape(out_ref.shape)
    log_ref[...] = log_total


def attend(got, unit, near_bias, far_bias):
    group_size, _, channels = got.shape
    far_rows = FAR_SLOTS * 16
    rows = group_size * unit
    heads = channels // HEAD_DIM
    base = 2 * far_rows // unit
    far_spec = (group_size, far_rows, HEAD_DIM)
    own_spec = (group_size, unit, HEAD_DIM)
    return pl.pallas_call(
        attention_kernel,
        grid=(heads,),
        in_specs=[
            pl.BlockSpec(far_spec, lambda h: (0, 0, h)),
            pl.BlockSpec(far_spec, lambda h: (0, 1, h)),
            pl.BlockSpec(own_spec, lambda h: (0, base, h)),
            pl.BlockSpec(own_spec, lambda h: (0, base + 1, h)),
            pl.BlockSpec(own_spec, lambda h: (0, base + 2, h)),
            pl.BlockSpec((rows, rows), lambda h: (0, 0)),
            pl.BlockSpec((rows, group_size * far_rows), lambda h: (0, 0)),
        ],
        out_specs=[
            pl.BlockSpec(own_spec, lambda h: (0, 0, h)),
            pl.BlockSpec((None, rows, 1), lambda h: (h, 0, 0)),
        ],
        out_shape=[
            jax.ShapeDtypeStruct((group_size, unit, channels), jnp.bfloat16),
            jax.ShapeDtypeStruct((heads, rows, 1), jnp.float32),
        ],
    )(got, got, got, got, got, near_bias, far_bias)


def class_of(devices, frame_devs):
    return devices // frame_devs // 4 * frame_devs + devices % frame_devs


def ranked_pick(candidates, wanted, slot_count):
    rank = jnp.cumsum(wanted.astype(jnp.int32), axis=-1) - 1
    slots = jnp.arange(slot_count, dtype=jnp.int32)
    hit = wanted[..., None] & (rank[..., None] == slots)
    picked = jnp.sum(jnp.where(hit, candidates[..., None], 0), axis=-2)
    return picked, jnp.any(hit, axis=-2)


def shards(query_feats, key_feats, value_feats, owner_map, pattern):
    group_size = lax.axis_size("seq")
    device = lax.axis_index("seq")
    local_rows, channels = query_feats.shape
    strips = local_rows // (4 * WIDTH)
    blocks = WIDTH // 4
    piece_count = strips * blocks
    tile_count = owner_map.shape[0]
    own_count = tile_count // group_size
    capacity = (piece_count + group_size - 1) // group_size
    unit = capacity * 16
    frame_devs = group_size // FRAMES
    devices = jnp.arange(group_size, dtype=jnp.int32)
    local_iota = jnp.arange(piece_count, dtype=jnp.int32)
    cap_iota = jnp.arange(capacity, dtype=jnp.int32)
    slice_iota = jnp.arange(4, dtype=jnp.int32)
    token_iota = jnp.arange(16, dtype=jnp.int32)

    def piece_rows(pieces):
        strip = pieces // blocks
        column = pieces % blocks
        return (
            strip[..., None] * (4 * WIDTH)
            + (token_iota // 4) * WIDTH
            + column[..., None] * 4
            + token_iota % 4
        )

    own_rank, class_rank = owner_tables(owner_map, group_size, piece_count)
    my_class = class_of(device, frame_devs)
    my_tiles = my_class * piece_count + local_iota
    my_owner = jnp.take(owner_map, my_tiles)
    my_slot = jnp.take(class_rank, my_tiles)
    send_hit = (my_owner[None, None, :] == devices[:, None, None]) & (
        my_slot[None, None, :] == cap_iota[None, :, None]
    )
    send_index = jnp.sum(jnp.where(send_hit, local_iota[None, None, :], 0), axis=2)
    own_send_rows = piece_rows(send_index).reshape(group_size, unit)
    requests = request_table(owner_map, pattern, group_size)
    wanted = (requests >= 0) & (requests // piece_count == my_class)
    far_send_piece, _ = ranked_pick(requests % piece_count, wanted, FAR_SLOTS)
    far_send_rows = piece_rows(far_send_piece).reshape(group_size, FAR_SLOTS * 16)
    send_rows = jnp.concatenate(
        [
            far_send_rows + local_rows,
            far_send_rows + 2 * local_rows,
            own_send_rows,
            own_send_rows + local_rows,
            own_send_rows + 2 * local_rows,
        ],
        axis=1,
    ).reshape(-1)
    source_class = class_of(devices, frame_devs)
    class_tiles = source_class[:, None] * piece_count + local_iota[None, :]
    mine = jnp.take(owner_map, class_tiles) == device
    near_hit = mine[:, None, :] & (
        jnp.take(class_rank, class_tiles)[:, None, :] == cap_iota[None, :, None]
    )
    near_tile = jnp.sum(jnp.where(near_hit, class_tiles[:, None, :], 0), axis=2)
    near_tile_rows = jnp.broadcast_to(near_tile[:, :, None], (group_size, capacity, 16)).reshape(-1)
    my_requests = jnp.take(requests, device, axis=0)
    far_wanted = (my_requests[None, :] >= 0) & (
        my_requests[None, :] // piece_count == source_class[:, None]
    )
    far_tile, far_valid = ranked_pick(
        jnp.broadcast_to(my_requests[None, :], (group_size, group_size)), far_wanted, FAR_SLOTS
    )
    far_tile = jnp.where(far_valid, far_tile, -1)
    far_tile_rows = jnp.broadcast_to(
        far_tile[:, :, None], (group_size, FAR_SLOTS, 16)
    ).reshape(-1)
    own_ids = owned_tiles(owner_map, own_rank, device, own_count)
    listed = jnp.take(pattern, own_ids, axis=0)
    near_ok = jnp.any(listed[:, :, None] == near_tile_rows[None, None, :], axis=1)
    far_ok = jnp.any(listed[:, :, None] == far_tile_rows[None, None, :], axis=1)
    query_own = jnp.take(own_rank, near_tile_rows)
    near_bias = jnp.where(jnp.take(near_ok, query_own, axis=0), 0.0, masked_score)
    far_bias = jnp.where(jnp.take(far_ok, query_own, axis=0), 0.0, masked_score)
    near_bias = near_bias.astype(jnp.float32)
    far_bias = far_bias.astype(jnp.float32)
    chunk_width = channels // HEAD_CHUNKS
    outputs = []
    logs = []
    for chunk in range(HEAD_CHUNKS):
        columns = slice(chunk * chunk_width, (chunk + 1) * chunk_width)
        stacked = jnp.concatenate(
            [query_feats[:, columns], key_feats[:, columns], value_feats[:, columns]], axis=0
        )
        sent = jnp.take(stacked, send_rows, axis=0).reshape(group_size, -1, chunk_width)
        got = lax.all_to_all(sent, "seq", split_axis=0, concat_axis=0, tiled=True)
        mixed, head_logs = attend(got, unit, near_bias, far_bias)
        returned = lax.all_to_all(mixed, "seq", split_axis=0, concat_axis=0, tiled=True)
        outputs.append(returned.reshape(-1, chunk_width))
        logs.append(head_logs[:, :, 0])
    head_logs = jnp.concatenate(logs, axis=0)
    own_class = own_ids // piece_count
    own_slot = jnp.take(class_rank, own_ids)
    gather_rows = (
        supplier_of(own_class[:, None], slice_iota[None, :], frame_devs) * capacity
        + own_slot[:, None]
    )
    log_rows = (gather_rows[:, :, None] * 16 + token_iota).reshape(-1)
    heads = channels // HEAD_DIM
    log_sums = (
        jnp.take(head_logs, log_rows, axis=1)
        .reshape(heads, own_count, 64)
        .transpose(1, 0, 2)
        .reshape(1, own_count, heads * 64)
    )
    local_iota_rows = jnp.arange(local_rows, dtype=jnp.int32)
    strip = local_iota_rows // (4 * WIDTH)
    height = local_iota_rows % (4 * WIDTH) // WIDTH
    column = local_iota_rows % WIDTH
    piece = strip * blocks + column // 4
    token = height * 4 + column % 4
    back_rows = (jnp.take(my_owner, piece) * capacity + jnp.take(my_slot, piece)) * 16 + token
    attended = jnp.take(jnp.concatenate(outputs, axis=1), back_rows, axis=0)
    return (attended, log_sums)


def solution(mesh):
    placed = (
        P(("groups", "seq"), None),
        P(("groups", "seq"), None),
        P(("groups", "seq"), None),
        P("groups"),
        P("groups", None),
    )
    return jax.shard_map(
        shards,
        mesh=mesh,
        in_specs=placed,
        out_specs=(P(("groups", "seq"), None), P(("groups", "seq"), None, None)),
        check_vma=False,
    )
```

```python
import jax
import jax.numpy as jnp
from jax import lax
from jax.sharding import PartitionSpec as P
from jax.experimental import pallas as pl

HEADS = 20
HEAD_DIM = 128
WIDTH = 64
FRAMES = 16


masked_score = -1e30


def frame_pieces(rows_in, strips):
    channels = rows_in.shape[1]
    shaped = rows_in.reshape(strips, 4, WIDTH // 4, 4, channels)
    return shaped.transpose(0, 2, 1, 3, 4).reshape(strips * (WIDTH // 4), 16, channels)


def frame_rows(pieces, strips):
    channels = pieces.shape[2]
    shaped = pieces.reshape(strips, WIDTH // 4, 4, 4, channels)
    return shaped.transpose(0, 2, 1, 3, 4).reshape(strips * 4 * WIDTH, channels)


def owner_tables(owner_map, group_size, piece_count):
    tile_count = owner_map.shape[0]
    devices = jnp.arange(group_size, dtype=jnp.int32)
    onehot = (owner_map[:, None] == devices[None, :]).astype(jnp.int32)
    running = jnp.cumsum(onehot, axis=0)
    own_rank = jnp.sum(onehot * running, axis=1) - 1
    by_class = owner_map.reshape(tile_count // piece_count, piece_count)
    local_iota = jnp.arange(piece_count, dtype=jnp.int32)
    earlier = (by_class[:, :, None] == by_class[:, None, :]) & (
        local_iota[None, None, :] < local_iota[None, :, None]
    )
    class_rank = jnp.sum(earlier.astype(jnp.int32), axis=2).reshape(tile_count)
    return (own_rank, class_rank)


def owned_tiles(owner_map, own_rank, device, own_count):
    tile_iota = jnp.arange(owner_map.shape[0], dtype=jnp.int32)
    slot_iota = jnp.arange(own_count, dtype=jnp.int32)
    match_rows = (owner_map[None, :] == device) & (own_rank[None, :] == slot_iota[:, None])
    return jnp.sum(jnp.where(match_rows, tile_iota[None, :], 0), axis=1)


def request_table(owner_map, pattern, group_size):
    devices = jnp.arange(group_size, dtype=jnp.int32)
    entry_owner = jnp.take(owner_map, pattern)
    foreign = entry_owner != owner_map[:, None]
    entry_hit = (entry_owner[:, :, None] == devices[None, None, :]) & foreign[:, :, None]
    per_tile = jnp.max(jnp.where(entry_hit, pattern[:, :, None], -1), axis=1)
    per_user = owner_map[None, :] == devices[:, None]
    return jnp.max(jnp.where(per_user[:, :, None], per_tile[None, :, :], -1), axis=1)


def supplier_of(tile_class, frame_slice, frame_devs):
    return (4 * (tile_class // frame_devs) + frame_slice) * frame_devs + tile_class % frame_devs


def expand_mask(block_mask):
    query_tiles = block_mask.shape[0]
    key_tiles = block_mask.shape[1]
    wide = jnp.broadcast_to(block_mask[:, None, :, None], (query_tiles, 64, key_tiles, 64))
    return wide.reshape(query_tiles * 64, key_tiles * 64)


def head_part(matrix, offset):
    return lax.dynamic_slice_in_dim(matrix, offset, HEAD_DIM, 1)


def head_scores(query_head, key_rows, offset, mask):
    key_head = head_part(key_rows, offset)
    scores = lax.dot_general(
        query_head, key_head, (((1,), (1,)), ((), ())), preferred_element_type=jnp.float32
    ) * HEAD_DIM ** (-0.5)
    return jnp.where(mask, scores, masked_score)


FAR_SLOTS = 4
HEAD_CHUNKS = 2


def attention_kernel(
    far_key_ref, far_value_ref, query_ref, near_key_ref, near_value_ref, near_bias_ref,
    far_bias_ref, out_ref, log_ref
):
    def flat(ref):
        block = ref[...]
        return block.reshape(block.shape[0] * block.shape[1], block.shape[2])

    query = flat(query_ref)
    dims = (((1,), (1,)), ((), ()))
    scale = HEAD_DIM ** (-0.5)
    near_scores = lax.dot_general(
        query, flat(near_key_ref), dims, preferred_element_type=jnp.float32
    ) * scale + near_bias_ref[...]
    far_scores = lax.dot_general(
        query, flat(far_key_ref), dims, preferred_element_type=jnp.float32
    ) * scale + far_bias_ref[...]
    row_max = jnp.maximum(
        jnp.max(near_scores, axis=1, keepdims=True), jnp.max(far_scores, axis=1, keepdims=True)
    )
    near_exp = jnp.exp(near_scores - row_max)
    far_exp = jnp.exp(far_scores - row_max)
    total = jnp.sum(near_exp, axis=1, keepdims=True) + jnp.sum(far_exp, axis=1, keepdims=True)
    log_total = row_max + jnp.log(total)
    inverse = 1.0 / total
    near_weights = (near_exp * inverse).astype(jnp.bfloat16)
    far_weights = (far_exp * inverse).astype(jnp.bfloat16)
    mixed = jnp.dot(near_weights, flat(near_value_ref), preferred_element_type=jnp.float32)
    mixed = mixed + jnp.dot(far_weights, flat(far_value_ref), preferred_element_type=jnp.float32)
    out_ref[...] = mixed.astype(out_ref.dtype).reshape(out_ref.shape)
    log_ref[...] = log_total


def attend(got, unit, near_bias, far_bias):
    group_size, _, channels = got.shape
    far_rows = FAR_SLOTS * 16
    rows = group_size * unit
    heads = channels // HEAD_DIM
    base = 2 * far_rows // unit
    far_spec = (group_size, far_rows, HEAD_DIM)
    own_spec = (group_size, unit, HEAD_DIM)
    return pl.pallas_call(
        attention_kernel,
        grid=(heads,),
        in_specs=[
            pl.BlockSpec(far_spec, lambda h: (0, 0, h)),
            pl.BlockSpec(far_spec, lambda h: (0, 1, h)),
            pl.BlockSpec(own_spec, lambda h: (0, base, h)),
            pl.BlockSpec(own_spec, lambda h: (0, base + 1, h)),
            pl.BlockSpec(own_spec, lambda h: (0, base + 2, h)),
            pl.BlockSpec((rows, rows), lambda h: (0, 0)),
            pl.BlockSpec((rows, group_size * far_rows), lambda h: (0, 0)),
        ],
        out_specs=[
            pl.BlockSpec(own_spec, lambda h: (0, 0, h)),
            pl.BlockSpec((None, rows, 1), lambda h: (h, 0, 0)),
        ],
        out_shape=[
            jax.ShapeDtypeStruct((group_size, unit, channels), jnp.bfloat16),
            jax.ShapeDtypeStruct((heads, rows, 1), jnp.float32),
        ],
    )(got, got, got, got, got, near_bias, far_bias)


def class_of(devices, frame_devs):
    return devices // frame_devs // 4 * frame_devs + devices % frame_devs


def ranked_pick(candidates, wanted, slot_count):
    rank = jnp.cumsum(wanted.astype(jnp.int32), axis=-1) - 1
    slots = jnp.arange(slot_count, dtype=jnp.int32)
    hit = wanted[..., None] & (rank[..., None] == slots)
    picked = jnp.sum(jnp.where(hit, candidates[..., None], 0), axis=-2)
    return picked, jnp.any(hit, axis=-2)


def shards(query_feats, key_feats, value_feats, owner_map, pattern):
    group_size = lax.axis_size("seq")
    device = lax.axis_index("seq")
    local_rows, channels = query_feats.shape
    strips = local_rows // (4 * WIDTH)
    blocks = WIDTH // 4
    piece_count = strips * blocks
    tile_count = owner_map.shape[0]
    own_count = tile_count // group_size
    capacity = (piece_count + group_size - 1) // group_size
    unit = capacity * 16
    frame_devs = group_size // FRAMES
    devices = jnp.arange(group_size, dtype=jnp.int32)
    local_iota = jnp.arange(piece_count, dtype=jnp.int32)
    cap_iota = jnp.arange(capacity, dtype=jnp.int32)
    slice_iota = jnp.arange(4, dtype=jnp.int32)
    token_iota = jnp.arange(16, dtype=jnp.int32)

    def piece_rows(pieces):
        strip = pieces // blocks
        column = pieces % blocks
        return (
            strip[..., None] * (4 * WIDTH)
            + (token_iota // 4) * WIDTH
            + column[..., None] * 4
            + token_iota % 4
        )

    own_rank, class_rank = owner_tables(owner_map, group_size, piece_count)
    my_class = class_of(device, frame_devs)
    my_tiles = my_class * piece_count + local_iota
    my_owner = jnp.take(owner_map, my_tiles)
    my_slot = jnp.take(class_rank, my_tiles)
    send_hit = (my_owner[None, None, :] == devices[:, None, None]) & (
        my_slot[None, None, :] == cap_iota[None, :, None]
    )
    send_index = jnp.sum(jnp.where(send_hit, local_iota[None, None, :], 0), axis=2)
    own_send_rows = piece_rows(send_index).reshape(group_size, unit)
    requests = request_table(owner_map, pattern, group_size)
    wanted = (requests >= 0) & (requests // piece_count == my_class)
    far_send_piece, _ = ranked_pick(requests % piece_count, wanted, FAR_SLOTS)
    far_send_rows = piece_rows(far_send_piece).reshape(group_size, FAR_SLOTS * 16)
    source_class = class_of(devices, frame_devs)
    class_tiles = source_class[:, None] * piece_count + local_iota[None, :]
    mine = jnp.take(owner_map, class_tiles) == device
    near_hit = mine[:, None, :] & (
        jnp.take(class_rank, class_tiles)[:, None, :] == cap_iota[None, :, None]
    )
    near_tile = jnp.sum(jnp.where(near_hit, class_tiles[:, None, :], 0), axis=2)
    near_tile_rows = jnp.broadcast_to(near_tile[:, :, None], (group_size, capacity, 16)).reshape(-1)
    my_requests = jnp.take(requests, device, axis=0)
    far_wanted = (my_requests[None, :] >= 0) & (
        my_requests[None, :] // piece_count == source_class[:, None]
    )
    far_tile, far_valid = ranked_pick(
        jnp.broadcast_to(my_requests[None, :], (group_size, group_size)), far_wanted, FAR_SLOTS
    )
    far_tile = jnp.where(far_valid, far_tile, -1)
    far_tile_rows = jnp.broadcast_to(
        far_tile[:, :, None], (group_size, FAR_SLOTS, 16)
    ).reshape(-1)
    own_ids = owned_tiles(owner_map, own_rank, device, own_count)
    listed = jnp.take(pattern, own_ids, axis=0)
    near_ok = jnp.any(listed[:, :, None] == near_tile_rows[None, None, :], axis=1)
    far_ok = jnp.any(listed[:, :, None] == far_tile_rows[None, None, :], axis=1)
    query_own = jnp.take(own_rank, near_tile_rows)
    near_bias = jnp.where(jnp.take(near_ok, query_own, axis=0), 0.0, masked_score)
    far_bias = jnp.where(jnp.take(far_ok, query_own, axis=0), 0.0, masked_score)
    near_bias = near_bias.astype(jnp.float32)
    far_bias = far_bias.astype(jnp.float32)
    chunk_width = channels // HEAD_CHUNKS
    outputs = []
    logs = []
    taken = lax.optimization_barrier(
        (
            jnp.take(key_feats, far_send_rows.reshape(-1), axis=0).reshape(group_size, -1, channels),
            jnp.take(value_feats, far_send_rows.reshape(-1), axis=0).reshape(group_size, -1, channels),
            jnp.take(query_feats, own_send_rows.reshape(-1), axis=0).reshape(group_size, -1, channels),
            jnp.take(key_feats, own_send_rows.reshape(-1), axis=0).reshape(group_size, -1, channels),
            jnp.take(value_feats, own_send_rows.reshape(-1), axis=0).reshape(group_size, -1, channels),
        )
    )
    for chunk in range(HEAD_CHUNKS):
        columns = slice(chunk * chunk_width, (chunk + 1) * chunk_width)
        sent = jnp.concatenate([part[:, :, columns] for part in taken], axis=1)
        got = lax.all_to_all(sent, "seq", split_axis=0, concat_axis=0, tiled=True)
        mixed, head_logs = attend(got, unit, near_bias, far_bias)
        returned = lax.all_to_all(mixed, "seq", split_axis=0, concat_axis=0, tiled=True)
        outputs.append(returned.reshape(-1, chunk_width))
        logs.append(head_logs[:, :, 0])
    head_logs = jnp.concatenate(logs, axis=0)
    own_class = own_ids // piece_count
    own_slot = jnp.take(class_rank, own_ids)
    gather_rows = (
        supplier_of(own_class[:, None], slice_iota[None, :], frame_devs) * capacity
        + own_slot[:, None]
    )
    log_rows = (gather_rows[:, :, None] * 16 + token_iota).reshape(-1)
    heads = channels // HEAD_DIM
    log_sums = (
        jnp.take(head_logs, log_rows, axis=1)
        .reshape(heads, own_count, 64)
        .transpose(1, 0, 2)
        .reshape(1, own_count, heads * 64)
    )
    local_iota_rows = jnp.arange(local_rows, dtype=jnp.int32)
    strip = local_iota_rows // (4 * WIDTH)
    height = local_iota_rows % (4 * WIDTH) // WIDTH
    column = local_iota_rows % WIDTH
    piece = strip * blocks + column // 4
    token = height * 4 + column % 4
    back_rows = (jnp.take(my_owner, piece) * capacity + jnp.take(my_slot, piece)) * 16 + token
    attended = jnp.take(jnp.concatenate(outputs, axis=1), back_rows, axis=0)
    return (attended, log_sums)


def solution(mesh):
    placed = (
        P(("groups", "seq"), None),
        P(("groups", "seq"), None),
        P(("groups", "seq"), None),
        P("groups"),
        P("groups", None),
    )
    return jax.shard_map(
        shards,
        mesh=mesh,
        in_specs=placed,
        out_specs=(P(("groups", "seq"), None), P(("groups", "seq"), None, None)),
        check_vma=False,
    )
```

```python
import jax
import jax.numpy as jnp
from jax import lax
from jax.sharding import PartitionSpec as P
from jax.experimental import pallas as pl

HEADS = 20
HEAD_DIM = 128
WIDTH = 64
FRAMES = 16


masked_score = -1e30


def frame_pieces(rows_in, strips):
    channels = rows_in.shape[1]
    shaped = rows_in.reshape(strips, 4, WIDTH // 4, 4, channels)
    return shaped.transpose(0, 2, 1, 3, 4).reshape(strips * (WIDTH // 4), 16, channels)


def frame_rows(pieces, strips):
    channels = pieces.shape[2]
    shaped = pieces.reshape(strips, WIDTH // 4, 4, 4, channels)
    return shaped.transpose(0, 2, 1, 3, 4).reshape(strips * 4 * WIDTH, channels)


def owner_tables(owner_map, group_size, piece_count):
    tile_count = owner_map.shape[0]
    devices = jnp.arange(group_size, dtype=jnp.int32)
    onehot = (owner_map[:, None] == devices[None, :]).astype(jnp.int32)
    running = jnp.cumsum(onehot, axis=0)
    own_rank = jnp.sum(onehot * running, axis=1) - 1
    by_class = owner_map.reshape(tile_count // piece_count, piece_count)
    local_iota = jnp.arange(piece_count, dtype=jnp.int32)
    earlier = (by_class[:, :, None] == by_class[:, None, :]) & (
        local_iota[None, None, :] < local_iota[None, :, None]
    )
    class_rank = jnp.sum(earlier.astype(jnp.int32), axis=2).reshape(tile_count)
    return (own_rank, class_rank)


def owned_tiles(owner_map, own_rank, device, own_count):
    tile_iota = jnp.arange(owner_map.shape[0], dtype=jnp.int32)
    slot_iota = jnp.arange(own_count, dtype=jnp.int32)
    match_rows = (owner_map[None, :] == device) & (own_rank[None, :] == slot_iota[:, None])
    return jnp.sum(jnp.where(match_rows, tile_iota[None, :], 0), axis=1)


def pick(table, index):
    iota = jnp.arange(table.shape[0], dtype=jnp.int32)
    hit = index[..., None] == iota
    return jnp.sum(jnp.where(hit, table, 0), axis=-1).astype(table.dtype)


def pick_rows(table, index):
    iota = jnp.arange(table.shape[0], dtype=jnp.int32)
    hit = (index[..., None] == iota)[..., None]
    return jnp.sum(jnp.where(hit, table, 0), axis=-2).astype(table.dtype)


def request_table(owner_map, pattern, group_size):
    devices = jnp.arange(group_size, dtype=jnp.int32)
    entry_owner = pick(owner_map, pattern)
    foreign = entry_owner != owner_map[:, None]
    entry_hit = (entry_owner[:, :, None] == devices[None, None, :]) & foreign[:, :, None]
    per_tile = jnp.max(jnp.where(entry_hit, pattern[:, :, None], -1), axis=1)
    per_user = owner_map[None, :] == devices[:, None]
    return jnp.max(jnp.where(per_user[:, :, None], per_tile[None, :, :], -1), axis=1)


def supplier_of(tile_class, frame_slice, frame_devs):
    return (4 * (tile_class // frame_devs) + frame_slice) * frame_devs + tile_class % frame_devs


def expand_mask(block_mask):
    query_tiles = block_mask.shape[0]
    key_tiles = block_mask.shape[1]
    wide = jnp.broadcast_to(block_mask[:, None, :, None], (query_tiles, 64, key_tiles, 64))
    return wide.reshape(query_tiles * 64, key_tiles * 64)


def head_part(matrix, offset):
    return lax.dynamic_slice_in_dim(matrix, offset, HEAD_DIM, 1)


def head_scores(query_head, key_rows, offset, mask):
    key_head = head_part(key_rows, offset)
    scores = lax.dot_general(
        query_head, key_head, (((1,), (1,)), ((), ())), preferred_element_type=jnp.float32
    ) * HEAD_DIM ** (-0.5)
    return jnp.where(mask, scores, masked_score)


FAR_SLOTS = 4
HEAD_CHUNKS = 2


def attention_kernel(
    far_key_ref, far_value_ref, query_ref, near_key_ref, near_value_ref, near_bias_ref,
    far_bias_ref, out_ref, log_ref
):
    def flat(ref):
        block = ref[...]
        return block.reshape(block.shape[0] * block.shape[1], block.shape[2])

    query = flat(query_ref)
    dims = (((1,), (1,)), ((), ()))
    scale = HEAD_DIM ** (-0.5)
    near_scores = lax.dot_general(
        query, flat(near_key_ref), dims, preferred_element_type=jnp.float32
    ) * scale + near_bias_ref[...]
    far_scores = lax.dot_general(
        query, flat(far_key_ref), dims, preferred_element_type=jnp.float32
    ) * scale + far_bias_ref[...]
    row_max = jnp.maximum(
        jnp.max(near_scores, axis=1, keepdims=True), jnp.max(far_scores, axis=1, keepdims=True)
    )
    near_exp = jnp.exp(near_scores - row_max)
    far_exp = jnp.exp(far_scores - row_max)
    total = jnp.sum(near_exp, axis=1, keepdims=True) + jnp.sum(far_exp, axis=1, keepdims=True)
    log_total = row_max + jnp.log(total)
    inverse = 1.0 / total
    near_weights = (near_exp * inverse).astype(jnp.bfloat16)
    far_weights = (far_exp * inverse).astype(jnp.bfloat16)
    mixed = jnp.dot(near_weights, flat(near_value_ref), preferred_element_type=jnp.float32)
    mixed = mixed + jnp.dot(far_weights, flat(far_value_ref), preferred_element_type=jnp.float32)
    out_ref[...] = mixed.astype(out_ref.dtype).reshape(out_ref.shape)
    log_ref[...] = log_total


def attend(got, unit, near_bias, far_bias):
    group_size, _, channels = got.shape
    far_rows = FAR_SLOTS * 16
    rows = group_size * unit
    heads = channels // HEAD_DIM
    base = 2 * far_rows // unit
    far_spec = (group_size, far_rows, HEAD_DIM)
    own_spec = (group_size, unit, HEAD_DIM)
    return pl.pallas_call(
        attention_kernel,
        grid=(heads,),
        in_specs=[
            pl.BlockSpec(far_spec, lambda h: (0, 0, h)),
            pl.BlockSpec(far_spec, lambda h: (0, 1, h)),
            pl.BlockSpec(own_spec, lambda h: (0, base, h)),
            pl.BlockSpec(own_spec, lambda h: (0, base + 1, h)),
            pl.BlockSpec(own_spec, lambda h: (0, base + 2, h)),
            pl.BlockSpec((rows, rows), lambda h: (0, 0)),
            pl.BlockSpec((rows, group_size * far_rows), lambda h: (0, 0)),
        ],
        out_specs=[
            pl.BlockSpec(own_spec, lambda h: (0, 0, h)),
            pl.BlockSpec((None, rows, 1), lambda h: (h, 0, 0)),
        ],
        out_shape=[
            jax.ShapeDtypeStruct((group_size, unit, channels), jnp.bfloat16),
            jax.ShapeDtypeStruct((heads, rows, 1), jnp.float32),
        ],
    )(got, got, got, got, got, near_bias, far_bias)


def class_of(devices, frame_devs):
    return devices // frame_devs // 4 * frame_devs + devices % frame_devs


def ranked_pick(candidates, wanted, slot_count):
    rank = jnp.cumsum(wanted.astype(jnp.int32), axis=-1) - 1
    slots = jnp.arange(slot_count, dtype=jnp.int32)
    hit = wanted[..., None] & (rank[..., None] == slots)
    picked = jnp.sum(jnp.where(hit, candidates[..., None], 0), axis=-2)
    return picked, jnp.any(hit, axis=-2)


def shards(query_feats, key_feats, value_feats, owner_map, pattern):
    group_size = lax.axis_size("seq")
    device = lax.axis_index("seq")
    local_rows, channels = query_feats.shape
    strips = local_rows // (4 * WIDTH)
    blocks = WIDTH // 4
    piece_count = strips * blocks
    tile_count = owner_map.shape[0]
    own_count = tile_count // group_size
    capacity = (piece_count + group_size - 1) // group_size
    unit = capacity * 16
    frame_devs = group_size // FRAMES
    devices = jnp.arange(group_size, dtype=jnp.int32)
    local_iota = jnp.arange(piece_count, dtype=jnp.int32)
    cap_iota = jnp.arange(capacity, dtype=jnp.int32)
    slice_iota = jnp.arange(4, dtype=jnp.int32)
    token_iota = jnp.arange(16, dtype=jnp.int32)

    def piece_rows(pieces):
        strip = pieces // blocks
        column = pieces % blocks
        return (
            strip[..., None] * (4 * WIDTH)
            + (token_iota // 4) * WIDTH
            + column[..., None] * 4
            + token_iota % 4
        )

    own_rank, class_rank = owner_tables(owner_map, group_size, piece_count)
    my_class = class_of(device, frame_devs)
    my_tiles = my_class * piece_count + local_iota
    my_owner = lax.dynamic_slice_in_dim(owner_map, my_class * piece_count, piece_count)
    my_slot = lax.dynamic_slice_in_dim(class_rank, my_class * piece_count, piece_count)
    send_hit = (my_owner[None, None, :] == devices[:, None, None]) & (
        my_slot[None, None, :] == cap_iota[None, :, None]
    )
    send_index = jnp.sum(jnp.where(send_hit, local_iota[None, None, :], 0), axis=2)
    own_send_rows = piece_rows(send_index).reshape(group_size, unit)
    requests = request_table(owner_map, pattern, group_size)
    wanted = (requests >= 0) & (requests // piece_count == my_class)
    far_send_piece, _ = ranked_pick(requests % piece_count, wanted, FAR_SLOTS)
    far_send_rows = piece_rows(far_send_piece).reshape(group_size, FAR_SLOTS * 16)
    source_class = class_of(devices, frame_devs)
    class_tiles = source_class[:, None] * piece_count + local_iota[None, :]
    class_count = tile_count // piece_count
    mine = pick_rows(owner_map.reshape(class_count, piece_count), source_class) == device
    near_hit = mine[:, None, :] & (
        pick_rows(class_rank.reshape(class_count, piece_count), source_class)[:, None, :]
        == cap_iota[None, :, None]
    )
    near_tile = jnp.sum(jnp.where(near_hit, class_tiles[:, None, :], 0), axis=2)
    near_tile_rows = jnp.broadcast_to(near_tile[:, :, None], (group_size, capacity, 16)).reshape(-1)
    my_requests = lax.dynamic_index_in_dim(requests, device, axis=0, keepdims=False)
    far_wanted = (my_requests[None, :] >= 0) & (
        my_requests[None, :] // piece_count == source_class[:, None]
    )
    far_tile, far_valid = ranked_pick(
        jnp.broadcast_to(my_requests[None, :], (group_size, group_size)), far_wanted, FAR_SLOTS
    )
    far_tile = jnp.where(far_valid, far_tile, -1)
    far_tile_rows = jnp.broadcast_to(
        far_tile[:, :, None], (group_size, FAR_SLOTS, 16)
    ).reshape(-1)
    own_ids = owned_tiles(owner_map, own_rank, device, own_count)
    listed = pick_rows(pattern, own_ids)
    near_ok = jnp.any(listed[:, :, None] == near_tile_rows[None, None, :], axis=1)
    far_ok = jnp.any(listed[:, :, None] == far_tile_rows[None, None, :], axis=1)
    query_own = pick(own_rank, near_tile_rows)
    near_bias = jnp.where(jnp.take(near_ok, query_own, axis=0), 0.0, masked_score)
    far_bias = jnp.where(jnp.take(far_ok, query_own, axis=0), 0.0, masked_score)
    near_bias = near_bias.astype(jnp.float32)
    far_bias = far_bias.astype(jnp.float32)
    chunk_width = channels // HEAD_CHUNKS
    outputs = []
    logs = []
    taken = lax.optimization_barrier(
        (
            jnp.take(key_feats, far_send_rows.reshape(-1), axis=0).reshape(group_size, -1, channels),
            jnp.take(value_feats, far_send_rows.reshape(-1), axis=0).reshape(group_size, -1, channels),
            jnp.take(query_feats, own_send_rows.reshape(-1), axis=0).reshape(group_size, -1, channels),
            jnp.take(key_feats, own_send_rows.reshape(-1), axis=0).reshape(group_size, -1, channels),
            jnp.take(value_feats, own_send_rows.reshape(-1), axis=0).reshape(group_size, -1, channels),
        )
    )
    for chunk in range(HEAD_CHUNKS):
        columns = slice(chunk * chunk_width, (chunk + 1) * chunk_width)
        sent = jnp.concatenate([part[:, :, columns] for part in taken], axis=1)
        got = lax.all_to_all(sent, "seq", split_axis=0, concat_axis=0, tiled=True)
        mixed, head_logs = attend(got, unit, near_bias, far_bias)
        returned = lax.all_to_all(mixed, "seq", split_axis=0, concat_axis=0, tiled=True)
        outputs.append(returned.reshape(-1, chunk_width))
        logs.append(head_logs[:, :, 0])
    head_logs = jnp.concatenate(logs, axis=0)
    own_class = own_ids // piece_count
    own_slot = pick(class_rank, own_ids)
    gather_rows = (
        supplier_of(own_class[:, None], slice_iota[None, :], frame_devs) * capacity
        + own_slot[:, None]
    )
    log_rows = (gather_rows[:, :, None] * 16 + token_iota).reshape(-1)
    heads = channels // HEAD_DIM
    log_sums = (
        jnp.take(head_logs, log_rows, axis=1)
        .reshape(heads, own_count, 64)
        .transpose(1, 0, 2)
        .reshape(1, own_count, heads * 64)
    )
    local_iota_rows = jnp.arange(local_rows, dtype=jnp.int32)
    strip = local_iota_rows // (4 * WIDTH)
    height = local_iota_rows % (4 * WIDTH) // WIDTH
    column = local_iota_rows % WIDTH
    piece = strip * blocks + column // 4
    token = height * 4 + column % 4
    back_rows = (pick(my_owner, piece) * capacity + pick(my_slot, piece)) * 16 + token
    attended = jnp.take(jnp.concatenate(outputs, axis=1), back_rows, axis=0)
    return (attended, log_sums)


def solution(mesh):
    placed = (
        P(("groups", "seq"), None),
        P(("groups", "seq"), None),
        P(("groups", "seq"), None),
        P("groups"),
        P("groups", None),
    )
    return jax.shard_map(
        shards,
        mesh=mesh,
        in_specs=placed,
        out_specs=(P(("groups", "seq"), None), P(("groups", "seq"), None, None)),
        check_vma=False,
    )
```

```python
import jax
import jax.numpy as jnp
from jax import lax
from jax.sharding import PartitionSpec as P
from jax.experimental import pallas as pl

HEADS = 20
HEAD_DIM = 128
WIDTH = 64
FRAMES = 16


masked_score = -1e30


def frame_pieces(rows_in, strips):
    channels = rows_in.shape[1]
    shaped = rows_in.reshape(strips, 4, WIDTH // 4, 4, channels)
    return shaped.transpose(0, 2, 1, 3, 4).reshape(strips * (WIDTH // 4), 16, channels)


def frame_rows(pieces, strips):
    channels = pieces.shape[2]
    shaped = pieces.reshape(strips, WIDTH // 4, 4, 4, channels)
    return shaped.transpose(0, 2, 1, 3, 4).reshape(strips * 4 * WIDTH, channels)


def owner_tables(owner_map, group_size, piece_count):
    tile_count = owner_map.shape[0]
    devices = jnp.arange(group_size, dtype=jnp.int32)
    onehot = (owner_map[:, None] == devices[None, :]).astype(jnp.int32)
    running = jnp.cumsum(onehot, axis=0)
    own_rank = jnp.sum(onehot * running, axis=1) - 1
    by_class = owner_map.reshape(tile_count // piece_count, piece_count)
    local_iota = jnp.arange(piece_count, dtype=jnp.int32)
    earlier = (by_class[:, :, None] == by_class[:, None, :]) & (
        local_iota[None, None, :] < local_iota[None, :, None]
    )
    class_rank = jnp.sum(earlier.astype(jnp.int32), axis=2).reshape(tile_count)
    return (own_rank, class_rank)


def owned_tiles(owner_map, own_rank, device, own_count):
    tile_iota = jnp.arange(owner_map.shape[0], dtype=jnp.int32)
    slot_iota = jnp.arange(own_count, dtype=jnp.int32)
    match_rows = (owner_map[None, :] == device) & (own_rank[None, :] == slot_iota[:, None])
    return jnp.sum(jnp.where(match_rows, tile_iota[None, :], 0), axis=1)


def pick(table, index):
    iota = jnp.arange(table.shape[0], dtype=jnp.int32)
    hit = index[..., None] == iota
    return jnp.sum(jnp.where(hit, table, 0), axis=-1).astype(table.dtype)


def pick_rows(table, index):
    iota = jnp.arange(table.shape[0], dtype=jnp.int32)
    hit = (index[..., None] == iota)[..., None]
    return jnp.sum(jnp.where(hit, table, 0), axis=-2).astype(table.dtype)


def request_table(owner_map, pattern, group_size):
    devices = jnp.arange(group_size, dtype=jnp.int32)
    entry_owner = pick(owner_map, pattern)
    foreign = entry_owner != owner_map[:, None]
    entry_hit = (entry_owner[:, :, None] == devices[None, None, :]) & foreign[:, :, None]
    per_tile = jnp.max(jnp.where(entry_hit, pattern[:, :, None], -1), axis=1)
    per_user = owner_map[None, :] == devices[:, None]
    return jnp.max(jnp.where(per_user[:, :, None], per_tile[None, :, :], -1), axis=1)


def supplier_of(tile_class, frame_slice, frame_devs):
    return (4 * (tile_class // frame_devs) + frame_slice) * frame_devs + tile_class % frame_devs


def expand_mask(block_mask):
    query_tiles = block_mask.shape[0]
    key_tiles = block_mask.shape[1]
    wide = jnp.broadcast_to(block_mask[:, None, :, None], (query_tiles, 64, key_tiles, 64))
    return wide.reshape(query_tiles * 64, key_tiles * 64)


def head_part(matrix, offset):
    return lax.dynamic_slice_in_dim(matrix, offset, HEAD_DIM, 1)


def head_scores(query_head, key_rows, offset, mask):
    key_head = head_part(key_rows, offset)
    scores = lax.dot_general(
        query_head, key_head, (((1,), (1,)), ((), ())), preferred_element_type=jnp.float32
    ) * HEAD_DIM ** (-0.5)
    return jnp.where(mask, scores, masked_score)


FAR_SLOTS = 4
HEAD_CHUNKS = 4


def attention_kernel(
    far_key_ref, far_value_ref, query_ref, near_key_ref, near_value_ref, near_bias_ref,
    far_bias_ref, out_ref, log_ref
):
    def flat(ref):
        block = ref[...]
        return block.reshape(block.shape[0] * block.shape[1], block.shape[2])

    query = flat(query_ref)
    dims = (((1,), (1,)), ((), ()))
    scale = HEAD_DIM ** (-0.5)
    near_scores = lax.dot_general(
        query, flat(near_key_ref), dims, preferred_element_type=jnp.float32
    ) * scale + near_bias_ref[...]
    far_scores = lax.dot_general(
        query, flat(far_key_ref), dims, preferred_element_type=jnp.float32
    ) * scale + far_bias_ref[...]
    row_max = jnp.maximum(
        jnp.max(near_scores, axis=1, keepdims=True), jnp.max(far_scores, axis=1, keepdims=True)
    )
    near_exp = jnp.exp(near_scores - row_max)
    far_exp = jnp.exp(far_scores - row_max)
    total = jnp.sum(near_exp, axis=1, keepdims=True) + jnp.sum(far_exp, axis=1, keepdims=True)
    log_total = row_max + jnp.log(total)
    inverse = 1.0 / total
    near_weights = (near_exp * inverse).astype(jnp.bfloat16)
    far_weights = (far_exp * inverse).astype(jnp.bfloat16)
    mixed = jnp.dot(near_weights, flat(near_value_ref), preferred_element_type=jnp.float32)
    mixed = mixed + jnp.dot(far_weights, flat(far_value_ref), preferred_element_type=jnp.float32)
    out_ref[...] = mixed.astype(out_ref.dtype).reshape(out_ref.shape)
    log_ref[...] = log_total


def attend(got, unit, near_bias, far_bias):
    group_size, _, channels = got.shape
    far_rows = FAR_SLOTS * 16
    rows = group_size * unit
    heads = channels // HEAD_DIM
    base = 2 * far_rows // unit
    far_spec = (group_size, far_rows, HEAD_DIM)
    own_spec = (group_size, unit, HEAD_DIM)
    return pl.pallas_call(
        attention_kernel,
        grid=(heads,),
        in_specs=[
            pl.BlockSpec(far_spec, lambda h: (0, 0, h)),
            pl.BlockSpec(far_spec, lambda h: (0, 1, h)),
            pl.BlockSpec(own_spec, lambda h: (0, base, h)),
            pl.BlockSpec(own_spec, lambda h: (0, base + 1, h)),
            pl.BlockSpec(own_spec, lambda h: (0, base + 2, h)),
            pl.BlockSpec((rows, rows), lambda h: (0, 0)),
            pl.BlockSpec((rows, group_size * far_rows), lambda h: (0, 0)),
        ],
        out_specs=[
            pl.BlockSpec(own_spec, lambda h: (0, 0, h)),
            pl.BlockSpec((None, rows, 1), lambda h: (h, 0, 0)),
        ],
        out_shape=[
            jax.ShapeDtypeStruct((group_size, unit, channels), jnp.bfloat16),
            jax.ShapeDtypeStruct((heads, rows, 1), jnp.float32),
        ],
    )(got, got, got, got, got, near_bias, far_bias)


def class_of(devices, frame_devs):
    return devices // frame_devs // 4 * frame_devs + devices % frame_devs


def ranked_pick(candidates, wanted, slot_count):
    rank = jnp.cumsum(wanted.astype(jnp.int32), axis=-1) - 1
    slots = jnp.arange(slot_count, dtype=jnp.int32)
    hit = wanted[..., None] & (rank[..., None] == slots)
    picked = jnp.sum(jnp.where(hit, candidates[..., None], 0), axis=-2)
    return picked, jnp.any(hit, axis=-2)


def shards(query_feats, key_feats, value_feats, owner_map, pattern):
    group_size = lax.axis_size("seq")
    device = lax.axis_index("seq")
    local_rows, channels = query_feats.shape
    strips = local_rows // (4 * WIDTH)
    blocks = WIDTH // 4
    piece_count = strips * blocks
    tile_count = owner_map.shape[0]
    own_count = tile_count // group_size
    capacity = (piece_count + group_size - 1) // group_size
    unit = capacity * 16
    frame_devs = group_size // FRAMES
    devices = jnp.arange(group_size, dtype=jnp.int32)
    local_iota = jnp.arange(piece_count, dtype=jnp.int32)
    cap_iota = jnp.arange(capacity, dtype=jnp.int32)
    slice_iota = jnp.arange(4, dtype=jnp.int32)
    token_iota = jnp.arange(16, dtype=jnp.int32)

    def piece_rows(pieces):
        strip = pieces // blocks
        column = pieces % blocks
        return (
            strip[..., None] * (4 * WIDTH)
            + (token_iota // 4) * WIDTH
            + column[..., None] * 4
            + token_iota % 4
        )

    own_rank, class_rank = owner_tables(owner_map, group_size, piece_count)
    my_class = class_of(device, frame_devs)
    my_tiles = my_class * piece_count + local_iota
    my_owner = lax.dynamic_slice_in_dim(owner_map, my_class * piece_count, piece_count)
    my_slot = lax.dynamic_slice_in_dim(class_rank, my_class * piece_count, piece_count)
    send_hit = (my_owner[None, None, :] == devices[:, None, None]) & (
        my_slot[None, None, :] == cap_iota[None, :, None]
    )
    send_index = jnp.sum(jnp.where(send_hit, local_iota[None, None, :], 0), axis=2)
    own_send_rows = piece_rows(send_index).reshape(group_size, unit)
    requests = request_table(owner_map, pattern, group_size)
    wanted = (requests >= 0) & (requests // piece_count == my_class)
    far_send_piece, _ = ranked_pick(requests % piece_count, wanted, FAR_SLOTS)
    far_send_rows = piece_rows(far_send_piece).reshape(group_size, FAR_SLOTS * 16)
    source_class = class_of(devices, frame_devs)
    class_tiles = source_class[:, None] * piece_count + local_iota[None, :]
    class_count = tile_count // piece_count
    mine = pick_rows(owner_map.reshape(class_count, piece_count), source_class) == device
    near_hit = mine[:, None, :] & (
        pick_rows(class_rank.reshape(class_count, piece_count), source_class)[:, None, :]
        == cap_iota[None, :, None]
    )
    near_tile = jnp.sum(jnp.where(near_hit, class_tiles[:, None, :], 0), axis=2)
    near_tile_rows = jnp.broadcast_to(near_tile[:, :, None], (group_size, capacity, 16)).reshape(-1)
    my_requests = lax.dynamic_index_in_dim(requests, device, axis=0, keepdims=False)
    far_wanted = (my_requests[None, :] >= 0) & (
        my_requests[None, :] // piece_count == source_class[:, None]
    )
    far_tile, far_valid = ranked_pick(
        jnp.broadcast_to(my_requests[None, :], (group_size, group_size)), far_wanted, FAR_SLOTS
    )
    far_tile = jnp.where(far_valid, far_tile, -1)
    far_tile_rows = jnp.broadcast_to(
        far_tile[:, :, None], (group_size, FAR_SLOTS, 16)
    ).reshape(-1)
    own_ids = owned_tiles(owner_map, own_rank, device, own_count)
    listed = pick_rows(pattern, own_ids)
    near_ok = jnp.any(listed[:, :, None] == near_tile_rows[None, None, :], axis=1)
    far_ok = jnp.any(listed[:, :, None] == far_tile_rows[None, None, :], axis=1)
    query_own = pick(own_rank, near_tile_rows)
    near_bias = jnp.where(jnp.take(near_ok, query_own, axis=0), 0.0, masked_score)
    far_bias = jnp.where(jnp.take(far_ok, query_own, axis=0), 0.0, masked_score)
    near_bias = near_bias.astype(jnp.float32)
    far_bias = far_bias.astype(jnp.float32)
    chunk_width = channels // HEAD_CHUNKS
    outputs = []
    logs = []
    taken = lax.optimization_barrier(
        (
            jnp.take(key_feats, far_send_rows.reshape(-1), axis=0).reshape(group_size, -1, channels),
            jnp.take(value_feats, far_send_rows.reshape(-1), axis=0).reshape(group_size, -1, channels),
            jnp.take(query_feats, own_send_rows.reshape(-1), axis=0).reshape(group_size, -1, channels),
            jnp.take(key_feats, own_send_rows.reshape(-1), axis=0).reshape(group_size, -1, channels),
            jnp.take(value_feats, own_send_rows.reshape(-1), axis=0).reshape(group_size, -1, channels),
        )
    )
    for chunk in range(HEAD_CHUNKS):
        columns = slice(chunk * chunk_width, (chunk + 1) * chunk_width)
        sent = jnp.concatenate([part[:, :, columns] for part in taken], axis=1)
        got = lax.all_to_all(sent, "seq", split_axis=0, concat_axis=0, tiled=True)
        mixed, head_logs = attend(got, unit, near_bias, far_bias)
        returned = lax.all_to_all(mixed, "seq", split_axis=0, concat_axis=0, tiled=True)
        outputs.append(returned.reshape(-1, chunk_width))
        logs.append(head_logs[:, :, 0])
    head_logs = jnp.concatenate(logs, axis=0)
    own_class = own_ids // piece_count
    own_slot = pick(class_rank, own_ids)
    gather_rows = (
        supplier_of(own_class[:, None], slice_iota[None, :], frame_devs) * capacity
        + own_slot[:, None]
    )
    log_rows = (gather_rows[:, :, None] * 16 + token_iota).reshape(-1)
    heads = channels // HEAD_DIM
    log_sums = (
        jnp.take(head_logs, log_rows, axis=1)
        .reshape(heads, own_count, 64)
        .transpose(1, 0, 2)
        .reshape(1, own_count, heads * 64)
    )
    local_iota_rows = jnp.arange(local_rows, dtype=jnp.int32)
    strip = local_iota_rows // (4 * WIDTH)
    height = local_iota_rows % (4 * WIDTH) // WIDTH
    column = local_iota_rows % WIDTH
    piece = strip * blocks + column // 4
    token = height * 4 + column % 4
    back_rows = (pick(my_owner, piece) * capacity + pick(my_slot, piece)) * 16 + token
    attended = jnp.take(jnp.concatenate(outputs, axis=1), back_rows, axis=0)
    return (attended, log_sums)


def solution(mesh):
    placed = (
        P(("groups", "seq"), None),
        P(("groups", "seq"), None),
        P(("groups", "seq"), None),
        P("groups"),
        P("groups", None),
    )
    return jax.shard_map(
        shards,
        mesh=mesh,
        in_specs=placed,
        out_specs=(P(("groups", "seq"), None), P(("groups", "seq"), None, None)),
        check_vma=False,
    )
```

```python
import jax
import jax.numpy as jnp
from jax import lax
from jax.sharding import PartitionSpec as P
from jax.experimental import pallas as pl

HEADS = 20
HEAD_DIM = 128
WIDTH = 64
FRAMES = 16


masked_score = -1e30


def frame_pieces(rows_in, strips):
    channels = rows_in.shape[1]
    shaped = rows_in.reshape(strips, 4, WIDTH // 4, 4, channels)
    return shaped.transpose(0, 2, 1, 3, 4).reshape(strips * (WIDTH // 4), 16, channels)


def frame_rows(pieces, strips):
    channels = pieces.shape[2]
    shaped = pieces.reshape(strips, WIDTH // 4, 4, 4, channels)
    return shaped.transpose(0, 2, 1, 3, 4).reshape(strips * 4 * WIDTH, channels)


def owner_tables(owner_map, group_size, piece_count):
    tile_count = owner_map.shape[0]
    devices = jnp.arange(group_size, dtype=jnp.int32)
    onehot = (owner_map[:, None] == devices[None, :]).astype(jnp.int32)
    running = jnp.cumsum(onehot, axis=0)
    own_rank = jnp.sum(onehot * running, axis=1) - 1
    by_class = owner_map.reshape(tile_count // piece_count, piece_count)
    local_iota = jnp.arange(piece_count, dtype=jnp.int32)
    earlier = (by_class[:, :, None] == by_class[:, None, :]) & (
        local_iota[None, None, :] < local_iota[None, :, None]
    )
    class_rank = jnp.sum(earlier.astype(jnp.int32), axis=2).reshape(tile_count)
    return (own_rank, class_rank)


def owned_tiles(owner_map, own_rank, device, own_count):
    tile_iota = jnp.arange(owner_map.shape[0], dtype=jnp.int32)
    slot_iota = jnp.arange(own_count, dtype=jnp.int32)
    match_rows = (owner_map[None, :] == device) & (own_rank[None, :] == slot_iota[:, None])
    return jnp.sum(jnp.where(match_rows, tile_iota[None, :], 0), axis=1)


def pick(table, index):
    iota = jnp.arange(table.shape[0], dtype=jnp.int32)
    hit = index[..., None] == iota
    return jnp.sum(jnp.where(hit, table, 0), axis=-1).astype(table.dtype)


def pick_rows(table, index):
    iota = jnp.arange(table.shape[0], dtype=jnp.int32)
    hit = (index[..., None] == iota)[..., None]
    return jnp.sum(jnp.where(hit, table, 0), axis=-2).astype(table.dtype)


def request_table(owner_map, pattern, group_size):
    devices = jnp.arange(group_size, dtype=jnp.int32)
    entry_owner = pick(owner_map, pattern)
    foreign = entry_owner != owner_map[:, None]
    entry_hit = (entry_owner[:, :, None] == devices[None, None, :]) & foreign[:, :, None]
    per_tile = jnp.max(jnp.where(entry_hit, pattern[:, :, None], -1), axis=1)
    per_user = owner_map[None, :] == devices[:, None]
    return jnp.max(jnp.where(per_user[:, :, None], per_tile[None, :, :], -1), axis=1)


def supplier_of(tile_class, frame_slice, frame_devs):
    return (4 * (tile_class // frame_devs) + frame_slice) * frame_devs + tile_class % frame_devs


def expand_mask(block_mask):
    query_tiles = block_mask.shape[0]
    key_tiles = block_mask.shape[1]
    wide = jnp.broadcast_to(block_mask[:, None, :, None], (query_tiles, 64, key_tiles, 64))
    return wide.reshape(query_tiles * 64, key_tiles * 64)


def head_part(matrix, offset):
    return lax.dynamic_slice_in_dim(matrix, offset, HEAD_DIM, 1)


def head_scores(query_head, key_rows, offset, mask):
    key_head = head_part(key_rows, offset)
    scores = lax.dot_general(
        query_head, key_head, (((1,), (1,)), ((), ())), preferred_element_type=jnp.float32
    ) * HEAD_DIM ** (-0.5)
    return jnp.where(mask, scores, masked_score)


FAR_SLOTS = 4
HEAD_CHUNKS = 2


def attention_kernel(
    far_key_ref, far_value_ref, query_ref, near_key_ref, near_value_ref, near_bias_ref,
    far_bias_ref, out_ref, log_ref
):
    def flat(ref):
        block = ref[...]
        return block.reshape(block.shape[0] * block.shape[1], block.shape[2])

    query = flat(query_ref)
    dims = (((1,), (1,)), ((), ()))
    scale = HEAD_DIM ** (-0.5)
    near_scores = lax.dot_general(
        query, flat(near_key_ref), dims, preferred_element_type=jnp.float32
    ) * scale + near_bias_ref[...]
    far_scores = lax.dot_general(
        query, flat(far_key_ref), dims, preferred_element_type=jnp.float32
    ) * scale + far_bias_ref[...]
    row_max = jnp.maximum(
        jnp.max(near_scores, axis=1, keepdims=True), jnp.max(far_scores, axis=1, keepdims=True)
    )
    near_exp = jnp.exp(near_scores - row_max)
    far_exp = jnp.exp(far_scores - row_max)
    total = jnp.sum(near_exp, axis=1, keepdims=True) + jnp.sum(far_exp, axis=1, keepdims=True)
    log_total = row_max + jnp.log(total)
    inverse = 1.0 / total
    near_weights = (near_exp * inverse).astype(jnp.bfloat16)
    far_weights = (far_exp * inverse).astype(jnp.bfloat16)
    mixed = jnp.dot(near_weights, flat(near_value_ref), preferred_element_type=jnp.float32)
    mixed = mixed + jnp.dot(far_weights, flat(far_value_ref), preferred_element_type=jnp.float32)
    out_ref[...] = mixed.astype(out_ref.dtype).reshape(out_ref.shape)
    log_ref[...] = log_total


def attend(got, unit, near_bias, far_bias):
    group_size, _, channels = got.shape
    far_rows = FAR_SLOTS * 16
    rows = group_size * unit
    heads = channels // HEAD_DIM
    base = 2 * far_rows // unit
    far_spec = (group_size, far_rows, HEAD_DIM)
    own_spec = (group_size, unit, HEAD_DIM)
    return pl.pallas_call(
        attention_kernel,
        grid=(heads,),
        in_specs=[
            pl.BlockSpec(far_spec, lambda h: (0, 0, h)),
            pl.BlockSpec(far_spec, lambda h: (0, 1, h)),
            pl.BlockSpec(own_spec, lambda h: (0, base, h)),
            pl.BlockSpec(own_spec, lambda h: (0, base + 1, h)),
            pl.BlockSpec(own_spec, lambda h: (0, base + 2, h)),
            pl.BlockSpec((rows, rows), lambda h: (0, 0)),
            pl.BlockSpec((rows, group_size * far_rows), lambda h: (0, 0)),
        ],
        out_specs=[
            pl.BlockSpec(own_spec, lambda h: (0, 0, h)),
            pl.BlockSpec((None, rows, 1), lambda h: (h, 0, 0)),
        ],
        out_shape=[
            jax.ShapeDtypeStruct((group_size, unit, channels), jnp.bfloat16),
            jax.ShapeDtypeStruct((heads, rows, 1), jnp.float32),
        ],
    )(got, got, got, got, got, near_bias, far_bias)


def class_of(devices, frame_devs):
    return devices // frame_devs // 4 * frame_devs + devices % frame_devs


def ranked_pick(candidates, wanted, slot_count):
    rank = jnp.cumsum(wanted.astype(jnp.int32), axis=-1) - 1
    slots = jnp.arange(slot_count, dtype=jnp.int32)
    hit = wanted[..., None] & (rank[..., None] == slots)
    picked = jnp.sum(jnp.where(hit, candidates[..., None], 0), axis=-2)
    return picked, jnp.any(hit, axis=-2)


def shards(query_feats, key_feats, value_feats, owner_map, pattern):
    group_size = lax.axis_size("seq")
    device = lax.axis_index("seq")
    local_rows, channels = query_feats.shape
    strips = local_rows // (4 * WIDTH)
    blocks = WIDTH // 4
    piece_count = strips * blocks
    tile_count = owner_map.shape[0]
    own_count = tile_count // group_size
    capacity = (piece_count + group_size - 1) // group_size
    unit = capacity * 16
    frame_devs = group_size // FRAMES
    devices = jnp.arange(group_size, dtype=jnp.int32)
    local_iota = jnp.arange(piece_count, dtype=jnp.int32)
    cap_iota = jnp.arange(capacity, dtype=jnp.int32)
    slice_iota = jnp.arange(4, dtype=jnp.int32)
    token_iota = jnp.arange(16, dtype=jnp.int32)

    def piece_rows(pieces):
        strip = pieces // blocks
        column = pieces % blocks
        return (
            strip[..., None] * (4 * WIDTH)
            + (token_iota // 4) * WIDTH
            + column[..., None] * 4
            + token_iota % 4
        )

    own_rank, class_rank = owner_tables(owner_map, group_size, piece_count)
    my_class = class_of(device, frame_devs)
    my_tiles = my_class * piece_count + local_iota
    my_owner = lax.dynamic_slice_in_dim(owner_map, my_class * piece_count, piece_count)
    my_slot = lax.dynamic_slice_in_dim(class_rank, my_class * piece_count, piece_count)
    send_hit = (my_owner[None, None, :] == devices[:, None, None]) & (
        my_slot[None, None, :] == cap_iota[None, :, None]
    )
    send_index = jnp.sum(jnp.where(send_hit, local_iota[None, None, :], 0), axis=2)
    own_send_rows = piece_rows(send_index).reshape(group_size, unit)
    requests = request_table(owner_map, pattern, group_size)
    wanted = (requests >= 0) & (requests // piece_count == my_class)
    far_send_piece, _ = ranked_pick(requests % piece_count, wanted, FAR_SLOTS)
    far_send_rows = piece_rows(far_send_piece).reshape(group_size, FAR_SLOTS * 16)
    source_class = class_of(devices, frame_devs)
    class_tiles = source_class[:, None] * piece_count + local_iota[None, :]
    class_count = tile_count // piece_count
    mine = pick_rows(owner_map.reshape(class_count, piece_count), source_class) == device
    near_hit = mine[:, None, :] & (
        pick_rows(class_rank.reshape(class_count, piece_count), source_class)[:, None, :]
        == cap_iota[None, :, None]
    )
    near_tile = jnp.sum(jnp.where(near_hit, class_tiles[:, None, :], 0), axis=2)
    near_tile_rows = jnp.broadcast_to(near_tile[:, :, None], (group_size, capacity, 16)).reshape(-1)
    my_requests = lax.dynamic_index_in_dim(requests, device, axis=0, keepdims=False)
    far_wanted = (my_requests[None, :] >= 0) & (
        my_requests[None, :] // piece_count == source_class[:, None]
    )
    far_tile, far_valid = ranked_pick(
        jnp.broadcast_to(my_requests[None, :], (group_size, group_size)), far_wanted, FAR_SLOTS
    )
    far_tile = jnp.where(far_valid, far_tile, -1)
    far_tile_rows = jnp.broadcast_to(
        far_tile[:, :, None], (group_size, FAR_SLOTS, 16)
    ).reshape(-1)
    own_ids = owned_tiles(owner_map, own_rank, device, own_count)
    listed = pick_rows(pattern, own_ids)
    near_ok = jnp.any(listed[:, :, None] == near_tile_rows[None, None, :], axis=1)
    far_ok = jnp.any(listed[:, :, None] == far_tile_rows[None, None, :], axis=1)
    query_own = pick(own_rank, near_tile_rows)
    near_bias = jnp.where(jnp.take(near_ok, query_own, axis=0), 0.0, masked_score)
    far_bias = jnp.where(jnp.take(far_ok, query_own, axis=0), 0.0, masked_score)
    near_bias = near_bias.astype(jnp.float32)
    far_bias = far_bias.astype(jnp.float32)
    chunk_width = channels // HEAD_CHUNKS
    outputs = []
    logs = []
    sources = (
        (key_feats, far_send_rows),
        (value_feats, far_send_rows),
        (query_feats, own_send_rows),
        (key_feats, own_send_rows),
        (value_feats, own_send_rows),
    )
    for chunk in range(HEAD_CHUNKS):
        columns = slice(chunk * chunk_width, (chunk + 1) * chunk_width)
        sent = jnp.concatenate(
            [
                jnp.take(source[:, columns], rows.reshape(-1), axis=0).reshape(
                    group_size, -1, chunk_width
                )
                for source, rows in sources
            ],
            axis=1,
        )
        got = lax.all_to_all(sent, "seq", split_axis=0, concat_axis=0, tiled=True)
        mixed, head_logs = attend(got, unit, near_bias, far_bias)
        returned = lax.all_to_all(mixed, "seq", split_axis=0, concat_axis=0, tiled=True)
        outputs.append(returned.reshape(-1, chunk_width))
        logs.append(head_logs[:, :, 0])
    head_logs = jnp.concatenate(logs, axis=0)
    own_class = own_ids // piece_count
    own_slot = pick(class_rank, own_ids)
    gather_rows = (
        supplier_of(own_class[:, None], slice_iota[None, :], frame_devs) * capacity
        + own_slot[:, None]
    )
    log_rows = (gather_rows[:, :, None] * 16 + token_iota).reshape(-1)
    heads = channels // HEAD_DIM
    log_sums = (
        jnp.take(head_logs, log_rows, axis=1)
        .reshape(heads, own_count, 64)
        .transpose(1, 0, 2)
        .reshape(1, own_count, heads * 64)
    )
    local_iota_rows = jnp.arange(local_rows, dtype=jnp.int32)
    strip = local_iota_rows // (4 * WIDTH)
    height = local_iota_rows % (4 * WIDTH) // WIDTH
    column = local_iota_rows % WIDTH
    piece = strip * blocks + column // 4
    token = height * 4 + column % 4
    back_rows = (pick(my_owner, piece) * capacity + pick(my_slot, piece)) * 16 + token
    attended = jnp.take(jnp.concatenate(outputs, axis=1), back_rows, axis=0)
    return (attended, log_sums)


def solution(mesh):
    placed = (
        P(("groups", "seq"), None),
        P(("groups", "seq"), None),
        P(("groups", "seq"), None),
        P("groups"),
        P("groups", None),
    )
    return jax.shard_map(
        shards,
        mesh=mesh,
        in_specs=placed,
        out_specs=(P(("groups", "seq"), None), P(("groups", "seq"), None, None)),
        check_vma=False,
    )
```

```python
import jax
import jax.numpy as jnp
from jax import lax
from jax.sharding import PartitionSpec as P
from jax.experimental import pallas as pl

HEADS = 20
HEAD_DIM = 128
WIDTH = 64
FRAMES = 16


masked_score = -1e30


def frame_pieces(rows_in, strips):
    channels = rows_in.shape[1]
    shaped = rows_in.reshape(strips, 4, WIDTH // 4, 4, channels)
    return shaped.transpose(0, 2, 1, 3, 4).reshape(strips * (WIDTH // 4), 16, channels)


def frame_rows(pieces, strips):
    channels = pieces.shape[2]
    shaped = pieces.reshape(strips, WIDTH // 4, 4, 4, channels)
    return shaped.transpose(0, 2, 1, 3, 4).reshape(strips * 4 * WIDTH, channels)


def owner_tables(owner_map, group_size, piece_count):
    tile_count = owner_map.shape[0]
    devices = jnp.arange(group_size, dtype=jnp.int32)
    onehot = (owner_map[:, None] == devices[None, :]).astype(jnp.int32)
    running = jnp.cumsum(onehot, axis=0)
    own_rank = jnp.sum(onehot * running, axis=1) - 1
    by_class = owner_map.reshape(tile_count // piece_count, piece_count)
    local_iota = jnp.arange(piece_count, dtype=jnp.int32)
    earlier = (by_class[:, :, None] == by_class[:, None, :]) & (
        local_iota[None, None, :] < local_iota[None, :, None]
    )
    class_rank = jnp.sum(earlier.astype(jnp.int32), axis=2).reshape(tile_count)
    return (own_rank, class_rank)


def owned_tiles(owner_map, own_rank, device, own_count):
    tile_iota = jnp.arange(owner_map.shape[0], dtype=jnp.int32)
    slot_iota = jnp.arange(own_count, dtype=jnp.int32)
    match_rows = (owner_map[None, :] == device) & (own_rank[None, :] == slot_iota[:, None])
    return jnp.sum(jnp.where(match_rows, tile_iota[None, :], 0), axis=1)


def pick(table, index):
    iota = jnp.arange(table.shape[0], dtype=jnp.int32)
    hit = index[..., None] == iota
    return jnp.sum(jnp.where(hit, table, 0), axis=-1).astype(table.dtype)


def pick_rows(table, index):
    iota = jnp.arange(table.shape[0], dtype=jnp.int32)
    hit = (index[..., None] == iota)[..., None]
    return jnp.sum(jnp.where(hit, table, 0), axis=-2).astype(table.dtype)


def request_table(owner_map, pattern, group_size):
    devices = jnp.arange(group_size, dtype=jnp.int32)
    entry_owner = pick(owner_map, pattern)
    foreign = entry_owner != owner_map[:, None]
    entry_hit = (entry_owner[:, :, None] == devices[None, None, :]) & foreign[:, :, None]
    per_tile = jnp.max(jnp.where(entry_hit, pattern[:, :, None], -1), axis=1)
    per_user = owner_map[None, :] == devices[:, None]
    return jnp.max(jnp.where(per_user[:, :, None], per_tile[None, :, :], -1), axis=1)


def supplier_of(tile_class, frame_slice, frame_devs):
    return (4 * (tile_class // frame_devs) + frame_slice) * frame_devs + tile_class % frame_devs


def expand_mask(block_mask):
    query_tiles = block_mask.shape[0]
    key_tiles = block_mask.shape[1]
    wide = jnp.broadcast_to(block_mask[:, None, :, None], (query_tiles, 64, key_tiles, 64))
    return wide.reshape(query_tiles * 64, key_tiles * 64)


def head_part(matrix, offset):
    return lax.dynamic_slice_in_dim(matrix, offset, HEAD_DIM, 1)


def head_scores(query_head, key_rows, offset, mask):
    key_head = head_part(key_rows, offset)
    scores = lax.dot_general(
        query_head, key_head, (((1,), (1,)), ((), ())), preferred_element_type=jnp.float32
    ) * HEAD_DIM ** (-0.5)
    return jnp.where(mask, scores, masked_score)


FAR_SLOTS = 4
INTERPRET = False


def attention_kernel(
    query_ref, near_key_ref, near_value_ref, far_key_ref, far_value_ref, near_bias_ref,
    far_bias_ref, out_ref, log_ref
):
    def flat(ref):
        block = ref[...]
        return block.reshape(block.shape[0] * block.shape[1], block.shape[2])

    query = flat(query_ref)
    dims = (((1,), (1,)), ((), ()))
    scale = HEAD_DIM ** (-0.5)
    near_scores = lax.dot_general(
        query, flat(near_key_ref), dims, preferred_element_type=jnp.float32
    ) * scale + near_bias_ref[...]
    far_scores = lax.dot_general(
        query, flat(far_key_ref), dims, preferred_element_type=jnp.float32
    ) * scale + far_bias_ref[...]
    row_max = jnp.maximum(
        jnp.max(near_scores, axis=1, keepdims=True), jnp.max(far_scores, axis=1, keepdims=True)
    )
    near_exp = jnp.exp(near_scores - row_max)
    far_exp = jnp.exp(far_scores - row_max)
    total = jnp.sum(near_exp, axis=1, keepdims=True) + jnp.sum(far_exp, axis=1, keepdims=True)
    log_total = row_max + jnp.log(total)
    inverse = 1.0 / total
    near_weights = (near_exp * inverse).astype(jnp.bfloat16)
    far_weights = (far_exp * inverse).astype(jnp.bfloat16)
    mixed = jnp.dot(near_weights, flat(near_value_ref), preferred_element_type=jnp.float32)
    mixed = mixed + jnp.dot(far_weights, flat(far_value_ref), preferred_element_type=jnp.float32)
    out_ref[...] = mixed.astype(out_ref.dtype).reshape(out_ref.shape)
    log_ref[...] = log_total


def attend(got_query, got_keys, unit, near_bias, far_bias):
    group_size, clients, _, channels = got_query.shape
    half = got_keys.shape[0]
    far_rows = FAR_SLOTS * 16
    rows = group_size * unit
    heads = channels // HEAD_DIM
    far_base = 4 * unit // far_rows
    query_spec = (group_size, None, unit, HEAD_DIM)
    near_spec = (half, unit, HEAD_DIM)
    far_spec = (half, far_rows, HEAD_DIM)
    return pl.pallas_call(
        attention_kernel,
        grid=(clients, heads),
        in_specs=[
            pl.BlockSpec(query_spec, lambda k, h: (0, k, 0, h)),
            pl.BlockSpec(near_spec, lambda k, h: (0, k, h)),
            pl.BlockSpec(near_spec, lambda k, h: (0, 2 + k, h)),
            pl.BlockSpec(far_spec, lambda k, h: (0, far_base + k, h)),
            pl.BlockSpec(far_spec, lambda k, h: (0, far_base + 2 + k, h)),
            pl.BlockSpec((None, rows, half * unit), lambda k, h: (k, 0, 0)),
            pl.BlockSpec((None, rows, half * far_rows), lambda k, h: (k, 0, 0)),
        ],
        out_specs=[
            pl.BlockSpec(query_spec, lambda k, h: (0, k, 0, h)),
            pl.BlockSpec((None, None, rows, 1), lambda k, h: (k, h, 0, 0)),
        ],
        out_shape=[
            jax.ShapeDtypeStruct((group_size, clients, unit, channels), jnp.float32),
            jax.ShapeDtypeStruct((clients, heads, rows, 1), jnp.float32),
        ],
        interpret=INTERPRET,
    )(got_query, got_keys, got_keys, got_keys, got_keys, near_bias, far_bias)


def class_of(devices, frame_devs):
    return devices // frame_devs // 4 * frame_devs + devices % frame_devs


def ranked_pick(candidates, wanted, slot_count):
    rank = jnp.cumsum(wanted.astype(jnp.int32), axis=-1) - 1
    slots = jnp.arange(slot_count, dtype=jnp.int32)
    hit = wanted[..., None] & (rank[..., None] == slots)
    picked = jnp.sum(jnp.where(hit, candidates[..., None], 0), axis=-2)
    return picked, jnp.any(hit, axis=-2)


def log_add(first, second):
    top = jnp.maximum(first, second)
    return top + jnp.log(jnp.exp(first - top) + jnp.exp(second - top))


def shards(query_feats, key_feats, value_feats, owner_map, pattern):
    group_size = lax.axis_size("seq")
    half = group_size // 2
    device = lax.axis_index("seq")
    local_rows, channels = query_feats.shape
    heads = channels // HEAD_DIM
    strips = local_rows // (4 * WIDTH)
    blocks = WIDTH // 4
    piece_count = strips * blocks
    tile_count = owner_map.shape[0]
    class_count = tile_count // piece_count
    own_count = tile_count // group_size
    capacity = (piece_count + group_size - 1) // group_size
    unit = capacity * 16
    frame_devs = group_size // FRAMES
    devices = jnp.arange(group_size, dtype=jnp.int32)
    shifts = jnp.arange(half, dtype=jnp.int32)
    local_iota = jnp.arange(piece_count, dtype=jnp.int32)
    cap_iota = jnp.arange(capacity, dtype=jnp.int32)
    slice_iota = jnp.arange(4, dtype=jnp.int32)
    token_iota = jnp.arange(16, dtype=jnp.int32)

    def partner(ids):
        return (ids + half) % group_size

    def piece_rows(pieces):
        strip = pieces // blocks
        column = pieces % blocks
        return (
            strip[..., None] * (4 * WIDTH)
            + (token_iota // 4) * WIDTH
            + column[..., None] * 4
            + token_iota % 4
        )

    own_rank, class_rank = owner_tables(owner_map, group_size, piece_count)
    owner_by_class = owner_map.reshape(class_count, piece_count)
    rank_by_class = class_rank.reshape(class_count, piece_count)
    my_class = class_of(device, frame_devs)
    my_owner = lax.dynamic_slice_in_dim(owner_map, my_class * piece_count, piece_count)
    my_slot = lax.dynamic_slice_in_dim(class_rank, my_class * piece_count, piece_count)
    requests = request_table(owner_map, pattern, group_size)

    def my_pieces(owners):
        hit = (my_owner == owners[..., None, None]) & (my_slot == cap_iota[:, None])
        return jnp.sum(jnp.where(hit, local_iota, 0), axis=-1)

    def far_pieces(clients, source_class):
        asked = pick_rows(requests, clients)
        wanted = (asked >= 0) & (asked // piece_count == source_class)
        return ranked_pick(asked, wanted, FAR_SLOTS)

    clients_of = jnp.stack([devices, partner(devices)], axis=1)
    query_rows = piece_rows(my_pieces(clients_of)).reshape(-1)
    half_base = device // half * half
    key_dests = half_base + (device % half + shifts) % half
    dest_clients = pick_rows(clients_of, key_dests)
    near_rows = piece_rows(my_pieces(dest_clients)).reshape(half, -1)
    far_tiles, _ = far_pieces(dest_clients, my_class)
    far_rows = piece_rows(far_tiles % piece_count).reshape(half, -1)
    sent_query = jnp.take(query_feats, query_rows, axis=0).reshape(group_size, -1, channels)
    payload = jnp.concatenate(
        [
            jnp.take(key_feats, near_rows.reshape(-1), axis=0).reshape(half, -1, channels),
            jnp.take(value_feats, near_rows.reshape(-1), axis=0).reshape(half, -1, channels),
            jnp.take(key_feats, far_rows.reshape(-1), axis=0).reshape(half, -1, channels),
            jnp.take(value_feats, far_rows.reshape(-1), axis=0).reshape(half, -1, channels),
        ],
        axis=1,
    )
    got_query = lax.all_to_all(sent_query, "seq", split_axis=0, concat_axis=0, tiled=True)
    got_query = got_query.reshape(group_size, 2, unit, channels)
    received = [payload[0]]
    for shift in range(1, half):
        pairs = [(d, d // half * half + (d % half + shift) % half) for d in range(group_size)]
        received.append(lax.ppermute(payload[shift], "seq", pairs))
    got_keys = jnp.stack(received, axis=0)
    key_sources = half_base + (device % half - shifts) % half
    key_source_class = class_of(key_sources, frame_devs)
    all_class = class_of(devices, frame_devs)
    near_biases = []
    far_biases = []
    for client in (device, partner(device)):
        def own_tiles_of(source_class):
            mine = pick_rows(owner_by_class, source_class) == client
            ranks = pick_rows(rank_by_class, source_class)
            hit = mine[:, None, :] & (ranks[:, None, :] == cap_iota[None, :, None])
            tiles = source_class[:, None, None] * piece_count + local_iota
            return jnp.sum(jnp.where(hit, tiles, 0), axis=2)

        query_tiles = own_tiles_of(all_class)
        query_tile_rows = jnp.broadcast_to(
            query_tiles[:, :, None], (group_size, capacity, 16)
        ).reshape(-1)
        near_tiles = own_tiles_of(key_source_class)
        near_tile_rows = jnp.broadcast_to(near_tiles[:, :, None], (half, capacity, 16)).reshape(-1)
        client_far, client_valid = far_pieces(
            jnp.broadcast_to(client, (half,)), key_source_class[:, None]
        )
        client_far = jnp.where(client_valid, client_far, -1)
        far_tile_rows = jnp.broadcast_to(
            client_far[:, :, None], (half, FAR_SLOTS, 16)
        ).reshape(-1)
        own_ids = owned_tiles(owner_map, own_rank, client, own_count)
        listed = pick_rows(pattern, own_ids)
        near_ok = jnp.any(listed[:, :, None] == near_tile_rows[None, None, :], axis=1)
        far_ok = jnp.any(listed[:, :, None] == far_tile_rows[None, None, :], axis=1)
        query_own = pick(own_rank, query_tile_rows)
        near_biases.append(
            jnp.where(jnp.take(near_ok, query_own, axis=0), 0.0, masked_score).astype(jnp.float32)
        )
        far_biases.append(
            jnp.where(jnp.take(far_ok, query_own, axis=0), 0.0, masked_score).astype(jnp.float32)
        )
    mixed, head_logs = attend(
        got_query, got_keys, unit, jnp.stack(near_biases), jnp.stack(far_biases)
    )
    head_logs = head_logs[..., 0]
    sent_logs = head_logs.reshape(2, heads, group_size, unit).transpose(2, 0, 3, 1)
    returned = lax.all_to_all(mixed, "seq", split_axis=0, concat_axis=0, tiled=True)
    returned_logs = lax.all_to_all(sent_logs, "seq", split_axis=0, concat_axis=0, tiled=True)
    partner_pairs = [(d, (d + half) % group_size) for d in range(group_size)]
    partner_logs = lax.ppermute(head_logs[1], "seq", partner_pairs)
    total_logs = log_add(head_logs[0], partner_logs)
    own_ids = owned_tiles(owner_map, own_rank, device, own_count)
    own_class = own_ids // piece_count
    own_slot = pick(class_rank, own_ids)
    gather_rows = (
        supplier_of(own_class[:, None], slice_iota[None, :], frame_devs) * capacity
        + own_slot[:, None]
    )
    log_rows = (gather_rows[:, :, None] * 16 + token_iota).reshape(-1)
    log_sums = (
        jnp.take(total_logs, log_rows, axis=1)
        .reshape(heads, own_count, 64)
        .transpose(1, 0, 2)
        .reshape(1, own_count, heads * 64)
    )
    local_iota_rows = jnp.arange(local_rows, dtype=jnp.int32)
    strip = local_iota_rows // (4 * WIDTH)
    height = local_iota_rows % (4 * WIDTH) // WIDTH
    column = local_iota_rows % WIDTH
    piece = strip * blocks + column // 4
    token = height * 4 + column % 4
    row_owner = pick(my_owner, piece)
    row_slot = pick(my_slot, piece)
    first_rows = ((row_owner * 2) * capacity + row_slot) * 16 + token
    second_rows = ((partner(row_owner) * 2 + 1) * capacity + row_slot) * 16 + token
    flat_out = returned.reshape(-1, channels)
    flat_logs = returned_logs.reshape(-1, heads)
    first_logs = jnp.take(flat_logs, first_rows, axis=0)
    second_logs = jnp.take(flat_logs, second_rows, axis=0)
    joint = log_add(first_logs, second_logs)
    first_weight = jnp.exp(first_logs - joint)[:, :, None]
    second_weight = jnp.exp(second_logs - joint)[:, :, None]
    first_out = jnp.take(flat_out, first_rows, axis=0)
    second_out = jnp.take(flat_out, second_rows, axis=0)
    attended = (
        first_out.reshape(local_rows, heads, HEAD_DIM) * first_weight
        + second_out.reshape(local_rows, heads, HEAD_DIM) * second_weight
    )
    return (attended.reshape(local_rows, channels).astype(jnp.bfloat16), log_sums)


def solution(mesh):
    placed = (
        P(("groups", "seq"), None),
        P(("groups", "seq"), None),
        P(("groups", "seq"), None),
        P("groups"),
        P("groups", None),
    )
    return jax.shard_map(
        shards,
        mesh=mesh,
        in_specs=placed,
        out_specs=(P(("groups", "seq"), None), P(("groups", "seq"), None, None)),
        check_vma=False,
    )
```

```python
import jax
import jax.numpy as jnp
from jax import lax
from jax.sharding import PartitionSpec as P
from jax.experimental import pallas as pl

HEADS = 20
HEAD_DIM = 128
WIDTH = 64
FRAMES = 16


masked_score = -1e30


def frame_pieces(rows_in, strips):
    channels = rows_in.shape[1]
    shaped = rows_in.reshape(strips, 4, WIDTH // 4, 4, channels)
    return shaped.transpose(0, 2, 1, 3, 4).reshape(strips * (WIDTH // 4), 16, channels)


def frame_rows(pieces, strips):
    channels = pieces.shape[2]
    shaped = pieces.reshape(strips, WIDTH // 4, 4, 4, channels)
    return shaped.transpose(0, 2, 1, 3, 4).reshape(strips * 4 * WIDTH, channels)


def owner_tables(owner_map, group_size, piece_count):
    tile_count = owner_map.shape[0]
    devices = jnp.arange(group_size, dtype=jnp.int32)
    onehot = (owner_map[:, None] == devices[None, :]).astype(jnp.int32)
    running = jnp.cumsum(onehot, axis=0)
    own_rank = jnp.sum(onehot * running, axis=1) - 1
    by_class = owner_map.reshape(tile_count // piece_count, piece_count)
    local_iota = jnp.arange(piece_count, dtype=jnp.int32)
    earlier = (by_class[:, :, None] == by_class[:, None, :]) & (
        local_iota[None, None, :] < local_iota[None, :, None]
    )
    class_rank = jnp.sum(earlier.astype(jnp.int32), axis=2).reshape(tile_count)
    return (own_rank, class_rank)


def owned_tiles(owner_map, own_rank, device, own_count):
    tile_iota = jnp.arange(owner_map.shape[0], dtype=jnp.int32)
    slot_iota = jnp.arange(own_count, dtype=jnp.int32)
    match_rows = (owner_map[None, :] == device) & (own_rank[None, :] == slot_iota[:, None])
    return jnp.sum(jnp.where(match_rows, tile_iota[None, :], 0), axis=1)


def pick(table, index):
    iota = jnp.arange(table.shape[0], dtype=jnp.int32)
    hit = index[..., None] == iota
    return jnp.sum(jnp.where(hit, table, 0), axis=-1).astype(table.dtype)


def pick_rows(table, index):
    iota = jnp.arange(table.shape[0], dtype=jnp.int32)
    hit = (index[..., None] == iota)[..., None]
    return jnp.sum(jnp.where(hit, table, 0), axis=-2).astype(table.dtype)


def request_table(owner_map, pattern, group_size):
    devices = jnp.arange(group_size, dtype=jnp.int32)
    entry_owner = pick(owner_map, pattern)
    foreign = entry_owner != owner_map[:, None]
    entry_hit = (entry_owner[:, :, None] == devices[None, None, :]) & foreign[:, :, None]
    per_tile = jnp.max(jnp.where(entry_hit, pattern[:, :, None], -1), axis=1)
    per_user = owner_map[None, :] == devices[:, None]
    return jnp.max(jnp.where(per_user[:, :, None], per_tile[None, :, :], -1), axis=1)


def supplier_of(tile_class, frame_slice, frame_devs):
    return (4 * (tile_class // frame_devs) + frame_slice) * frame_devs + tile_class % frame_devs


def expand_mask(block_mask):
    query_tiles = block_mask.shape[0]
    key_tiles = block_mask.shape[1]
    wide = jnp.broadcast_to(block_mask[:, None, :, None], (query_tiles, 64, key_tiles, 64))
    return wide.reshape(query_tiles * 64, key_tiles * 64)


def head_part(matrix, offset):
    return lax.dynamic_slice_in_dim(matrix, offset, HEAD_DIM, 1)


def head_scores(query_head, key_rows, offset, mask):
    key_head = head_part(key_rows, offset)
    scores = lax.dot_general(
        query_head, key_head, (((1,), (1,)), ((), ())), preferred_element_type=jnp.float32
    ) * HEAD_DIM ** (-0.5)
    return jnp.where(mask, scores, masked_score)


FAR_SLOTS = 4
HEAD_CHUNKS = 2


def attention_kernel(
    far_key_ref, far_value_ref, query_ref, near_key_ref, near_value_ref, near_bias_ref,
    far_bias_ref, out_ref, log_ref
):
    def flat(ref):
        block = ref[...]
        return block.reshape(block.shape[0] * block.shape[1], block.shape[2])

    query = flat(query_ref)
    dims = (((1,), (1,)), ((), ()))
    scale = HEAD_DIM ** (-0.5)
    near_scores = lax.dot_general(
        query, flat(near_key_ref), dims, preferred_element_type=jnp.float32
    ) * scale + near_bias_ref[...]
    far_scores = lax.dot_general(
        query, flat(far_key_ref), dims, preferred_element_type=jnp.float32
    ) * scale + far_bias_ref[...]
    row_max = jnp.maximum(
        jnp.max(near_scores, axis=1, keepdims=True), jnp.max(far_scores, axis=1, keepdims=True)
    )
    near_exp = jnp.exp(near_scores - row_max)
    far_exp = jnp.exp(far_scores - row_max)
    total = jnp.sum(near_exp, axis=1, keepdims=True) + jnp.sum(far_exp, axis=1, keepdims=True)
    log_total = row_max + jnp.log(total)
    inverse = 1.0 / total
    near_weights = (near_exp * inverse).astype(jnp.bfloat16)
    far_weights = (far_exp * inverse).astype(jnp.bfloat16)
    mixed = jnp.dot(near_weights, flat(near_value_ref), preferred_element_type=jnp.float32)
    mixed = mixed + jnp.dot(far_weights, flat(far_value_ref), preferred_element_type=jnp.float32)
    out_ref[...] = mixed.astype(out_ref.dtype).reshape(out_ref.shape)
    log_ref[...] = log_total


def attend(got, unit, near_bias, far_bias):
    group_size, _, channels = got.shape
    far_rows = FAR_SLOTS * 16
    rows = group_size * unit
    heads = channels // HEAD_DIM
    base = 2 * far_rows // unit
    far_spec = (group_size, far_rows, HEAD_DIM)
    own_spec = (group_size, unit, HEAD_DIM)
    return pl.pallas_call(
        attention_kernel,
        grid=(heads,),
        in_specs=[
            pl.BlockSpec(far_spec, lambda h: (0, 0, h)),
            pl.BlockSpec(far_spec, lambda h: (0, 1, h)),
            pl.BlockSpec(own_spec, lambda h: (0, base, h)),
            pl.BlockSpec(own_spec, lambda h: (0, base + 1, h)),
            pl.BlockSpec(own_spec, lambda h: (0, base + 2, h)),
            pl.BlockSpec((rows, rows), lambda h: (0, 0)),
            pl.BlockSpec((rows, group_size * far_rows), lambda h: (0, 0)),
        ],
        out_specs=[
            pl.BlockSpec(own_spec, lambda h: (0, 0, h)),
            pl.BlockSpec((None, rows, 1), lambda h: (h, 0, 0)),
        ],
        out_shape=[
            jax.ShapeDtypeStruct((group_size, unit, channels), jnp.bfloat16),
            jax.ShapeDtypeStruct((heads, rows, 1), jnp.float32),
        ],
    )(got, got, got, got, got, near_bias, far_bias)


def class_of(devices, frame_devs):
    return devices // frame_devs // 4 * frame_devs + devices % frame_devs


def ranked_pick(candidates, wanted, slot_count):
    rank = jnp.cumsum(wanted.astype(jnp.int32), axis=-1) - 1
    slots = jnp.arange(slot_count, dtype=jnp.int32)
    hit = wanted[..., None] & (rank[..., None] == slots)
    picked = jnp.sum(jnp.where(hit, candidates[..., None], 0), axis=-2)
    return picked, jnp.any(hit, axis=-2)


def shards(query_feats, key_feats, value_feats, owner_map, pattern):
    group_size = lax.axis_size("seq")
    device = lax.axis_index("seq")
    local_rows, channels = query_feats.shape
    strips = local_rows // (4 * WIDTH)
    blocks = WIDTH // 4
    piece_count = strips * blocks
    tile_count = owner_map.shape[0]
    own_count = tile_count // group_size
    capacity = (piece_count + group_size - 1) // group_size
    unit = capacity * 16
    frame_devs = group_size // FRAMES
    devices = jnp.arange(group_size, dtype=jnp.int32)
    local_iota = jnp.arange(piece_count, dtype=jnp.int32)
    cap_iota = jnp.arange(capacity, dtype=jnp.int32)
    slice_iota = jnp.arange(4, dtype=jnp.int32)
    token_iota = jnp.arange(16, dtype=jnp.int32)

    def piece_rows(pieces):
        strip = pieces // blocks
        column = pieces % blocks
        return (
            strip[..., None] * (4 * WIDTH)
            + (token_iota // 4) * WIDTH
            + column[..., None] * 4
            + token_iota % 4
        )

    own_rank, class_rank = owner_tables(owner_map, group_size, piece_count)
    my_class = class_of(device, frame_devs)
    my_tiles = my_class * piece_count + local_iota
    my_owner = lax.dynamic_slice_in_dim(owner_map, my_class * piece_count, piece_count)
    my_slot = lax.dynamic_slice_in_dim(class_rank, my_class * piece_count, piece_count)
    send_hit = (my_owner[None, None, :] == devices[:, None, None]) & (
        my_slot[None, None, :] == cap_iota[None, :, None]
    )
    send_index = jnp.sum(jnp.where(send_hit, local_iota[None, None, :], 0), axis=2)
    own_send_rows = piece_rows(send_index).reshape(group_size, unit)
    requests = request_table(owner_map, pattern, group_size)
    wanted = (requests >= 0) & (requests // piece_count == my_class)
    far_send_piece, _ = ranked_pick(requests % piece_count, wanted, FAR_SLOTS)
    far_send_rows = piece_rows(far_send_piece).reshape(group_size, FAR_SLOTS * 16)
    source_class = class_of(devices, frame_devs)
    class_tiles = source_class[:, None] * piece_count + local_iota[None, :]
    class_count = tile_count // piece_count
    mine = pick_rows(owner_map.reshape(class_count, piece_count), source_class) == device
    near_hit = mine[:, None, :] & (
        pick_rows(class_rank.reshape(class_count, piece_count), source_class)[:, None, :]
        == cap_iota[None, :, None]
    )
    near_tile = jnp.sum(jnp.where(near_hit, class_tiles[:, None, :], 0), axis=2)
    near_tile_rows = jnp.broadcast_to(near_tile[:, :, None], (group_size, capacity, 16)).reshape(-1)
    my_requests = lax.dynamic_index_in_dim(requests, device, axis=0, keepdims=False)
    far_wanted = (my_requests[None, :] >= 0) & (
        my_requests[None, :] // piece_count == source_class[:, None]
    )
    far_tile, far_valid = ranked_pick(
        jnp.broadcast_to(my_requests[None, :], (group_size, group_size)), far_wanted, FAR_SLOTS
    )
    far_tile = jnp.where(far_valid, far_tile, -1)
    far_tile_rows = jnp.broadcast_to(
        far_tile[:, :, None], (group_size, FAR_SLOTS, 16)
    ).reshape(-1)
    own_ids = owned_tiles(owner_map, own_rank, device, own_count)
    listed = pick_rows(pattern, own_ids)
    near_ok = jnp.any(listed[:, :, None] == near_tile_rows[None, None, :], axis=1)
    far_ok = jnp.any(listed[:, :, None] == far_tile_rows[None, None, :], axis=1)
    query_own = pick(own_rank, near_tile_rows)
    near_bias = jnp.where(jnp.take(near_ok, query_own, axis=0), 0.0, masked_score)
    far_bias = jnp.where(jnp.take(far_ok, query_own, axis=0), 0.0, masked_score)
    near_bias = near_bias.astype(jnp.float32)
    far_bias = far_bias.astype(jnp.float32)
    chunk_width = channels // HEAD_CHUNKS
    outputs = []
    logs = []
    taken = lax.optimization_barrier(
        (
            jnp.take(key_feats, far_send_rows.reshape(-1), axis=0).reshape(group_size, -1, channels),
            jnp.take(value_feats, far_send_rows.reshape(-1), axis=0).reshape(group_size, -1, channels),
            jnp.take(query_feats, own_send_rows.reshape(-1), axis=0).reshape(group_size, -1, channels),
            jnp.take(key_feats, own_send_rows.reshape(-1), axis=0).reshape(group_size, -1, channels),
            jnp.take(value_feats, own_send_rows.reshape(-1), axis=0).reshape(group_size, -1, channels),
        )
    )
    for chunk in range(HEAD_CHUNKS):
        columns = slice(chunk * chunk_width, (chunk + 1) * chunk_width)
        sent = jnp.concatenate([part[:, :, columns] for part in taken], axis=1)
        got = lax.all_to_all(sent, "seq", split_axis=0, concat_axis=0, tiled=True)
        mixed, head_logs = attend(got, unit, near_bias, far_bias)
        outputs.append(mixed)
        logs.append(head_logs[:, :, 0])
    head_logs = jnp.concatenate(logs, axis=0)
    own_class = own_ids // piece_count
    own_slot = pick(class_rank, own_ids)
    gather_rows = (
        supplier_of(own_class[:, None], slice_iota[None, :], frame_devs) * capacity
        + own_slot[:, None]
    )
    log_rows = (gather_rows[:, :, None] * 16 + token_iota).reshape(-1)
    heads = channels // HEAD_DIM
    log_sums = (
        jnp.take(head_logs, log_rows, axis=1)
        .reshape(heads, own_count, 64)
        .transpose(1, 0, 2)
        .reshape(1, own_count, heads * 64)
    )
    local_iota_rows = jnp.arange(local_rows, dtype=jnp.int32)
    strip = local_iota_rows // (4 * WIDTH)
    height = local_iota_rows % (4 * WIDTH) // WIDTH
    column = local_iota_rows % WIDTH
    piece = strip * blocks + column // 4
    token = height * 4 + column % 4
    back_rows = (pick(my_owner, piece) * capacity + pick(my_slot, piece)) * 16 + token
    returned = lax.all_to_all(
        jnp.concatenate(outputs, axis=2), "seq", split_axis=0, concat_axis=0, tiled=True
    )
    attended = jnp.take(returned.reshape(-1, channels), back_rows, axis=0)
    return (attended, log_sums)


def solution(mesh):
    placed = (
        P(("groups", "seq"), None),
        P(("groups", "seq"), None),
        P(("groups", "seq"), None),
        P("groups"),
        P("groups", None),
    )
    return jax.shard_map(
        shards,
        mesh=mesh,
        in_specs=placed,
        out_specs=(P(("groups", "seq"), None), P(("groups", "seq"), None, None)),
        check_vma=False,
    )
```

```python
import jax
import jax.numpy as jnp
from jax import lax
from jax.sharding import PartitionSpec as P
from jax.experimental import pallas as pl

HEADS = 20
HEAD_DIM = 128
WIDTH = 64
FRAMES = 16


masked_score = -1e30


def frame_pieces(rows_in, strips):
    channels = rows_in.shape[1]
    shaped = rows_in.reshape(strips, 4, WIDTH // 4, 4, channels)
    return shaped.transpose(0, 2, 1, 3, 4).reshape(strips * (WIDTH // 4), 16, channels)


def frame_rows(pieces, strips):
    channels = pieces.shape[2]
    shaped = pieces.reshape(strips, WIDTH // 4, 4, 4, channels)
    return shaped.transpose(0, 2, 1, 3, 4).reshape(strips * 4 * WIDTH, channels)


def owner_tables(owner_map, group_size, piece_count):
    tile_count = owner_map.shape[0]
    devices = jnp.arange(group_size, dtype=jnp.int32)
    onehot = (owner_map[:, None] == devices[None, :]).astype(jnp.int32)
    running = jnp.cumsum(onehot, axis=0)
    own_rank = jnp.sum(onehot * running, axis=1) - 1
    by_class = owner_map.reshape(tile_count // piece_count, piece_count)
    local_iota = jnp.arange(piece_count, dtype=jnp.int32)
    earlier = (by_class[:, :, None] == by_class[:, None, :]) & (
        local_iota[None, None, :] < local_iota[None, :, None]
    )
    class_rank = jnp.sum(earlier.astype(jnp.int32), axis=2).reshape(tile_count)
    return (own_rank, class_rank)


def owned_tiles(owner_map, own_rank, device, own_count):
    tile_iota = jnp.arange(owner_map.shape[0], dtype=jnp.int32)
    slot_iota = jnp.arange(own_count, dtype=jnp.int32)
    match_rows = (owner_map[None, :] == device) & (own_rank[None, :] == slot_iota[:, None])
    return jnp.sum(jnp.where(match_rows, tile_iota[None, :], 0), axis=1)


def pick(table, index):
    iota = jnp.arange(table.shape[0], dtype=jnp.int32)
    hit = index[..., None] == iota
    return jnp.sum(jnp.where(hit, table, 0), axis=-1).astype(table.dtype)


def pick_rows(table, index):
    iota = jnp.arange(table.shape[0], dtype=jnp.int32)
    hit = (index[..., None] == iota)[..., None]
    return jnp.sum(jnp.where(hit, table, 0), axis=-2).astype(table.dtype)


def request_table(owner_map, pattern, group_size):
    devices = jnp.arange(group_size, dtype=jnp.int32)
    entry_owner = pick(owner_map, pattern)
    foreign = entry_owner != owner_map[:, None]
    entry_hit = (entry_owner[:, :, None] == devices[None, None, :]) & foreign[:, :, None]
    per_tile = jnp.max(jnp.where(entry_hit, pattern[:, :, None], -1), axis=1)
    per_user = owner_map[None, :] == devices[:, None]
    return jnp.max(jnp.where(per_user[:, :, None], per_tile[None, :, :], -1), axis=1)


def supplier_of(tile_class, frame_slice, frame_devs):
    return (4 * (tile_class // frame_devs) + frame_slice) * frame_devs + tile_class % frame_devs


def expand_mask(block_mask):
    query_tiles = block_mask.shape[0]
    key_tiles = block_mask.shape[1]
    wide = jnp.broadcast_to(block_mask[:, None, :, None], (query_tiles, 64, key_tiles, 64))
    return wide.reshape(query_tiles * 64, key_tiles * 64)


def head_part(matrix, offset):
    return lax.dynamic_slice_in_dim(matrix, offset, HEAD_DIM, 1)


def head_scores(query_head, key_rows, offset, mask):
    key_head = head_part(key_rows, offset)
    scores = lax.dot_general(
        query_head, key_head, (((1,), (1,)), ((), ())), preferred_element_type=jnp.float32
    ) * HEAD_DIM ** (-0.5)
    return jnp.where(mask, scores, masked_score)


FAR_SLOTS = 4
INTERPRET = False
HEAD_CHUNKS = 2


def attention_kernel(
    far_key_ref, far_value_ref, query_ref, near_key_ref, near_value_ref, near_bias_ref,
    far_bias_ref, out_ref, log_ref
):
    def flat(ref):
        block = ref[...]
        return block.reshape(block.shape[0] * block.shape[1], block.shape[2])

    query = flat(query_ref)
    dims = (((1,), (1,)), ((), ()))
    scale = HEAD_DIM ** (-0.5)
    near_scores = lax.dot_general(
        query, flat(near_key_ref), dims, preferred_element_type=jnp.float32
    ) * scale + near_bias_ref[...]
    far_scores = lax.dot_general(
        query, flat(far_key_ref), dims, preferred_element_type=jnp.float32
    ) * scale + far_bias_ref[...]
    row_max = jnp.maximum(
        jnp.max(near_scores, axis=1, keepdims=True), jnp.max(far_scores, axis=1, keepdims=True)
    )
    near_exp = jnp.exp(near_scores - row_max)
    far_exp = jnp.exp(far_scores - row_max)
    total = jnp.sum(near_exp, axis=1, keepdims=True) + jnp.sum(far_exp, axis=1, keepdims=True)
    log_total = row_max + jnp.log(total)
    inverse = 1.0 / total
    near_weights = (near_exp * inverse).astype(jnp.bfloat16)
    far_weights = (far_exp * inverse).astype(jnp.bfloat16)
    mixed = jnp.dot(near_weights, flat(near_value_ref), preferred_element_type=jnp.float32)
    mixed = mixed + jnp.dot(far_weights, flat(far_value_ref), preferred_element_type=jnp.float32)
    out_ref[...] = mixed.astype(out_ref.dtype).reshape(out_ref.shape)
    log_ref[...] = log_total


def attend(got, unit, near_bias, far_bias):
    group_size, _, channels = got.shape
    far_rows = FAR_SLOTS * 16
    rows = group_size * unit
    heads = channels // HEAD_DIM
    base = 2 * far_rows // unit
    far_spec = (group_size, far_rows, HEAD_DIM)
    own_spec = (group_size, unit, HEAD_DIM)
    return pl.pallas_call(
        attention_kernel,
        grid=(heads,),
        in_specs=[
            pl.BlockSpec(far_spec, lambda h: (0, 0, h)),
            pl.BlockSpec(far_spec, lambda h: (0, 1, h)),
            pl.BlockSpec(own_spec, lambda h: (0, base, h)),
            pl.BlockSpec(own_spec, lambda h: (0, base + 1, h)),
            pl.BlockSpec(own_spec, lambda h: (0, base + 2, h)),
            pl.BlockSpec((rows, rows), lambda h: (0, 0)),
            pl.BlockSpec((rows, group_size * far_rows), lambda h: (0, 0)),
        ],
        out_specs=[
            pl.BlockSpec(own_spec, lambda h: (0, 0, h)),
            pl.BlockSpec((None, rows, 1), lambda h: (h, 0, 0)),
        ],
        out_shape=[
            jax.ShapeDtypeStruct((group_size, unit, channels), jnp.bfloat16),
            jax.ShapeDtypeStruct((heads, rows, 1), jnp.float32),
        ],
        interpret=INTERPRET,
    )(got, got, got, got, got, near_bias, far_bias)


def pack_kernel(far_hot_ref, own_hot_ref, query_ref, key_ref, value_ref, out_ref):
    far_hot = far_hot_ref[...]
    own_hot = own_hot_ref[...]
    far_rows = far_hot.shape[0]
    own_rows = own_hot.shape[0]

    def select(hot, source_ref):
        return jnp.dot(hot, source_ref[...], preferred_element_type=jnp.float32).astype(
            out_ref.dtype
        )

    out_ref[0:far_rows, :] = select(far_hot, key_ref)
    out_ref[far_rows : 2 * far_rows, :] = select(far_hot, value_ref)
    base = 2 * far_rows
    out_ref[base : base + own_rows, :] = select(own_hot, query_ref)
    out_ref[base + own_rows : base + 2 * own_rows, :] = select(own_hot, key_ref)
    out_ref[base + 2 * own_rows : base + 3 * own_rows, :] = select(own_hot, value_ref)


def pack(far_rows, own_rows, query_feats, key_feats, value_feats, chunks):
    group_size, far_count = far_rows.shape
    own_count = own_rows.shape[1]
    local_rows, channels = query_feats.shape
    width = channels // chunks
    row_iota = jnp.arange(local_rows, dtype=jnp.int32)
    far_hot = (far_rows[:, :, None] == row_iota).astype(jnp.bfloat16)
    own_hot = (own_rows[:, :, None] == row_iota).astype(jnp.bfloat16)
    total = 2 * far_count + 3 * own_count
    source_spec = pl.BlockSpec((local_rows, width), lambda c, j: (0, c))
    return pl.pallas_call(
        pack_kernel,
        grid=(chunks, group_size),
        in_specs=[
            pl.BlockSpec((None, far_count, local_rows), lambda c, j: (j, 0, 0)),
            pl.BlockSpec((None, own_count, local_rows), lambda c, j: (j, 0, 0)),
            source_spec,
            source_spec,
            source_spec,
        ],
        out_specs=pl.BlockSpec((None, None, total, width), lambda c, j: (c, j, 0, 0)),
        out_shape=jax.ShapeDtypeStruct((chunks, group_size, total, width), query_feats.dtype),
        interpret=INTERPRET,
    )(far_hot, own_hot, query_feats, key_feats, value_feats)


def class_of(devices, frame_devs):
    return devices // frame_devs // 4 * frame_devs + devices % frame_devs


def ranked_pick(candidates, wanted, slot_count):
    rank = jnp.cumsum(wanted.astype(jnp.int32), axis=-1) - 1
    slots = jnp.arange(slot_count, dtype=jnp.int32)
    hit = wanted[..., None] & (rank[..., None] == slots)
    picked = jnp.sum(jnp.where(hit, candidates[..., None], 0), axis=-2)
    return picked, jnp.any(hit, axis=-2)


def shards(query_feats, key_feats, value_feats, owner_map, pattern):
    group_size = lax.axis_size("seq")
    device = lax.axis_index("seq")
    local_rows, channels = query_feats.shape
    strips = local_rows // (4 * WIDTH)
    blocks = WIDTH // 4
    piece_count = strips * blocks
    tile_count = owner_map.shape[0]
    own_count = tile_count // group_size
    capacity = (piece_count + group_size - 1) // group_size
    unit = capacity * 16
    frame_devs = group_size // FRAMES
    devices = jnp.arange(group_size, dtype=jnp.int32)
    local_iota = jnp.arange(piece_count, dtype=jnp.int32)
    cap_iota = jnp.arange(capacity, dtype=jnp.int32)
    slice_iota = jnp.arange(4, dtype=jnp.int32)
    token_iota = jnp.arange(16, dtype=jnp.int32)

    def piece_rows(pieces):
        strip = pieces // blocks
        column = pieces % blocks
        return (
            strip[..., None] * (4 * WIDTH)
            + (token_iota // 4) * WIDTH
            + column[..., None] * 4
            + token_iota % 4
        )

    own_rank, class_rank = owner_tables(owner_map, group_size, piece_count)
    my_class = class_of(device, frame_devs)
    my_tiles = my_class * piece_count + local_iota
    my_owner = lax.dynamic_slice_in_dim(owner_map, my_class * piece_count, piece_count)
    my_slot = lax.dynamic_slice_in_dim(class_rank, my_class * piece_count, piece_count)
    send_hit = (my_owner[None, None, :] == devices[:, None, None]) & (
        my_slot[None, None, :] == cap_iota[None, :, None]
    )
    send_index = jnp.sum(jnp.where(send_hit, local_iota[None, None, :], 0), axis=2)
    own_send_rows = piece_rows(send_index).reshape(group_size, unit)
    requests = request_table(owner_map, pattern, group_size)
    wanted = (requests >= 0) & (requests // piece_count == my_class)
    far_send_piece, _ = ranked_pick(requests % piece_count, wanted, FAR_SLOTS)
    far_send_rows = piece_rows(far_send_piece).reshape(group_size, FAR_SLOTS * 16)
    source_class = class_of(devices, frame_devs)
    class_tiles = source_class[:, None] * piece_count + local_iota[None, :]
    class_count = tile_count // piece_count
    mine = pick_rows(owner_map.reshape(class_count, piece_count), source_class) == device
    near_hit = mine[:, None, :] & (
        pick_rows(class_rank.reshape(class_count, piece_count), source_class)[:, None, :]
        == cap_iota[None, :, None]
    )
    near_tile = jnp.sum(jnp.where(near_hit, class_tiles[:, None, :], 0), axis=2)
    near_tile_rows = jnp.broadcast_to(near_tile[:, :, None], (group_size, capacity, 16)).reshape(-1)
    my_requests = lax.dynamic_index_in_dim(requests, device, axis=0, keepdims=False)
    far_wanted = (my_requests[None, :] >= 0) & (
        my_requests[None, :] // piece_count == source_class[:, None]
    )
    far_tile, far_valid = ranked_pick(
        jnp.broadcast_to(my_requests[None, :], (group_size, group_size)), far_wanted, FAR_SLOTS
    )
    far_tile = jnp.where(far_valid, far_tile, -1)
    far_tile_rows = jnp.broadcast_to(
        far_tile[:, :, None], (group_size, FAR_SLOTS, 16)
    ).reshape(-1)
    own_ids = owned_tiles(owner_map, own_rank, device, own_count)
    listed = pick_rows(pattern, own_ids)
    near_ok = jnp.any(listed[:, :, None] == near_tile_rows[None, None, :], axis=1)
    far_ok = jnp.any(listed[:, :, None] == far_tile_rows[None, None, :], axis=1)
    query_own = pick(own_rank, near_tile_rows)
    near_bias = jnp.where(jnp.take(near_ok, query_own, axis=0), 0.0, masked_score)
    far_bias = jnp.where(jnp.take(far_ok, query_own, axis=0), 0.0, masked_score)
    near_bias = near_bias.astype(jnp.float32)
    far_bias = far_bias.astype(jnp.float32)
    chunk_width = channels // HEAD_CHUNKS
    outputs = []
    logs = []
    packed = pack(far_send_rows, own_send_rows, query_feats, key_feats, value_feats, HEAD_CHUNKS)
    for chunk in range(HEAD_CHUNKS):
        sent = packed[chunk]
        got = lax.all_to_all(sent, "seq", split_axis=0, concat_axis=0, tiled=True)
        mixed, head_logs = attend(got, unit, near_bias, far_bias)
        returned = lax.all_to_all(mixed, "seq", split_axis=0, concat_axis=0, tiled=True)
        outputs.append(returned.reshape(-1, chunk_width))
        logs.append(head_logs[:, :, 0])
    head_logs = jnp.concatenate(logs, axis=0)
    own_class = own_ids // piece_count
    own_slot = pick(class_rank, own_ids)
    gather_rows = (
        supplier_of(own_class[:, None], slice_iota[None, :], frame_devs) * capacity
        + own_slot[:, None]
    )
    log_rows = (gather_rows[:, :, None] * 16 + token_iota).reshape(-1)
    heads = channels // HEAD_DIM
    log_sums = (
        jnp.take(head_logs, log_rows, axis=1)
        .reshape(heads, own_count, 64)
        .transpose(1, 0, 2)
        .reshape(1, own_count, heads * 64)
    )
    local_iota_rows = jnp.arange(local_rows, dtype=jnp.int32)
    strip = local_iota_rows // (4 * WIDTH)
    height = local_iota_rows % (4 * WIDTH) // WIDTH
    column = local_iota_rows % WIDTH
    piece = strip * blocks + column // 4
    token = height * 4 + column % 4
    back_rows = (pick(my_owner, piece) * capacity + pick(my_slot, piece)) * 16 + token
    attended = jnp.take(jnp.concatenate(outputs, axis=1), back_rows, axis=0)
    return (attended, log_sums)


def solution(mesh):
    placed = (
        P(("groups", "seq"), None),
        P(("groups", "seq"), None),
        P(("groups", "seq"), None),
        P("groups"),
        P("groups", None),
    )
    return jax.shard_map(
        shards,
        mesh=mesh,
        in_specs=placed,
        out_specs=(P(("groups", "seq"), None), P(("groups", "seq"), None, None)),
        check_vma=False,
    )
```

```python
import jax
import jax.numpy as jnp
from jax import lax
from jax.sharding import PartitionSpec as P
from jax.experimental import pallas as pl

HEADS = 20
HEAD_DIM = 128
WIDTH = 64
FRAMES = 16


masked_score = -1e30


def frame_pieces(rows_in, strips):
    channels = rows_in.shape[1]
    shaped = rows_in.reshape(strips, 4, WIDTH // 4, 4, channels)
    return shaped.transpose(0, 2, 1, 3, 4).reshape(strips * (WIDTH // 4), 16, channels)


def frame_rows(pieces, strips):
    channels = pieces.shape[2]
    shaped = pieces.reshape(strips, WIDTH // 4, 4, 4, channels)
    return shaped.transpose(0, 2, 1, 3, 4).reshape(strips * 4 * WIDTH, channels)


def owner_tables(owner_map, group_size, piece_count):
    tile_count = owner_map.shape[0]
    devices = jnp.arange(group_size, dtype=jnp.int32)
    onehot = (owner_map[:, None] == devices[None, :]).astype(jnp.int32)
    running = jnp.cumsum(onehot, axis=0)
    own_rank = jnp.sum(onehot * running, axis=1) - 1
    by_class = owner_map.reshape(tile_count // piece_count, piece_count)
    local_iota = jnp.arange(piece_count, dtype=jnp.int32)
    earlier = (by_class[:, :, None] == by_class[:, None, :]) & (
        local_iota[None, None, :] < local_iota[None, :, None]
    )
    class_rank = jnp.sum(earlier.astype(jnp.int32), axis=2).reshape(tile_count)
    return (own_rank, class_rank)


def owned_tiles(owner_map, own_rank, device, own_count):
    tile_iota = jnp.arange(owner_map.shape[0], dtype=jnp.int32)
    slot_iota = jnp.arange(own_count, dtype=jnp.int32)
    match_rows = (owner_map[None, :] == device) & (own_rank[None, :] == slot_iota[:, None])
    return jnp.sum(jnp.where(match_rows, tile_iota[None, :], 0), axis=1)


def pick(table, index):
    iota = jnp.arange(table.shape[0], dtype=jnp.int32)
    hit = index[..., None] == iota
    return jnp.sum(jnp.where(hit, table, 0), axis=-1).astype(table.dtype)


def pick_rows(table, index):
    iota = jnp.arange(table.shape[0], dtype=jnp.int32)
    hit = (index[..., None] == iota)[..., None]
    return jnp.sum(jnp.where(hit, table, 0), axis=-2).astype(table.dtype)


def request_table(owner_map, pattern, group_size):
    devices = jnp.arange(group_size, dtype=jnp.int32)
    entry_owner = pick(owner_map, pattern)
    foreign = entry_owner != owner_map[:, None]
    entry_hit = (entry_owner[:, :, None] == devices[None, None, :]) & foreign[:, :, None]
    per_tile = jnp.max(jnp.where(entry_hit, pattern[:, :, None], -1), axis=1)
    per_user = owner_map[None, :] == devices[:, None]
    return jnp.max(jnp.where(per_user[:, :, None], per_tile[None, :, :], -1), axis=1)


def supplier_of(tile_class, frame_slice, frame_devs):
    return (4 * (tile_class // frame_devs) + frame_slice) * frame_devs + tile_class % frame_devs


def expand_mask(block_mask):
    query_tiles = block_mask.shape[0]
    key_tiles = block_mask.shape[1]
    wide = jnp.broadcast_to(block_mask[:, None, :, None], (query_tiles, 64, key_tiles, 64))
    return wide.reshape(query_tiles * 64, key_tiles * 64)


def head_part(matrix, offset):
    return lax.dynamic_slice_in_dim(matrix, offset, HEAD_DIM, 1)


def head_scores(query_head, key_rows, offset, mask):
    key_head = head_part(key_rows, offset)
    scores = lax.dot_general(
        query_head, key_head, (((1,), (1,)), ((), ())), preferred_element_type=jnp.float32
    ) * HEAD_DIM ** (-0.5)
    return jnp.where(mask, scores, masked_score)


FAR_SLOTS = 4
INTERPRET = False
HEAD_CHUNKS = 2


def attention_kernel(
    far_key_ref, far_value_ref, query_ref, near_key_ref, near_value_ref, near_bias_ref,
    far_bias_ref, out_ref, log_ref
):
    def flat(ref):
        block = ref[...]
        return block.reshape(block.shape[0] * block.shape[1], block.shape[2])

    query = flat(query_ref)
    dims = (((1,), (1,)), ((), ()))
    scale = HEAD_DIM ** (-0.5)
    near_scores = lax.dot_general(
        query, flat(near_key_ref), dims, preferred_element_type=jnp.float32
    ) * scale + near_bias_ref[...]
    far_scores = lax.dot_general(
        query, flat(far_key_ref), dims, preferred_element_type=jnp.float32
    ) * scale + far_bias_ref[...]
    row_max = jnp.maximum(
        jnp.max(near_scores, axis=1, keepdims=True), jnp.max(far_scores, axis=1, keepdims=True)
    )
    near_exp = jnp.exp(near_scores - row_max)
    far_exp = jnp.exp(far_scores - row_max)
    total = jnp.sum(near_exp, axis=1, keepdims=True) + jnp.sum(far_exp, axis=1, keepdims=True)
    log_total = row_max + jnp.log(total)
    inverse = 1.0 / total
    near_weights = (near_exp * inverse).astype(jnp.bfloat16)
    far_weights = (far_exp * inverse).astype(jnp.bfloat16)
    mixed = jnp.dot(near_weights, flat(near_value_ref), preferred_element_type=jnp.float32)
    mixed = mixed + jnp.dot(far_weights, flat(far_value_ref), preferred_element_type=jnp.float32)
    out_ref[...] = mixed.astype(out_ref.dtype).reshape(out_ref.shape)
    log_ref[...] = log_total


def attend(got, unit, near_bias, far_bias):
    group_size, _, channels = got.shape
    far_rows = FAR_SLOTS * 16
    rows = group_size * unit
    heads = channels // HEAD_DIM
    base = 2 * far_rows // unit
    far_spec = (group_size, far_rows, HEAD_DIM)
    own_spec = (group_size, unit, HEAD_DIM)
    return pl.pallas_call(
        attention_kernel,
        grid=(heads,),
        in_specs=[
            pl.BlockSpec(far_spec, lambda h: (0, 0, h)),
            pl.BlockSpec(far_spec, lambda h: (0, 1, h)),
            pl.BlockSpec(own_spec, lambda h: (0, base, h)),
            pl.BlockSpec(own_spec, lambda h: (0, base + 1, h)),
            pl.BlockSpec(own_spec, lambda h: (0, base + 2, h)),
            pl.BlockSpec((rows, rows), lambda h: (0, 0)),
            pl.BlockSpec((rows, group_size * far_rows), lambda h: (0, 0)),
        ],
        out_specs=[
            pl.BlockSpec(own_spec, lambda h: (0, 0, h)),
            pl.BlockSpec((None, rows, 1), lambda h: (h, 0, 0)),
        ],
        out_shape=[
            jax.ShapeDtypeStruct((group_size, unit, channels), jnp.bfloat16),
            jax.ShapeDtypeStruct((heads, rows, 1), jnp.float32),
        ],
        interpret=INTERPRET,
    )(got, got, got, got, got, near_bias, far_bias)


PACK_DESTS = 4


def pack_kernel(far_hot_ref, own_hot_ref, query_ref, key_ref, value_ref, *out_refs):
    far_hot = far_hot_ref[...]
    own_hot = own_hot_ref[...]
    dests, far_rows, local_rows = far_hot.shape
    own_rows = own_hot.shape[1]
    far_hot = far_hot.reshape(dests * far_rows, local_rows)
    own_hot = own_hot.reshape(dests * own_rows, local_rows)
    base = 2 * far_rows
    for index, out_ref in enumerate(out_refs):
        width = out_ref.shape[2]
        columns = slice(index * width, (index + 1) * width)

        def select(hot, source_ref, rows):
            picked = jnp.dot(hot, source_ref[:, columns], preferred_element_type=jnp.float32)
            return picked.astype(out_ref.dtype).reshape(dests, rows, width)

        out_ref[:, 0:far_rows, :] = select(far_hot, key_ref, far_rows)
        out_ref[:, far_rows:base, :] = select(far_hot, value_ref, far_rows)
        out_ref[:, base : base + own_rows, :] = select(own_hot, query_ref, own_rows)
        out_ref[:, base + own_rows : base + 2 * own_rows, :] = select(own_hot, key_ref, own_rows)
        out_ref[:, base + 2 * own_rows : base + 3 * own_rows, :] = select(
            own_hot, value_ref, own_rows
        )


def pack(far_rows, own_rows, query_feats, key_feats, value_feats, chunks):
    group_size, far_count = far_rows.shape
    own_count = own_rows.shape[1]
    local_rows, channels = query_feats.shape
    width = channels // chunks
    dests = PACK_DESTS if group_size % PACK_DESTS == 0 else 1
    row_iota = jnp.arange(local_rows, dtype=jnp.int32)
    far_hot = (far_rows[:, :, None] == row_iota).astype(jnp.bfloat16)
    own_hot = (own_rows[:, :, None] == row_iota).astype(jnp.bfloat16)
    total = 2 * far_count + 3 * own_count
    source_spec = pl.BlockSpec((local_rows, channels), lambda j: (0, 0))
    out_spec = pl.BlockSpec((dests, total, width), lambda j: (j, 0, 0))
    return pl.pallas_call(
        pack_kernel,
        grid=(group_size // dests,),
        in_specs=[
            pl.BlockSpec((dests, far_count, local_rows), lambda j: (j, 0, 0)),
            pl.BlockSpec((dests, own_count, local_rows), lambda j: (j, 0, 0)),
            source_spec,
            source_spec,
            source_spec,
        ],
        out_specs=[out_spec] * chunks,
        out_shape=[jax.ShapeDtypeStruct((group_size, total, width), query_feats.dtype)] * chunks,
        interpret=INTERPRET,
    )(far_hot, own_hot, query_feats, key_feats, value_feats)


def class_of(devices, frame_devs):
    return devices // frame_devs // 4 * frame_devs + devices % frame_devs


def ranked_pick(candidates, wanted, slot_count):
    rank = jnp.cumsum(wanted.astype(jnp.int32), axis=-1) - 1
    slots = jnp.arange(slot_count, dtype=jnp.int32)
    hit = wanted[..., None] & (rank[..., None] == slots)
    picked = jnp.sum(jnp.where(hit, candidates[..., None], 0), axis=-2)
    return picked, jnp.any(hit, axis=-2)


def shards(query_feats, key_feats, value_feats, owner_map, pattern):
    group_size = lax.axis_size("seq")
    device = lax.axis_index("seq")
    local_rows, channels = query_feats.shape
    strips = local_rows // (4 * WIDTH)
    blocks = WIDTH // 4
    piece_count = strips * blocks
    tile_count = owner_map.shape[0]
    own_count = tile_count // group_size
    capacity = (piece_count + group_size - 1) // group_size
    unit = capacity * 16
    frame_devs = group_size // FRAMES
    devices = jnp.arange(group_size, dtype=jnp.int32)
    local_iota = jnp.arange(piece_count, dtype=jnp.int32)
    cap_iota = jnp.arange(capacity, dtype=jnp.int32)
    slice_iota = jnp.arange(4, dtype=jnp.int32)
    token_iota = jnp.arange(16, dtype=jnp.int32)

    def piece_rows(pieces):
        strip = pieces // blocks
        column = pieces % blocks
        return (
            strip[..., None] * (4 * WIDTH)
            + (token_iota // 4) * WIDTH
            + column[..., None] * 4
            + token_iota % 4
        )

    own_rank, class_rank = owner_tables(owner_map, group_size, piece_count)
    my_class = class_of(device, frame_devs)
    my_tiles = my_class * piece_count + local_iota
    my_owner = lax.dynamic_slice_in_dim(owner_map, my_class * piece_count, piece_count)
    my_slot = lax.dynamic_slice_in_dim(class_rank, my_class * piece_count, piece_count)
    send_hit = (my_owner[None, None, :] == devices[:, None, None]) & (
        my_slot[None, None, :] == cap_iota[None, :, None]
    )
    send_index = jnp.sum(jnp.where(send_hit, local_iota[None, None, :], 0), axis=2)
    own_send_rows = piece_rows(send_index).reshape(group_size, unit)
    requests = request_table(owner_map, pattern, group_size)
    wanted = (requests >= 0) & (requests // piece_count == my_class)
    far_send_piece, _ = ranked_pick(requests % piece_count, wanted, FAR_SLOTS)
    far_send_rows = piece_rows(far_send_piece).reshape(group_size, FAR_SLOTS * 16)
    source_class = class_of(devices, frame_devs)
    class_tiles = source_class[:, None] * piece_count + local_iota[None, :]
    class_count = tile_count // piece_count
    mine = pick_rows(owner_map.reshape(class_count, piece_count), source_class) == device
    near_hit = mine[:, None, :] & (
        pick_rows(class_rank.reshape(class_count, piece_count), source_class)[:, None, :]
        == cap_iota[None, :, None]
    )
    near_tile = jnp.sum(jnp.where(near_hit, class_tiles[:, None, :], 0), axis=2)
    near_tile_rows = jnp.broadcast_to(near_tile[:, :, None], (group_size, capacity, 16)).reshape(-1)
    my_requests = lax.dynamic_index_in_dim(requests, device, axis=0, keepdims=False)
    far_wanted = (my_requests[None, :] >= 0) & (
        my_requests[None, :] // piece_count == source_class[:, None]
    )
    far_tile, far_valid = ranked_pick(
        jnp.broadcast_to(my_requests[None, :], (group_size, group_size)), far_wanted, FAR_SLOTS
    )
    far_tile = jnp.where(far_valid, far_tile, -1)
    far_tile_rows = jnp.broadcast_to(
        far_tile[:, :, None], (group_size, FAR_SLOTS, 16)
    ).reshape(-1)
    own_ids = owned_tiles(owner_map, own_rank, device, own_count)
    listed = pick_rows(pattern, own_ids)
    near_ok = jnp.any(listed[:, :, None] == near_tile_rows[None, None, :], axis=1)
    far_ok = jnp.any(listed[:, :, None] == far_tile_rows[None, None, :], axis=1)
    query_own = pick(own_rank, near_tile_rows)
    near_bias = jnp.where(jnp.take(near_ok, query_own, axis=0), 0.0, masked_score)
    far_bias = jnp.where(jnp.take(far_ok, query_own, axis=0), 0.0, masked_score)
    near_bias = near_bias.astype(jnp.float32)
    far_bias = far_bias.astype(jnp.float32)
    chunk_width = channels // HEAD_CHUNKS
    outputs = []
    logs = []
    packed = pack(far_send_rows, own_send_rows, query_feats, key_feats, value_feats, HEAD_CHUNKS)
    for chunk in range(HEAD_CHUNKS):
        sent = packed[chunk]
        got = lax.all_to_all(sent, "seq", split_axis=0, concat_axis=0, tiled=True)
        mixed, head_logs = attend(got, unit, near_bias, far_bias)
        returned = lax.all_to_all(mixed, "seq", split_axis=0, concat_axis=0, tiled=True)
        outputs.append(returned.reshape(-1, chunk_width))
        logs.append(head_logs[:, :, 0])
    head_logs = jnp.concatenate(logs, axis=0)
    own_class = own_ids // piece_count
    own_slot = pick(class_rank, own_ids)
    gather_rows = (
        supplier_of(own_class[:, None], slice_iota[None, :], frame_devs) * capacity
        + own_slot[:, None]
    )
    log_rows = (gather_rows[:, :, None] * 16 + token_iota).reshape(-1)
    heads = channels // HEAD_DIM
    log_sums = (
        jnp.take(head_logs, log_rows, axis=1)
        .reshape(heads, own_count, 64)
        .transpose(1, 0, 2)
        .reshape(1, own_count, heads * 64)
    )
    local_iota_rows = jnp.arange(local_rows, dtype=jnp.int32)
    strip = local_iota_rows // (4 * WIDTH)
    height = local_iota_rows % (4 * WIDTH) // WIDTH
    column = local_iota_rows % WIDTH
    piece = strip * blocks + column // 4
    token = height * 4 + column % 4
    back_rows = (pick(my_owner, piece) * capacity + pick(my_slot, piece)) * 16 + token
    attended = jnp.take(jnp.concatenate(outputs, axis=1), back_rows, axis=0)
    return (attended, log_sums)


def solution(mesh):
    placed = (
        P(("groups", "seq"), None),
        P(("groups", "seq"), None),
        P(("groups", "seq"), None),
        P("groups"),
        P("groups", None),
    )
    return jax.shard_map(
        shards,
        mesh=mesh,
        in_specs=placed,
        out_specs=(P(("groups", "seq"), None), P(("groups", "seq"), None, None)),
        check_vma=False,
    )
```

```python
import jax
import jax.numpy as jnp
from jax import lax
from jax.sharding import PartitionSpec as P
from jax.experimental import pallas as pl

HEADS = 20
HEAD_DIM = 128
WIDTH = 64
FRAMES = 16


masked_score = -1e30


def frame_pieces(rows_in, strips):
    channels = rows_in.shape[1]
    shaped = rows_in.reshape(strips, 4, WIDTH // 4, 4, channels)
    return shaped.transpose(0, 2, 1, 3, 4).reshape(strips * (WIDTH // 4), 16, channels)


def frame_rows(pieces, strips):
    channels = pieces.shape[2]
    shaped = pieces.reshape(strips, WIDTH // 4, 4, 4, channels)
    return shaped.transpose(0, 2, 1, 3, 4).reshape(strips * 4 * WIDTH, channels)


def owner_tables(owner_map, group_size, piece_count):
    tile_count = owner_map.shape[0]
    devices = jnp.arange(group_size, dtype=jnp.int32)
    onehot = (owner_map[:, None] == devices[None, :]).astype(jnp.int32)
    running = jnp.cumsum(onehot, axis=0)
    own_rank = jnp.sum(onehot * running, axis=1) - 1
    by_class = owner_map.reshape(tile_count // piece_count, piece_count)
    local_iota = jnp.arange(piece_count, dtype=jnp.int32)
    earlier = (by_class[:, :, None] == by_class[:, None, :]) & (
        local_iota[None, None, :] < local_iota[None, :, None]
    )
    class_rank = jnp.sum(earlier.astype(jnp.int32), axis=2).reshape(tile_count)
    return (own_rank, class_rank)


def owned_tiles(owner_map, own_rank, device, own_count):
    tile_iota = jnp.arange(owner_map.shape[0], dtype=jnp.int32)
    slot_iota = jnp.arange(own_count, dtype=jnp.int32)
    match_rows = (owner_map[None, :] == device) & (own_rank[None, :] == slot_iota[:, None])
    return jnp.sum(jnp.where(match_rows, tile_iota[None, :], 0), axis=1)


def pick(table, index):
    iota = jnp.arange(table.shape[0], dtype=jnp.int32)
    hit = index[..., None] == iota
    return jnp.sum(jnp.where(hit, table, 0), axis=-1).astype(table.dtype)


def pick_rows(table, index):
    iota = jnp.arange(table.shape[0], dtype=jnp.int32)
    hit = (index[..., None] == iota)[..., None]
    return jnp.sum(jnp.where(hit, table, 0), axis=-2).astype(table.dtype)


def request_table(owner_map, pattern, group_size):
    devices = jnp.arange(group_size, dtype=jnp.int32)
    entry_owner = pick(owner_map, pattern)
    foreign = entry_owner != owner_map[:, None]
    entry_hit = (entry_owner[:, :, None] == devices[None, None, :]) & foreign[:, :, None]
    per_tile = jnp.max(jnp.where(entry_hit, pattern[:, :, None], -1), axis=1)
    per_user = owner_map[None, :] == devices[:, None]
    return jnp.max(jnp.where(per_user[:, :, None], per_tile[None, :, :], -1), axis=1)


def supplier_of(tile_class, frame_slice, frame_devs):
    return (4 * (tile_class // frame_devs) + frame_slice) * frame_devs + tile_class % frame_devs


def expand_mask(block_mask):
    query_tiles = block_mask.shape[0]
    key_tiles = block_mask.shape[1]
    wide = jnp.broadcast_to(block_mask[:, None, :, None], (query_tiles, 64, key_tiles, 64))
    return wide.reshape(query_tiles * 64, key_tiles * 64)


def head_part(matrix, offset):
    return lax.dynamic_slice_in_dim(matrix, offset, HEAD_DIM, 1)


def head_scores(query_head, key_rows, offset, mask):
    key_head = head_part(key_rows, offset)
    scores = lax.dot_general(
        query_head, key_head, (((1,), (1,)), ((), ())), preferred_element_type=jnp.float32
    ) * HEAD_DIM ** (-0.5)
    return jnp.where(mask, scores, masked_score)


FAR_SLOTS = 4
INTERPRET = False
HEAD_CHUNKS = 2
LAST_SPLITS = 2


def attention_kernel(
    far_key_ref, far_value_ref, query_ref, near_key_ref, near_value_ref, near_bias_ref,
    far_bias_ref, out_ref, log_ref
):
    def flat(ref):
        block = ref[...]
        return block.reshape(block.shape[0] * block.shape[1], block.shape[2])

    query = flat(query_ref)
    dims = (((1,), (1,)), ((), ()))
    scale = HEAD_DIM ** (-0.5)
    near_scores = lax.dot_general(
        query, flat(near_key_ref), dims, preferred_element_type=jnp.float32
    ) * scale + near_bias_ref[...]
    far_scores = lax.dot_general(
        query, flat(far_key_ref), dims, preferred_element_type=jnp.float32
    ) * scale + far_bias_ref[...]
    row_max = jnp.maximum(
        jnp.max(near_scores, axis=1, keepdims=True), jnp.max(far_scores, axis=1, keepdims=True)
    )
    near_exp = jnp.exp(near_scores - row_max)
    far_exp = jnp.exp(far_scores - row_max)
    total = jnp.sum(near_exp, axis=1, keepdims=True) + jnp.sum(far_exp, axis=1, keepdims=True)
    log_total = row_max + jnp.log(total)
    inverse = 1.0 / total
    near_weights = (near_exp * inverse).astype(jnp.bfloat16)
    far_weights = (far_exp * inverse).astype(jnp.bfloat16)
    mixed = jnp.dot(near_weights, flat(near_value_ref), preferred_element_type=jnp.float32)
    mixed = mixed + jnp.dot(far_weights, flat(far_value_ref), preferred_element_type=jnp.float32)
    out_ref[...] = mixed.astype(out_ref.dtype).reshape(out_ref.shape)
    log_ref[...] = log_total


def attend(got, unit, near_bias, far_bias, first_head, heads):
    group_size, _, channels = got.shape
    far_rows = FAR_SLOTS * 16
    rows = group_size * unit
    base = 2 * far_rows // unit
    far_spec = (group_size, far_rows, HEAD_DIM)
    own_spec = (group_size, unit, HEAD_DIM)
    return pl.pallas_call(
        attention_kernel,
        grid=(heads,),
        in_specs=[
            pl.BlockSpec(far_spec, lambda h: (0, 0, first_head + h)),
            pl.BlockSpec(far_spec, lambda h: (0, 1, first_head + h)),
            pl.BlockSpec(own_spec, lambda h: (0, base, first_head + h)),
            pl.BlockSpec(own_spec, lambda h: (0, base + 1, first_head + h)),
            pl.BlockSpec(own_spec, lambda h: (0, base + 2, first_head + h)),
            pl.BlockSpec((rows, rows), lambda h: (0, 0)),
            pl.BlockSpec((rows, group_size * far_rows), lambda h: (0, 0)),
        ],
        out_specs=[
            pl.BlockSpec(own_spec, lambda h: (0, 0, h)),
            pl.BlockSpec((None, rows, 1), lambda h: (h, 0, 0)),
        ],
        out_shape=[
            jax.ShapeDtypeStruct((group_size, unit, heads * HEAD_DIM), jnp.bfloat16),
            jax.ShapeDtypeStruct((heads, rows, 1), jnp.float32),
        ],
        interpret=INTERPRET,
    )(got, got, got, got, got, near_bias, far_bias)


PACK_DESTS = 4


def pack_kernel(far_hot_ref, own_hot_ref, query_ref, key_ref, value_ref, *out_refs):
    far_hot = far_hot_ref[...]
    own_hot = own_hot_ref[...]
    dests, far_rows, local_rows = far_hot.shape
    own_rows = own_hot.shape[1]
    far_hot = far_hot.reshape(dests * far_rows, local_rows)
    own_hot = own_hot.reshape(dests * own_rows, local_rows)
    base = 2 * far_rows
    for index, out_ref in enumerate(out_refs):
        width = out_ref.shape[2]
        columns = slice(index * width, (index + 1) * width)

        def select(hot, source_ref, rows):
            picked = jnp.dot(hot, source_ref[:, columns], preferred_element_type=jnp.float32)
            return picked.astype(out_ref.dtype).reshape(dests, rows, width)

        out_ref[:, 0:far_rows, :] = select(far_hot, key_ref, far_rows)
        out_ref[:, far_rows:base, :] = select(far_hot, value_ref, far_rows)
        out_ref[:, base : base + own_rows, :] = select(own_hot, query_ref, own_rows)
        out_ref[:, base + own_rows : base + 2 * own_rows, :] = select(own_hot, key_ref, own_rows)
        out_ref[:, base + 2 * own_rows : base + 3 * own_rows, :] = select(
            own_hot, value_ref, own_rows
        )


def pack(far_rows, own_rows, query_feats, key_feats, value_feats, chunks):
    group_size, far_count = far_rows.shape
    own_count = own_rows.shape[1]
    local_rows, channels = query_feats.shape
    width = channels // chunks
    dests = PACK_DESTS if group_size % PACK_DESTS == 0 else 1
    row_iota = jnp.arange(local_rows, dtype=jnp.int32)
    far_hot = (far_rows[:, :, None] == row_iota).astype(jnp.bfloat16)
    own_hot = (own_rows[:, :, None] == row_iota).astype(jnp.bfloat16)
    total = 2 * far_count + 3 * own_count
    source_spec = pl.BlockSpec((local_rows, channels), lambda j: (0, 0))
    out_spec = pl.BlockSpec((dests, total, width), lambda j: (j, 0, 0))
    return pl.pallas_call(
        pack_kernel,
        grid=(group_size // dests,),
        in_specs=[
            pl.BlockSpec((dests, far_count, local_rows), lambda j: (j, 0, 0)),
            pl.BlockSpec((dests, own_count, local_rows), lambda j: (j, 0, 0)),
            source_spec,
            source_spec,
            source_spec,
        ],
        out_specs=[out_spec] * chunks,
        out_shape=[jax.ShapeDtypeStruct((group_size, total, width), query_feats.dtype)] * chunks,
        interpret=INTERPRET,
    )(far_hot, own_hot, query_feats, key_feats, value_feats)


def class_of(devices, frame_devs):
    return devices // frame_devs // 4 * frame_devs + devices % frame_devs


def ranked_pick(candidates, wanted, slot_count):
    rank = jnp.cumsum(wanted.astype(jnp.int32), axis=-1) - 1
    slots = jnp.arange(slot_count, dtype=jnp.int32)
    hit = wanted[..., None] & (rank[..., None] == slots)
    picked = jnp.sum(jnp.where(hit, candidates[..., None], 0), axis=-2)
    return picked, jnp.any(hit, axis=-2)


def shards(query_feats, key_feats, value_feats, owner_map, pattern):
    group_size = lax.axis_size("seq")
    device = lax.axis_index("seq")
    local_rows, channels = query_feats.shape
    strips = local_rows // (4 * WIDTH)
    blocks = WIDTH // 4
    piece_count = strips * blocks
    tile_count = owner_map.shape[0]
    own_count = tile_count // group_size
    capacity = (piece_count + group_size - 1) // group_size
    unit = capacity * 16
    frame_devs = group_size // FRAMES
    devices = jnp.arange(group_size, dtype=jnp.int32)
    local_iota = jnp.arange(piece_count, dtype=jnp.int32)
    cap_iota = jnp.arange(capacity, dtype=jnp.int32)
    slice_iota = jnp.arange(4, dtype=jnp.int32)
    token_iota = jnp.arange(16, dtype=jnp.int32)

    def piece_rows(pieces):
        strip = pieces // blocks
        column = pieces % blocks
        return (
            strip[..., None] * (4 * WIDTH)
            + (token_iota // 4) * WIDTH
            + column[..., None] * 4
            + token_iota % 4
        )

    own_rank, class_rank = owner_tables(owner_map, group_size, piece_count)
    my_class = class_of(device, frame_devs)
    my_tiles = my_class * piece_count + local_iota
    my_owner = lax.dynamic_slice_in_dim(owner_map, my_class * piece_count, piece_count)
    my_slot = lax.dynamic_slice_in_dim(class_rank, my_class * piece_count, piece_count)
    send_hit = (my_owner[None, None, :] == devices[:, None, None]) & (
        my_slot[None, None, :] == cap_iota[None, :, None]
    )
    send_index = jnp.sum(jnp.where(send_hit, local_iota[None, None, :], 0), axis=2)
    own_send_rows = piece_rows(send_index).reshape(group_size, unit)
    requests = request_table(owner_map, pattern, group_size)
    wanted = (requests >= 0) & (requests // piece_count == my_class)
    far_send_piece, _ = ranked_pick(requests % piece_count, wanted, FAR_SLOTS)
    far_send_rows = piece_rows(far_send_piece).reshape(group_size, FAR_SLOTS * 16)
    source_class = class_of(devices, frame_devs)
    class_tiles = source_class[:, None] * piece_count + local_iota[None, :]
    class_count = tile_count // piece_count
    mine = pick_rows(owner_map.reshape(class_count, piece_count), source_class) == device
    near_hit = mine[:, None, :] & (
        pick_rows(class_rank.reshape(class_count, piece_count), source_class)[:, None, :]
        == cap_iota[None, :, None]
    )
    near_tile = jnp.sum(jnp.where(near_hit, class_tiles[:, None, :], 0), axis=2)
    near_tile_rows = jnp.broadcast_to(near_tile[:, :, None], (group_size, capacity, 16)).reshape(-1)
    my_requests = lax.dynamic_index_in_dim(requests, device, axis=0, keepdims=False)
    far_wanted = (my_requests[None, :] >= 0) & (
        my_requests[None, :] // piece_count == source_class[:, None]
    )
    far_tile, far_valid = ranked_pick(
        jnp.broadcast_to(my_requests[None, :], (group_size, group_size)), far_wanted, FAR_SLOTS
    )
    far_tile = jnp.where(far_valid, far_tile, -1)
    far_tile_rows = jnp.broadcast_to(
        far_tile[:, :, None], (group_size, FAR_SLOTS, 16)
    ).reshape(-1)
    own_ids = owned_tiles(owner_map, own_rank, device, own_count)
    listed = pick_rows(pattern, own_ids)
    near_ok = jnp.any(listed[:, :, None] == near_tile_rows[None, None, :], axis=1)
    far_ok = jnp.any(listed[:, :, None] == far_tile_rows[None, None, :], axis=1)
    query_own = pick(own_rank, near_tile_rows)
    near_bias = jnp.where(jnp.take(near_ok, query_own, axis=0), 0.0, masked_score)
    far_bias = jnp.where(jnp.take(far_ok, query_own, axis=0), 0.0, masked_score)
    near_bias = near_bias.astype(jnp.float32)
    far_bias = far_bias.astype(jnp.float32)
    chunk_width = channels // HEAD_CHUNKS
    outputs = []
    logs = []
    packed = pack(far_send_rows, own_send_rows, query_feats, key_feats, value_feats, HEAD_CHUNKS)
    for chunk in range(HEAD_CHUNKS):
        sent = packed[chunk]
        got = lax.all_to_all(sent, "seq", split_axis=0, concat_axis=0, tiled=True)
        chunk_heads = chunk_width // HEAD_DIM
        parts = LAST_SPLITS if chunk == HEAD_CHUNKS - 1 else 1
        for part in range(parts):
            part_heads = chunk_heads // parts
            mixed, head_logs = attend(
                got, unit, near_bias, far_bias, part * part_heads, part_heads
            )
            returned = lax.all_to_all(mixed, "seq", split_axis=0, concat_axis=0, tiled=True)
            outputs.append(returned.reshape(-1, part_heads * HEAD_DIM))
            logs.append(head_logs[:, :, 0])
    head_logs = jnp.concatenate(logs, axis=0)
    own_class = own_ids // piece_count
    own_slot = pick(class_rank, own_ids)
    gather_rows = (
        supplier_of(own_class[:, None], slice_iota[None, :], frame_devs) * capacity
        + own_slot[:, None]
    )
    log_rows = (gather_rows[:, :, None] * 16 + token_iota).reshape(-1)
    heads = channels // HEAD_DIM
    log_sums = (
        jnp.take(head_logs, log_rows, axis=1)
        .reshape(heads, own_count, 64)
        .transpose(1, 0, 2)
        .reshape(1, own_count, heads * 64)
    )
    local_iota_rows = jnp.arange(local_rows, dtype=jnp.int32)
    strip = local_iota_rows // (4 * WIDTH)
    height = local_iota_rows % (4 * WIDTH) // WIDTH
    column = local_iota_rows % WIDTH
    piece = strip * blocks + column // 4
    token = height * 4 + column % 4
    back_rows = (pick(my_owner, piece) * capacity + pick(my_slot, piece)) * 16 + token
    attended = jnp.take(jnp.concatenate(outputs, axis=1), back_rows, axis=0)
    return (attended, log_sums)


def solution(mesh):
    placed = (
        P(("groups", "seq"), None),
        P(("groups", "seq"), None),
        P(("groups", "seq"), None),
        P("groups"),
        P("groups", None),
    )
    return jax.shard_map(
        shards,
        mesh=mesh,
        in_specs=placed,
        out_specs=(P(("groups", "seq"), None), P(("groups", "seq"), None, None)),
        check_vma=False,
    )
```

```python
import jax
import jax.numpy as jnp
from jax import lax
from jax.sharding import PartitionSpec as P
from jax.experimental import pallas as pl

HEADS = 20
HEAD_DIM = 128
WIDTH = 64
FRAMES = 16


masked_score = -1e30


def frame_pieces(rows_in, strips):
    channels = rows_in.shape[1]
    shaped = rows_in.reshape(strips, 4, WIDTH // 4, 4, channels)
    return shaped.transpose(0, 2, 1, 3, 4).reshape(strips * (WIDTH // 4), 16, channels)


def frame_rows(pieces, strips):
    channels = pieces.shape[2]
    shaped = pieces.reshape(strips, WIDTH // 4, 4, 4, channels)
    return shaped.transpose(0, 2, 1, 3, 4).reshape(strips * 4 * WIDTH, channels)


def owner_tables(owner_map, group_size, piece_count):
    tile_count = owner_map.shape[0]
    devices = jnp.arange(group_size, dtype=jnp.int32)
    onehot = (owner_map[:, None] == devices[None, :]).astype(jnp.int32)
    running = jnp.cumsum(onehot, axis=0)
    own_rank = jnp.sum(onehot * running, axis=1) - 1
    by_class = owner_map.reshape(tile_count // piece_count, piece_count)
    local_iota = jnp.arange(piece_count, dtype=jnp.int32)
    earlier = (by_class[:, :, None] == by_class[:, None, :]) & (
        local_iota[None, None, :] < local_iota[None, :, None]
    )
    class_rank = jnp.sum(earlier.astype(jnp.int32), axis=2).reshape(tile_count)
    return (own_rank, class_rank)


def owned_tiles(owner_map, own_rank, device, own_count):
    tile_iota = jnp.arange(owner_map.shape[0], dtype=jnp.int32)
    slot_iota = jnp.arange(own_count, dtype=jnp.int32)
    match_rows = (owner_map[None, :] == device) & (own_rank[None, :] == slot_iota[:, None])
    return jnp.sum(jnp.where(match_rows, tile_iota[None, :], 0), axis=1)


def pick(table, index):
    iota = jnp.arange(table.shape[0], dtype=jnp.int32)
    hit = index[..., None] == iota
    return jnp.sum(jnp.where(hit, table, 0), axis=-1).astype(table.dtype)


def pick_rows(table, index):
    iota = jnp.arange(table.shape[0], dtype=jnp.int32)
    hit = (index[..., None] == iota)[..., None]
    return jnp.sum(jnp.where(hit, table, 0), axis=-2).astype(table.dtype)


def request_table(owner_map, pattern, group_size):
    devices = jnp.arange(group_size, dtype=jnp.int32)
    entry_owner = pick(owner_map, pattern)
    foreign = entry_owner != owner_map[:, None]
    entry_hit = (entry_owner[:, :, None] == devices[None, None, :]) & foreign[:, :, None]
    per_tile = jnp.max(jnp.where(entry_hit, pattern[:, :, None], -1), axis=1)
    per_user = owner_map[None, :] == devices[:, None]
    return jnp.max(jnp.where(per_user[:, :, None], per_tile[None, :, :], -1), axis=1)


def supplier_of(tile_class, frame_slice, frame_devs):
    return (4 * (tile_class // frame_devs) + frame_slice) * frame_devs + tile_class % frame_devs


def expand_mask(block_mask):
    query_tiles = block_mask.shape[0]
    key_tiles = block_mask.shape[1]
    wide = jnp.broadcast_to(block_mask[:, None, :, None], (query_tiles, 64, key_tiles, 64))
    return wide.reshape(query_tiles * 64, key_tiles * 64)


def head_part(matrix, offset):
    return lax.dynamic_slice_in_dim(matrix, offset, HEAD_DIM, 1)


def head_scores(query_head, key_rows, offset, mask):
    key_head = head_part(key_rows, offset)
    scores = lax.dot_general(
        query_head, key_head, (((1,), (1,)), ((), ())), preferred_element_type=jnp.float32
    ) * HEAD_DIM ** (-0.5)
    return jnp.where(mask, scores, masked_score)


FAR_SLOTS = 4
INTERPRET = False
HEAD_CHUNKS = 2
LAST_SPLITS = 2


def attention_kernel(
    far_key_ref, far_value_ref, query_ref, near_key_ref, near_value_ref, near_bias_ref,
    far_bias_ref, out_ref, log_ref
):
    def flat(ref):
        block = ref[...]
        return block.reshape(block.shape[0] * block.shape[1], block.shape[2])

    query = flat(query_ref)
    dims = (((1,), (1,)), ((), ()))
    scale = HEAD_DIM ** (-0.5)
    near_scores = lax.dot_general(
        query, flat(near_key_ref), dims, preferred_element_type=jnp.float32
    ) * scale + near_bias_ref[...]
    far_scores = lax.dot_general(
        query, flat(far_key_ref), dims, preferred_element_type=jnp.float32
    ) * scale + far_bias_ref[...]
    row_max = jnp.maximum(
        jnp.max(near_scores, axis=1, keepdims=True), jnp.max(far_scores, axis=1, keepdims=True)
    )
    near_exp = jnp.exp(near_scores - row_max)
    far_exp = jnp.exp(far_scores - row_max)
    total = jnp.sum(near_exp, axis=1, keepdims=True) + jnp.sum(far_exp, axis=1, keepdims=True)
    log_total = row_max + jnp.log(total)
    inverse = 1.0 / total
    near_weights = (near_exp * inverse).astype(jnp.bfloat16)
    far_weights = (far_exp * inverse).astype(jnp.bfloat16)
    mixed = jnp.dot(near_weights, flat(near_value_ref), preferred_element_type=jnp.float32)
    mixed = mixed + jnp.dot(far_weights, flat(far_value_ref), preferred_element_type=jnp.float32)
    out_ref[...] = mixed.astype(out_ref.dtype).reshape(out_ref.shape)
    log_ref[...] = log_total


def attend(got, unit, near_bias, far_bias, first_head, heads):
    group_size, _, channels = got.shape
    far_rows = FAR_SLOTS * 16
    rows = group_size * unit
    base = 2 * far_rows // unit
    far_spec = (group_size, far_rows, HEAD_DIM)
    own_spec = (group_size, unit, HEAD_DIM)
    return pl.pallas_call(
        attention_kernel,
        grid=(heads,),
        in_specs=[
            pl.BlockSpec(far_spec, lambda h: (0, 0, first_head + h)),
            pl.BlockSpec(far_spec, lambda h: (0, 1, first_head + h)),
            pl.BlockSpec(own_spec, lambda h: (0, base, first_head + h)),
            pl.BlockSpec(own_spec, lambda h: (0, base + 1, first_head + h)),
            pl.BlockSpec(own_spec, lambda h: (0, base + 2, first_head + h)),
            pl.BlockSpec((rows, rows), lambda h: (0, 0)),
            pl.BlockSpec((rows, group_size * far_rows), lambda h: (0, 0)),
        ],
        out_specs=[
            pl.BlockSpec(own_spec, lambda h: (0, 0, h)),
            pl.BlockSpec((None, rows, 1), lambda h: (h, 0, 0)),
        ],
        out_shape=[
            jax.ShapeDtypeStruct((group_size, unit, heads * HEAD_DIM), jnp.bfloat16),
            jax.ShapeDtypeStruct((heads, rows, 1), jnp.float32),
        ],
        interpret=INTERPRET,
    )(got, got, got, got, got, near_bias, far_bias)


PACK_DESTS = 4


def pack_kernel(far_hot_ref, own_hot_ref, query_ref, key_ref, value_ref, *out_refs):
    far_hot = far_hot_ref[...]
    own_hot = own_hot_ref[...]
    dests, far_rows, local_rows = far_hot.shape
    own_rows = own_hot.shape[1]
    far_hot = far_hot.reshape(dests * far_rows, local_rows)
    own_hot = own_hot.reshape(dests * own_rows, local_rows)
    base = 2 * far_rows
    for index, out_ref in enumerate(out_refs):
        width = out_ref.shape[2]
        columns = slice(index * width, (index + 1) * width)

        def select(hot, source_ref, rows):
            picked = jnp.dot(hot, source_ref[:, columns], preferred_element_type=jnp.float32)
            return picked.astype(out_ref.dtype).reshape(dests, rows, width)

        out_ref[:, 0:far_rows, :] = select(far_hot, key_ref, far_rows)
        out_ref[:, far_rows:base, :] = select(far_hot, value_ref, far_rows)
        out_ref[:, base : base + own_rows, :] = select(own_hot, query_ref, own_rows)
        out_ref[:, base + own_rows : base + 2 * own_rows, :] = select(own_hot, key_ref, own_rows)
        out_ref[:, base + 2 * own_rows : base + 3 * own_rows, :] = select(
            own_hot, value_ref, own_rows
        )


def pack(far_rows, own_rows, query_feats, key_feats, value_feats, chunks):
    group_size, far_count = far_rows.shape
    own_count = own_rows.shape[1]
    local_rows, channels = query_feats.shape
    width = channels // chunks
    dests = PACK_DESTS if group_size % PACK_DESTS == 0 else 1
    row_iota = jnp.arange(local_rows, dtype=jnp.int32)
    far_hot = (far_rows[:, :, None] == row_iota).astype(jnp.bfloat16)
    own_hot = (own_rows[:, :, None] == row_iota).astype(jnp.bfloat16)
    total = 2 * far_count + 3 * own_count
    source_spec = pl.BlockSpec((local_rows, channels), lambda j: (0, 0))
    out_spec = pl.BlockSpec((dests, total, width), lambda j: (j, 0, 0))
    return pl.pallas_call(
        pack_kernel,
        grid=(group_size // dests,),
        in_specs=[
            pl.BlockSpec((dests, far_count, local_rows), lambda j: (j, 0, 0)),
            pl.BlockSpec((dests, own_count, local_rows), lambda j: (j, 0, 0)),
            source_spec,
            source_spec,
            source_spec,
        ],
        out_specs=[out_spec] * chunks,
        out_shape=[jax.ShapeDtypeStruct((group_size, total, width), query_feats.dtype)] * chunks,
        interpret=INTERPRET,
    )(far_hot, own_hot, query_feats, key_feats, value_feats)


def class_of(devices, frame_devs):
    return devices // frame_devs // 4 * frame_devs + devices % frame_devs


def ranked_pick(candidates, wanted, slot_count):
    rank = jnp.cumsum(wanted.astype(jnp.int32), axis=-1) - 1
    slots = jnp.arange(slot_count, dtype=jnp.int32)
    hit = wanted[..., None] & (rank[..., None] == slots)
    picked = jnp.sum(jnp.where(hit, candidates[..., None], 0), axis=-2)
    return picked, jnp.any(hit, axis=-2)


def shards(query_feats, key_feats, value_feats, owner_map, pattern):
    group_size = lax.axis_size("seq")
    device = lax.axis_index("seq")
    local_rows, channels = query_feats.shape
    strips = local_rows // (4 * WIDTH)
    blocks = WIDTH // 4
    piece_count = strips * blocks
    tile_count = owner_map.shape[0]
    own_count = tile_count // group_size
    capacity = (piece_count + group_size - 1) // group_size
    unit = capacity * 16
    frame_devs = group_size // FRAMES
    devices = jnp.arange(group_size, dtype=jnp.int32)
    local_iota = jnp.arange(piece_count, dtype=jnp.int32)
    cap_iota = jnp.arange(capacity, dtype=jnp.int32)
    slice_iota = jnp.arange(4, dtype=jnp.int32)
    token_iota = jnp.arange(16, dtype=jnp.int32)

    def piece_rows(pieces):
        strip = pieces // blocks
        column = pieces % blocks
        return (
            strip[..., None] * (4 * WIDTH)
            + (token_iota // 4) * WIDTH
            + column[..., None] * 4
            + token_iota % 4
        )

    own_rank, class_rank = owner_tables(owner_map, group_size, piece_count)
    my_class = class_of(device, frame_devs)
    my_tiles = my_class * piece_count + local_iota
    my_owner = lax.dynamic_slice_in_dim(owner_map, my_class * piece_count, piece_count)
    my_slot = lax.dynamic_slice_in_dim(class_rank, my_class * piece_count, piece_count)
    send_hit = (my_owner[None, None, :] == devices[:, None, None]) & (
        my_slot[None, None, :] == cap_iota[None, :, None]
    )
    send_index = jnp.sum(jnp.where(send_hit, local_iota[None, None, :], 0), axis=2)
    own_send_rows = piece_rows(send_index).reshape(group_size, unit)
    requests = request_table(owner_map, pattern, group_size)
    wanted = (requests >= 0) & (requests // piece_count == my_class)
    far_send_piece, _ = ranked_pick(requests % piece_count, wanted, FAR_SLOTS)
    far_send_rows = piece_rows(far_send_piece).reshape(group_size, FAR_SLOTS * 16)
    source_class = class_of(devices, frame_devs)
    class_tiles = source_class[:, None] * piece_count + local_iota[None, :]
    class_count = tile_count // piece_count
    mine = pick_rows(owner_map.reshape(class_count, piece_count), source_class) == device
    near_hit = mine[:, None, :] & (
        pick_rows(class_rank.reshape(class_count, piece_count), source_class)[:, None, :]
        == cap_iota[None, :, None]
    )
    near_tile = jnp.sum(jnp.where(near_hit, class_tiles[:, None, :], 0), axis=2)
    near_tile_rows = jnp.broadcast_to(near_tile[:, :, None], (group_size, capacity, 16)).reshape(-1)
    my_requests = lax.dynamic_index_in_dim(requests, device, axis=0, keepdims=False)
    far_wanted = (my_requests[None, :] >= 0) & (
        my_requests[None, :] // piece_count == source_class[:, None]
    )
    far_tile, far_valid = ranked_pick(
        jnp.broadcast_to(my_requests[None, :], (group_size, group_size)), far_wanted, FAR_SLOTS
    )
    far_tile = jnp.where(far_valid, far_tile, -1)
    far_tile_rows = jnp.broadcast_to(
        far_tile[:, :, None], (group_size, FAR_SLOTS, 16)
    ).reshape(-1)
    own_ids = owned_tiles(owner_map, own_rank, device, own_count)
    listed = pick_rows(pattern, own_ids)
    near_ok = jnp.any(listed[:, :, None] == near_tile_rows[None, None, :], axis=1)
    far_ok = jnp.any(listed[:, :, None] == far_tile_rows[None, None, :], axis=1)
    query_own = pick(own_rank, near_tile_rows)
    near_bias = jnp.where(jnp.take(near_ok, query_own, axis=0), 0.0, masked_score)
    far_bias = jnp.where(jnp.take(far_ok, query_own, axis=0), 0.0, masked_score)
    near_bias = near_bias.astype(jnp.float32)
    far_bias = far_bias.astype(jnp.float32)
    chunk_width = channels // HEAD_CHUNKS
    outputs = []
    logs = []
    packed = pack(far_send_rows, own_send_rows, query_feats, key_feats, value_feats, HEAD_CHUNKS)
    for chunk in range(HEAD_CHUNKS):
        sent = packed[chunk]
        got = lax.all_to_all(sent, "seq", split_axis=0, concat_axis=0, tiled=True)
        chunk_heads = chunk_width // HEAD_DIM
        parts = LAST_SPLITS
        for part in range(parts):
            part_heads = chunk_heads // parts
            mixed, head_logs = attend(
                got, unit, near_bias, far_bias, part * part_heads, part_heads
            )
            returned = lax.all_to_all(mixed, "seq", split_axis=0, concat_axis=0, tiled=True)
            outputs.append(returned.reshape(-1, part_heads * HEAD_DIM))
            logs.append(head_logs[:, :, 0])
    head_logs = jnp.concatenate(logs, axis=0)
    own_class = own_ids // piece_count
    own_slot = pick(class_rank, own_ids)
    gather_rows = (
        supplier_of(own_class[:, None], slice_iota[None, :], frame_devs) * capacity
        + own_slot[:, None]
    )
    log_rows = (gather_rows[:, :, None] * 16 + token_iota).reshape(-1)
    heads = channels // HEAD_DIM
    log_sums = (
        jnp.take(head_logs, log_rows, axis=1)
        .reshape(heads, own_count, 64)
        .transpose(1, 0, 2)
        .reshape(1, own_count, heads * 64)
    )
    local_iota_rows = jnp.arange(local_rows, dtype=jnp.int32)
    strip = local_iota_rows // (4 * WIDTH)
    height = local_iota_rows % (4 * WIDTH) // WIDTH
    column = local_iota_rows % WIDTH
    piece = strip * blocks + column // 4
    token = height * 4 + column % 4
    back_rows = (pick(my_owner, piece) * capacity + pick(my_slot, piece)) * 16 + token
    attended = jnp.take(jnp.concatenate(outputs, axis=1), back_rows, axis=0)
    return (attended, log_sums)


def solution(mesh):
    placed = (
        P(("groups", "seq"), None),
        P(("groups", "seq"), None),
        P(("groups", "seq"), None),
        P("groups"),
        P("groups", None),
    )
    return jax.shard_map(
        shards,
        mesh=mesh,
        in_specs=placed,
        out_specs=(P(("groups", "seq"), None), P(("groups", "seq"), None, None)),
        check_vma=False,
    )
```

```python
import jax
import jax.numpy as jnp
from jax import lax
from jax.sharding import PartitionSpec as P
from jax.experimental import pallas as pl

HEADS = 20
HEAD_DIM = 128
WIDTH = 64
FRAMES = 16


masked_score = -1e30


def frame_pieces(rows_in, strips):
    channels = rows_in.shape[1]
    shaped = rows_in.reshape(strips, 4, WIDTH // 4, 4, channels)
    return shaped.transpose(0, 2, 1, 3, 4).reshape(strips * (WIDTH // 4), 16, channels)


def frame_rows(pieces, strips):
    channels = pieces.shape[2]
    shaped = pieces.reshape(strips, WIDTH // 4, 4, 4, channels)
    return shaped.transpose(0, 2, 1, 3, 4).reshape(strips * 4 * WIDTH, channels)


def owner_tables(owner_map, group_size, piece_count):
    tile_count = owner_map.shape[0]
    devices = jnp.arange(group_size, dtype=jnp.int32)
    onehot = (owner_map[:, None] == devices[None, :]).astype(jnp.int32)
    running = jnp.cumsum(onehot, axis=0)
    own_rank = jnp.sum(onehot * running, axis=1) - 1
    by_class = owner_map.reshape(tile_count // piece_count, piece_count)
    local_iota = jnp.arange(piece_count, dtype=jnp.int32)
    earlier = (by_class[:, :, None] == by_class[:, None, :]) & (
        local_iota[None, None, :] < local_iota[None, :, None]
    )
    class_rank = jnp.sum(earlier.astype(jnp.int32), axis=2).reshape(tile_count)
    return (own_rank, class_rank)


def owned_tiles(owner_map, own_rank, device, own_count):
    tile_iota = jnp.arange(owner_map.shape[0], dtype=jnp.int32)
    slot_iota = jnp.arange(own_count, dtype=jnp.int32)
    match_rows = (owner_map[None, :] == device) & (own_rank[None, :] == slot_iota[:, None])
    return jnp.sum(jnp.where(match_rows, tile_iota[None, :], 0), axis=1)


def pick(table, index):
    iota = jnp.arange(table.shape[0], dtype=jnp.int32)
    hit = index[..., None] == iota
    return jnp.sum(jnp.where(hit, table, 0), axis=-1).astype(table.dtype)


def pick_rows(table, index):
    iota = jnp.arange(table.shape[0], dtype=jnp.int32)
    hit = (index[..., None] == iota)[..., None]
    return jnp.sum(jnp.where(hit, table, 0), axis=-2).astype(table.dtype)


def request_table(owner_map, pattern, group_size):
    devices = jnp.arange(group_size, dtype=jnp.int32)
    entry_owner = pick(owner_map, pattern)
    foreign = entry_owner != owner_map[:, None]
    entry_hit = (entry_owner[:, :, None] == devices[None, None, :]) & foreign[:, :, None]
    per_tile = jnp.max(jnp.where(entry_hit, pattern[:, :, None], -1), axis=1)
    per_user = owner_map[None, :] == devices[:, None]
    return jnp.max(jnp.where(per_user[:, :, None], per_tile[None, :, :], -1), axis=1)


def supplier_of(tile_class, frame_slice, frame_devs):
    return (4 * (tile_class // frame_devs) + frame_slice) * frame_devs + tile_class % frame_devs


def expand_mask(block_mask):
    query_tiles = block_mask.shape[0]
    key_tiles = block_mask.shape[1]
    wide = jnp.broadcast_to(block_mask[:, None, :, None], (query_tiles, 64, key_tiles, 64))
    return wide.reshape(query_tiles * 64, key_tiles * 64)


def head_part(matrix, offset):
    return lax.dynamic_slice_in_dim(matrix, offset, HEAD_DIM, 1)


def head_scores(query_head, key_rows, offset, mask):
    key_head = head_part(key_rows, offset)
    scores = lax.dot_general(
        query_head, key_head, (((1,), (1,)), ((), ())), preferred_element_type=jnp.float32
    ) * HEAD_DIM ** (-0.5)
    return jnp.where(mask, scores, masked_score)


FAR_SLOTS = 4
INTERPRET = False
HEAD_CHUNKS = 2


def attention_kernel(
    far_key_ref, far_value_ref, query_ref, near_key_ref, near_value_ref, near_bias_ref,
    far_bias_ref, out_ref, log_ref
):
    def flat(ref):
        block = ref[...]
        return block.reshape(block.shape[0] * block.shape[1], block.shape[2])

    query = flat(query_ref)
    dims = (((1,), (1,)), ((), ()))
    scale = HEAD_DIM ** (-0.5)
    near_scores = lax.dot_general(
        query, flat(near_key_ref), dims, preferred_element_type=jnp.float32
    ) * scale + near_bias_ref[...]
    far_scores = lax.dot_general(
        query, flat(far_key_ref), dims, preferred_element_type=jnp.float32
    ) * scale + far_bias_ref[...]
    row_max = jnp.maximum(
        jnp.max(near_scores, axis=1, keepdims=True), jnp.max(far_scores, axis=1, keepdims=True)
    )
    near_exp = jnp.exp(near_scores - row_max)
    far_exp = jnp.exp(far_scores - row_max)
    total = jnp.sum(near_exp, axis=1, keepdims=True) + jnp.sum(far_exp, axis=1, keepdims=True)
    log_total = row_max + jnp.log(total)
    inverse = 1.0 / total
    near_weights = (near_exp * inverse).astype(jnp.bfloat16)
    far_weights = (far_exp * inverse).astype(jnp.bfloat16)
    mixed = jnp.dot(near_weights, flat(near_value_ref), preferred_element_type=jnp.float32)
    mixed = mixed + jnp.dot(far_weights, flat(far_value_ref), preferred_element_type=jnp.float32)
    out_ref[...] = mixed.astype(out_ref.dtype).reshape(out_ref.shape)
    log_ref[...] = log_total


def attend(got, unit, near_bias, far_bias):
    group_size, _, channels = got.shape
    far_rows = FAR_SLOTS * 16
    rows = group_size * unit
    heads = channels // HEAD_DIM
    base = 2 * far_rows // unit
    far_spec = (group_size, far_rows, HEAD_DIM)
    own_spec = (group_size, unit, HEAD_DIM)
    return pl.pallas_call(
        attention_kernel,
        grid=(heads,),
        in_specs=[
            pl.BlockSpec(far_spec, lambda h: (0, 0, h)),
            pl.BlockSpec(far_spec, lambda h: (0, 1, h)),
            pl.BlockSpec(own_spec, lambda h: (0, base, h)),
            pl.BlockSpec(own_spec, lambda h: (0, base + 1, h)),
            pl.BlockSpec(own_spec, lambda h: (0, base + 2, h)),
            pl.BlockSpec((rows, rows), lambda h: (0, 0)),
            pl.BlockSpec((rows, group_size * far_rows), lambda h: (0, 0)),
        ],
        out_specs=[
            pl.BlockSpec(own_spec, lambda h: (0, 0, h)),
            pl.BlockSpec((None, rows, 1), lambda h: (h, 0, 0)),
        ],
        out_shape=[
            jax.ShapeDtypeStruct((group_size, unit, channels), jnp.bfloat16),
            jax.ShapeDtypeStruct((heads, rows, 1), jnp.float32),
        ],
        interpret=INTERPRET,
    )(got, got, got, got, got, near_bias, far_bias)


PACK_DESTS = 4


def pack_kernel(far_hot_ref, own_hot_ref, query_ref, key_ref, value_ref, *out_refs):
    far_hot = far_hot_ref[...]
    own_hot = own_hot_ref[...]
    dests, far_rows, local_rows = far_hot.shape
    own_rows = own_hot.shape[1]
    far_hot = far_hot.reshape(dests * far_rows, local_rows)
    own_hot = own_hot.reshape(dests * own_rows, local_rows)
    base = 2 * far_rows
    for index, out_ref in enumerate(out_refs):
        width = out_ref.shape[2]
        columns = slice(index * width, (index + 1) * width)

        def select(hot, source_ref, rows):
            picked = jnp.dot(hot, source_ref[:, columns], preferred_element_type=jnp.float32)
            return picked.astype(out_ref.dtype).reshape(dests, rows, width)

        out_ref[:, 0:far_rows, :] = select(far_hot, key_ref, far_rows)
        out_ref[:, far_rows:base, :] = select(far_hot, value_ref, far_rows)
        out_ref[:, base : base + own_rows, :] = select(own_hot, query_ref, own_rows)
        out_ref[:, base + own_rows : base + 2 * own_rows, :] = select(own_hot, key_ref, own_rows)
        out_ref[:, base + 2 * own_rows : base + 3 * own_rows, :] = select(
            own_hot, value_ref, own_rows
        )


def pack(far_rows, own_rows, query_feats, key_feats, value_feats, chunks):
    group_size, far_count = far_rows.shape
    own_count = own_rows.shape[1]
    local_rows, channels = query_feats.shape
    width = channels // chunks
    dests = PACK_DESTS if group_size % PACK_DESTS == 0 else 1
    row_iota = jnp.arange(local_rows, dtype=jnp.int32)
    far_hot = (far_rows[:, :, None] == row_iota).astype(jnp.bfloat16)
    own_hot = (own_rows[:, :, None] == row_iota).astype(jnp.bfloat16)
    total = 2 * far_count + 3 * own_count
    source_spec = pl.BlockSpec((local_rows, channels), lambda j: (0, 0))
    out_spec = pl.BlockSpec((dests, total, width), lambda j: (j, 0, 0))
    return pl.pallas_call(
        pack_kernel,
        grid=(group_size // dests,),
        in_specs=[
            pl.BlockSpec((dests, far_count, local_rows), lambda j: (j, 0, 0)),
            pl.BlockSpec((dests, own_count, local_rows), lambda j: (j, 0, 0)),
            source_spec,
            source_spec,
            source_spec,
        ],
        out_specs=[out_spec] * chunks,
        out_shape=[jax.ShapeDtypeStruct((group_size, total, width), query_feats.dtype)] * chunks,
        interpret=INTERPRET,
    )(far_hot, own_hot, query_feats, key_feats, value_feats)


def class_of(devices, frame_devs):
    return devices // frame_devs // 4 * frame_devs + devices % frame_devs


def ranked_pick(candidates, wanted, slot_count):
    rank = jnp.cumsum(wanted.astype(jnp.int32), axis=-1) - 1
    slots = jnp.arange(slot_count, dtype=jnp.int32)
    hit = wanted[..., None] & (rank[..., None] == slots)
    picked = jnp.sum(jnp.where(hit, candidates[..., None], 0), axis=-2)
    return picked, jnp.any(hit, axis=-2)


def shards(query_feats, key_feats, value_feats, owner_map, pattern):
    group_size = lax.axis_size("seq")
    device = lax.axis_index("seq")
    local_rows, channels = query_feats.shape
    strips = local_rows // (4 * WIDTH)
    blocks = WIDTH // 4
    piece_count = strips * blocks
    tile_count = owner_map.shape[0]
    own_count = tile_count // group_size
    capacity = (piece_count + group_size - 1) // group_size
    unit = capacity * 16
    frame_devs = group_size // FRAMES
    devices = jnp.arange(group_size, dtype=jnp.int32)
    local_iota = jnp.arange(piece_count, dtype=jnp.int32)
    cap_iota = jnp.arange(capacity, dtype=jnp.int32)
    slice_iota = jnp.arange(4, dtype=jnp.int32)
    token_iota = jnp.arange(16, dtype=jnp.int32)

    def piece_rows(pieces):
        strip = pieces // blocks
        column = pieces % blocks
        return (
            strip[..., None] * (4 * WIDTH)
            + (token_iota // 4) * WIDTH
            + column[..., None] * 4
            + token_iota % 4
        )

    own_rank, class_rank = owner_tables(owner_map, group_size, piece_count)
    my_class = class_of(device, frame_devs)
    my_tiles = my_class * piece_count + local_iota
    my_owner = lax.dynamic_slice_in_dim(owner_map, my_class * piece_count, piece_count)
    my_slot = lax.dynamic_slice_in_dim(class_rank, my_class * piece_count, piece_count)
    send_hit = (my_owner[None, None, :] == devices[:, None, None]) & (
        my_slot[None, None, :] == cap_iota[None, :, None]
    )
    send_index = jnp.sum(jnp.where(send_hit, local_iota[None, None, :], 0), axis=2)
    own_send_rows = piece_rows(send_index).reshape(group_size, unit)
    requests = request_table(owner_map, pattern, group_size)
    wanted = (requests >= 0) & (requests // piece_count == my_class)
    far_send_piece, _ = ranked_pick(requests % piece_count, wanted, FAR_SLOTS)
    far_send_rows = piece_rows(far_send_piece).reshape(group_size, FAR_SLOTS * 16)
    source_class = class_of(devices, frame_devs)
    class_tiles = source_class[:, None] * piece_count + local_iota[None, :]
    class_count = tile_count // piece_count
    mine = pick_rows(owner_map.reshape(class_count, piece_count), source_class) == device
    near_hit = mine[:, None, :] & (
        pick_rows(class_rank.reshape(class_count, piece_count), source_class)[:, None, :]
        == cap_iota[None, :, None]
    )
    near_tile = jnp.sum(jnp.where(near_hit, class_tiles[:, None, :], 0), axis=2)
    near_tile_rows = jnp.broadcast_to(near_tile[:, :, None], (group_size, capacity, 16)).reshape(-1)
    my_requests = lax.dynamic_index_in_dim(requests, device, axis=0, keepdims=False)
    far_wanted = (my_requests[None, :] >= 0) & (
        my_requests[None, :] // piece_count == source_class[:, None]
    )
    far_tile, far_valid = ranked_pick(
        jnp.broadcast_to(my_requests[None, :], (group_size, group_size)), far_wanted, FAR_SLOTS
    )
    far_tile = jnp.where(far_valid, far_tile, -1)
    far_tile_rows = jnp.broadcast_to(
        far_tile[:, :, None], (group_size, FAR_SLOTS, 16)
    ).reshape(-1)
    own_ids = owned_tiles(owner_map, own_rank, device, own_count)
    listed = pick_rows(pattern, own_ids)
    near_ok = jnp.any(listed[:, :, None] == near_tile_rows[None, None, :], axis=1)
    far_ok = jnp.any(listed[:, :, None] == far_tile_rows[None, None, :], axis=1)
    query_own = pick(own_rank, near_tile_rows)
    near_bias = jnp.where(jnp.take(near_ok, query_own, axis=0, mode="clip"), 0.0, masked_score)
    far_bias = jnp.where(jnp.take(far_ok, query_own, axis=0, mode="clip"), 0.0, masked_score)
    near_bias = near_bias.astype(jnp.float32)
    far_bias = far_bias.astype(jnp.float32)
    chunk_width = channels // HEAD_CHUNKS
    outputs = []
    logs = []
    packed = pack(far_send_rows, own_send_rows, query_feats, key_feats, value_feats, HEAD_CHUNKS)
    for chunk in range(HEAD_CHUNKS):
        sent = packed[chunk]
        got = lax.all_to_all(sent, "seq", split_axis=0, concat_axis=0, tiled=True)
        mixed, head_logs = attend(got, unit, near_bias, far_bias)
        returned = lax.all_to_all(mixed, "seq", split_axis=0, concat_axis=0, tiled=True)
        outputs.append(returned.reshape(-1, chunk_width))
        logs.append(head_logs[:, :, 0])
    head_logs = jnp.concatenate(logs, axis=0)
    own_class = own_ids // piece_count
    own_slot = pick(class_rank, own_ids)
    gather_rows = (
        supplier_of(own_class[:, None], slice_iota[None, :], frame_devs) * capacity
        + own_slot[:, None]
    )
    log_rows = (gather_rows[:, :, None] * 16 + token_iota).reshape(-1)
    heads = channels // HEAD_DIM
    log_sums = (
        jnp.take(head_logs, log_rows, axis=1, mode="clip")
        .reshape(heads, own_count, 64)
        .transpose(1, 0, 2)
        .reshape(1, own_count, heads * 64)
    )
    local_iota_rows = jnp.arange(local_rows, dtype=jnp.int32)
    strip = local_iota_rows // (4 * WIDTH)
    height = local_iota_rows % (4 * WIDTH) // WIDTH
    column = local_iota_rows % WIDTH
    piece = strip * blocks + column // 4
    token = height * 4 + column % 4
    back_rows = (pick(my_owner, piece) * capacity + pick(my_slot, piece)) * 16 + token
    attended = jnp.take(jnp.concatenate(outputs, axis=1), back_rows, axis=0, mode="clip")
    return (attended, log_sums)


def solution(mesh):
    placed = (
        P(("groups", "seq"), None),
        P(("groups", "seq"), None),
        P(("groups", "seq"), None),
        P("groups"),
        P("groups", None),
    )
    return jax.shard_map(
        shards,
        mesh=mesh,
        in_specs=placed,
        out_specs=(P(("groups", "seq"), None), P(("groups", "seq"), None, None)),
        check_vma=False,
    )
```

```python
import jax
import jax.numpy as jnp
from jax import lax
from jax.sharding import PartitionSpec as P
from jax.experimental import pallas as pl

HEADS = 20
HEAD_DIM = 128
WIDTH = 64
FRAMES = 16


masked_score = -1e30


def frame_pieces(rows_in, strips):
    channels = rows_in.shape[1]
    shaped = rows_in.reshape(strips, 4, WIDTH // 4, 4, channels)
    return shaped.transpose(0, 2, 1, 3, 4).reshape(strips * (WIDTH // 4), 16, channels)


def frame_rows(pieces, strips):
    channels = pieces.shape[2]
    shaped = pieces.reshape(strips, WIDTH // 4, 4, 4, channels)
    return shaped.transpose(0, 2, 1, 3, 4).reshape(strips * 4 * WIDTH, channels)


def owner_tables(owner_map, group_size, piece_count):
    tile_count = owner_map.shape[0]
    devices = jnp.arange(group_size, dtype=jnp.int32)
    onehot = (owner_map[:, None] == devices[None, :]).astype(jnp.int32)
    running = jnp.cumsum(onehot, axis=0)
    own_rank = jnp.sum(onehot * running, axis=1) - 1
    by_class = owner_map.reshape(tile_count // piece_count, piece_count)
    local_iota = jnp.arange(piece_count, dtype=jnp.int32)
    earlier = (by_class[:, :, None] == by_class[:, None, :]) & (
        local_iota[None, None, :] < local_iota[None, :, None]
    )
    class_rank = jnp.sum(earlier.astype(jnp.int32), axis=2).reshape(tile_count)
    return (own_rank, class_rank)


def owned_tiles(owner_map, own_rank, device, own_count):
    tile_iota = jnp.arange(owner_map.shape[0], dtype=jnp.int32)
    slot_iota = jnp.arange(own_count, dtype=jnp.int32)
    match_rows = (owner_map[None, :] == device) & (own_rank[None, :] == slot_iota[:, None])
    return jnp.sum(jnp.where(match_rows, tile_iota[None, :], 0), axis=1)


def pick(table, index):
    iota = jnp.arange(table.shape[0], dtype=jnp.int32)
    hit = index[..., None] == iota
    return jnp.sum(jnp.where(hit, table, 0), axis=-1).astype(table.dtype)


def pick_rows(table, index):
    iota = jnp.arange(table.shape[0], dtype=jnp.int32)
    hit = (index[..., None] == iota)[..., None]
    return jnp.sum(jnp.where(hit, table, 0), axis=-2).astype(table.dtype)


def request_table(owner_map, pattern, group_size):
    devices = jnp.arange(group_size, dtype=jnp.int32)
    entry_owner = pick(owner_map, pattern)
    foreign = entry_owner != owner_map[:, None]
    entry_hit = (entry_owner[:, :, None] == devices[None, None, :]) & foreign[:, :, None]
    per_tile = jnp.max(jnp.where(entry_hit, pattern[:, :, None], -1), axis=1)
    per_user = owner_map[None, :] == devices[:, None]
    return jnp.max(jnp.where(per_user[:, :, None], per_tile[None, :, :], -1), axis=1)


def supplier_of(tile_class, frame_slice, frame_devs):
    return (4 * (tile_class // frame_devs) + frame_slice) * frame_devs + tile_class % frame_devs


def expand_mask(block_mask):
    query_tiles = block_mask.shape[0]
    key_tiles = block_mask.shape[1]
    wide = jnp.broadcast_to(block_mask[:, None, :, None], (query_tiles, 64, key_tiles, 64))
    return wide.reshape(query_tiles * 64, key_tiles * 64)


def head_part(matrix, offset):
    return lax.dynamic_slice_in_dim(matrix, offset, HEAD_DIM, 1)


def head_scores(query_head, key_rows, offset, mask):
    key_head = head_part(key_rows, offset)
    scores = lax.dot_general(
        query_head, key_head, (((1,), (1,)), ((), ())), preferred_element_type=jnp.float32
    ) * HEAD_DIM ** (-0.5)
    return jnp.where(mask, scores, masked_score)


FAR_SLOTS = 4
INTERPRET = False
HEAD_CHUNKS = 2


def attention_kernel(
    far_key_ref, far_value_ref, query_ref, near_key_ref, near_value_ref, near_bias_ref,
    far_bias_ref, out_ref, log_ref
):
    def flat(ref):
        block = ref[...]
        return block.reshape(block.shape[0] * block.shape[1], block.shape[2])

    query = flat(query_ref)
    dims = (((1,), (1,)), ((), ()))
    scale = HEAD_DIM ** (-0.5)
    near_scores = lax.dot_general(
        query, flat(near_key_ref), dims, preferred_element_type=jnp.float32
    ) * scale + near_bias_ref[...]
    far_scores = lax.dot_general(
        query, flat(far_key_ref), dims, preferred_element_type=jnp.float32
    ) * scale + far_bias_ref[...]
    row_max = jnp.maximum(
        jnp.max(near_scores, axis=1, keepdims=True), jnp.max(far_scores, axis=1, keepdims=True)
    )
    near_exp = jnp.exp(near_scores - row_max)
    far_exp = jnp.exp(far_scores - row_max)
    total = jnp.sum(near_exp, axis=1, keepdims=True) + jnp.sum(far_exp, axis=1, keepdims=True)
    log_total = row_max + jnp.log(total)
    inverse = 1.0 / total
    near_weights = (near_exp * inverse).astype(jnp.bfloat16)
    far_weights = (far_exp * inverse).astype(jnp.bfloat16)
    mixed = jnp.dot(near_weights, flat(near_value_ref), preferred_element_type=jnp.float32)
    mixed = mixed + jnp.dot(far_weights, flat(far_value_ref), preferred_element_type=jnp.float32)
    out_ref[...] = mixed.astype(out_ref.dtype).reshape(out_ref.shape)
    log_ref[...] = log_total


def attend(got, unit, near_bias, far_bias):
    group_size, _, channels = got.shape
    far_rows = FAR_SLOTS * 16
    rows = group_size * unit
    heads = channels // HEAD_DIM
    base = 2 * far_rows // unit
    far_spec = (group_size, far_rows, HEAD_DIM)
    own_spec = (group_size, unit, HEAD_DIM)
    return pl.pallas_call(
        attention_kernel,
        grid=(heads,),
        in_specs=[
            pl.BlockSpec(far_spec, lambda h: (0, 0, h)),
            pl.BlockSpec(far_spec, lambda h: (0, 1, h)),
            pl.BlockSpec(own_spec, lambda h: (0, base, h)),
            pl.BlockSpec(own_spec, lambda h: (0, base + 1, h)),
            pl.BlockSpec(own_spec, lambda h: (0, base + 2, h)),
            pl.BlockSpec((rows, rows), lambda h: (0, 0)),
            pl.BlockSpec((rows, group_size * far_rows), lambda h: (0, 0)),
        ],
        out_specs=[
            pl.BlockSpec(own_spec, lambda h: (0, 0, h)),
            pl.BlockSpec((None, rows, 1), lambda h: (h, 0, 0)),
        ],
        out_shape=[
            jax.ShapeDtypeStruct((group_size, unit, channels), jnp.bfloat16),
            jax.ShapeDtypeStruct((heads, rows, 1), jnp.float32),
        ],
        interpret=INTERPRET,
    )(got, got, got, got, got, near_bias, far_bias)


PACK_DESTS = 4


def pack_kernel(far_hot_ref, own_hot_ref, query_ref, key_ref, value_ref, *out_refs):
    far_hot = far_hot_ref[...]
    own_hot = own_hot_ref[...]
    dests, far_rows, local_rows = far_hot.shape
    own_rows = own_hot.shape[1]
    far_hot = far_hot.reshape(dests * far_rows, local_rows)
    own_hot = own_hot.reshape(dests * own_rows, local_rows)
    base = 2 * far_rows
    for index, out_ref in enumerate(out_refs):
        width = out_ref.shape[2]
        columns = slice(index * width, (index + 1) * width)

        def select(hot, source_ref, rows):
            picked = jnp.dot(hot, source_ref[:, columns], preferred_element_type=jnp.float32)
            return picked.astype(out_ref.dtype).reshape(dests, rows, width)

        out_ref[:, 0:far_rows, :] = select(far_hot, key_ref, far_rows)
        out_ref[:, far_rows:base, :] = select(far_hot, value_ref, far_rows)
        out_ref[:, base : base + own_rows, :] = select(own_hot, query_ref, own_rows)
        out_ref[:, base + own_rows : base + 2 * own_rows, :] = select(own_hot, key_ref, own_rows)
        out_ref[:, base + 2 * own_rows : base + 3 * own_rows, :] = select(
            own_hot, value_ref, own_rows
        )


def pack(far_rows, own_rows, query_feats, key_feats, value_feats, chunks):
    group_size, far_count = far_rows.shape
    own_count = own_rows.shape[1]
    local_rows, channels = query_feats.shape
    width = channels // chunks
    dests = PACK_DESTS if group_size % PACK_DESTS == 0 else 1
    row_iota = jnp.arange(local_rows, dtype=jnp.int32)
    far_hot = (far_rows[:, :, None] == row_iota).astype(jnp.bfloat16)
    own_hot = (own_rows[:, :, None] == row_iota).astype(jnp.bfloat16)
    total = 2 * far_count + 3 * own_count
    source_spec = pl.BlockSpec((local_rows, channels), lambda j: (0, 0))
    out_spec = pl.BlockSpec((dests, total, width), lambda j: (j, 0, 0))
    return pl.pallas_call(
        pack_kernel,
        grid=(group_size // dests,),
        in_specs=[
            pl.BlockSpec((dests, far_count, local_rows), lambda j: (j, 0, 0)),
            pl.BlockSpec((dests, own_count, local_rows), lambda j: (j, 0, 0)),
            source_spec,
            source_spec,
            source_spec,
        ],
        out_specs=[out_spec] * chunks,
        out_shape=[jax.ShapeDtypeStruct((group_size, total, width), query_feats.dtype)] * chunks,
        interpret=INTERPRET,
    )(far_hot, own_hot, query_feats, key_feats, value_feats)


def class_of(devices, frame_devs):
    return devices // frame_devs // 4 * frame_devs + devices % frame_devs


def ranked_pick(candidates, wanted, slot_count):
    rank = jnp.cumsum(wanted.astype(jnp.int32), axis=-1) - 1
    slots = jnp.arange(slot_count, dtype=jnp.int32)
    hit = wanted[..., None] & (rank[..., None] == slots)
    picked = jnp.sum(jnp.where(hit, candidates[..., None], 0), axis=-2)
    return picked, jnp.any(hit, axis=-2)


def shards(query_feats, key_feats, value_feats, owner_map, pattern):
    group_size = lax.axis_size("seq")
    device = lax.axis_index("seq")
    local_rows, channels = query_feats.shape
    strips = local_rows // (4 * WIDTH)
    blocks = WIDTH // 4
    piece_count = strips * blocks
    tile_count = owner_map.shape[0]
    own_count = tile_count // group_size
    capacity = (piece_count + group_size - 1) // group_size
    unit = capacity * 16
    frame_devs = group_size // FRAMES
    devices = jnp.arange(group_size, dtype=jnp.int32)
    local_iota = jnp.arange(piece_count, dtype=jnp.int32)
    cap_iota = jnp.arange(capacity, dtype=jnp.int32)
    slice_iota = jnp.arange(4, dtype=jnp.int32)
    token_iota = jnp.arange(16, dtype=jnp.int32)

    def piece_rows(pieces):
        strip = pieces // blocks
        column = pieces % blocks
        return (
            strip[..., None] * (4 * WIDTH)
            + (token_iota // 4) * WIDTH
            + column[..., None] * 4
            + token_iota % 4
        )

    own_rank, class_rank = owner_tables(owner_map, group_size, piece_count)
    my_class = class_of(device, frame_devs)
    my_tiles = my_class * piece_count + local_iota
    my_owner = lax.dynamic_slice_in_dim(owner_map, my_class * piece_count, piece_count)
    my_slot = lax.dynamic_slice_in_dim(class_rank, my_class * piece_count, piece_count)
    send_hit = (my_owner[None, None, :] == devices[:, None, None]) & (
        my_slot[None, None, :] == cap_iota[None, :, None]
    )
    send_index = jnp.sum(jnp.where(send_hit, local_iota[None, None, :], 0), axis=2)
    own_send_rows = piece_rows(send_index).reshape(group_size, unit)
    requests = request_table(owner_map, pattern, group_size)
    wanted = (requests >= 0) & (requests // piece_count == my_class)
    far_send_piece, _ = ranked_pick(requests % piece_count, wanted, FAR_SLOTS)
    far_send_rows = piece_rows(far_send_piece).reshape(group_size, FAR_SLOTS * 16)
    source_class = class_of(devices, frame_devs)
    class_tiles = source_class[:, None] * piece_count + local_iota[None, :]
    class_count = tile_count // piece_count
    mine = pick_rows(owner_map.reshape(class_count, piece_count), source_class) == device
    near_hit = mine[:, None, :] & (
        pick_rows(class_rank.reshape(class_count, piece_count), source_class)[:, None, :]
        == cap_iota[None, :, None]
    )
    near_tile = jnp.sum(jnp.where(near_hit, class_tiles[:, None, :], 0), axis=2)
    near_tile_rows = jnp.broadcast_to(near_tile[:, :, None], (group_size, capacity, 16)).reshape(-1)
    my_requests = lax.dynamic_index_in_dim(requests, device, axis=0, keepdims=False)
    far_wanted = (my_requests[None, :] >= 0) & (
        my_requests[None, :] // piece_count == source_class[:, None]
    )
    far_tile, far_valid = ranked_pick(
        jnp.broadcast_to(my_requests[None, :], (group_size, group_size)), far_wanted, FAR_SLOTS
    )
    far_tile = jnp.where(far_valid, far_tile, -1)
    far_tile_rows = jnp.broadcast_to(
        far_tile[:, :, None], (group_size, FAR_SLOTS, 16)
    ).reshape(-1)
    own_ids = owned_tiles(owner_map, own_rank, device, own_count)
    listed = pick_rows(pattern, own_ids)
    near_ok = jnp.any(listed[:, :, None] == near_tile_rows[None, None, :], axis=1)
    far_ok = jnp.any(listed[:, :, None] == far_tile_rows[None, None, :], axis=1)
    query_own = pick(own_rank, near_tile_rows)
    near_bias = jnp.where(jnp.take(near_ok, query_own, axis=0, mode="clip"), 0.0, masked_score)
    far_bias = jnp.where(jnp.take(far_ok, query_own, axis=0, mode="clip"), 0.0, masked_score)
    near_bias = near_bias.astype(jnp.float32)
    far_bias = far_bias.astype(jnp.float32)
    chunk_width = channels // HEAD_CHUNKS
    outputs = []
    logs = []
    packed = pack(far_send_rows, own_send_rows, query_feats, key_feats, value_feats, HEAD_CHUNKS)
    for chunk in range(HEAD_CHUNKS):
        sent = packed[chunk]
        got = lax.all_to_all(sent, "seq", split_axis=0, concat_axis=0, tiled=True)
        mixed, head_logs = attend(got, unit, near_bias, far_bias)
        returned = lax.all_to_all(mixed, "seq", split_axis=0, concat_axis=0, tiled=True)
        outputs.append(returned.reshape(-1, chunk_width))
        logs.append(head_logs[:, :, 0])
    head_logs = jnp.concatenate(logs, axis=0)
    own_class = own_ids // piece_count
    own_slot = pick(class_rank, own_ids)
    gather_rows = (
        supplier_of(own_class[:, None], slice_iota[None, :], frame_devs) * capacity
        + own_slot[:, None]
    )
    log_rows = (gather_rows[:, :, None] * 16 + token_iota).reshape(-1)
    heads = channels // HEAD_DIM
    log_sums = (
        jnp.take(head_logs, log_rows, axis=1, mode="clip")
        .reshape(heads, own_count, 64)
        .transpose(1, 0, 2)
        .reshape(1, own_count, heads * 64)
    )
    local_iota_rows = jnp.arange(local_rows, dtype=jnp.int32)
    strip = local_iota_rows // (4 * WIDTH)
    height = local_iota_rows % (4 * WIDTH) // WIDTH
    column = local_iota_rows % WIDTH
    piece = strip * blocks + column // 4
    token = height * 4 + column % 4
    back_rows = (pick(my_owner, piece) * capacity + pick(my_slot, piece)) * 16 + token
    attended = jnp.concatenate(
        [jnp.take(part, back_rows, axis=0, mode="clip") for part in outputs], axis=1
    )
    return (attended, log_sums)


def solution(mesh):
    placed = (
        P(("groups", "seq"), None),
        P(("groups", "seq"), None),
        P(("groups", "seq"), None),
        P("groups"),
        P("groups", None),
    )
    return jax.shard_map(
        shards,
        mesh=mesh,
        in_specs=placed,
        out_specs=(P(("groups", "seq"), None), P(("groups", "seq"), None, None)),
        check_vma=False,
    )
```

```python
import jax
import jax.numpy as jnp
from jax import lax
from jax.sharding import PartitionSpec as P
from jax.experimental import pallas as pl

HEADS = 20
HEAD_DIM = 128
WIDTH = 64
FRAMES = 16


masked_score = -1e30


def frame_pieces(rows_in, strips):
    channels = rows_in.shape[1]
    shaped = rows_in.reshape(strips, 4, WIDTH // 4, 4, channels)
    return shaped.transpose(0, 2, 1, 3, 4).reshape(strips * (WIDTH // 4), 16, channels)


def frame_rows(pieces, strips):
    channels = pieces.shape[2]
    shaped = pieces.reshape(strips, WIDTH // 4, 4, 4, channels)
    return shaped.transpose(0, 2, 1, 3, 4).reshape(strips * 4 * WIDTH, channels)


def owner_tables(owner_map, group_size, piece_count):
    tile_count = owner_map.shape[0]
    devices = jnp.arange(group_size, dtype=jnp.int32)
    onehot = (owner_map[:, None] == devices[None, :]).astype(jnp.int32)
    running = jnp.cumsum(onehot, axis=0)
    own_rank = jnp.sum(onehot * running, axis=1) - 1
    by_class = owner_map.reshape(tile_count // piece_count, piece_count)
    local_iota = jnp.arange(piece_count, dtype=jnp.int32)
    earlier = (by_class[:, :, None] == by_class[:, None, :]) & (
        local_iota[None, None, :] < local_iota[None, :, None]
    )
    class_rank = jnp.sum(earlier.astype(jnp.int32), axis=2).reshape(tile_count)
    return (own_rank, class_rank)


def owned_tiles(owner_map, own_rank, device, own_count):
    tile_iota = jnp.arange(owner_map.shape[0], dtype=jnp.int32)
    slot_iota = jnp.arange(own_count, dtype=jnp.int32)
    match_rows = (owner_map[None, :] == device) & (own_rank[None, :] == slot_iota[:, None])
    return jnp.sum(jnp.where(match_rows, tile_iota[None, :], 0), axis=1)


def pick(table, index):
    iota = jnp.arange(table.shape[0], dtype=jnp.int32)
    hit = index[..., None] == iota
    return jnp.sum(jnp.where(hit, table, 0), axis=-1).astype(table.dtype)


def pick_rows(table, index):
    iota = jnp.arange(table.shape[0], dtype=jnp.int32)
    hit = (index[..., None] == iota)[..., None]
    return jnp.sum(jnp.where(hit, table, 0), axis=-2).astype(table.dtype)


def request_table(owner_map, pattern, group_size):
    devices = jnp.arange(group_size, dtype=jnp.int32)
    entry_owner = pick(owner_map, pattern)
    foreign = entry_owner != owner_map[:, None]
    entry_hit = (entry_owner[:, :, None] == devices[None, None, :]) & foreign[:, :, None]
    per_tile = jnp.max(jnp.where(entry_hit, pattern[:, :, None], -1), axis=1)
    per_user = owner_map[None, :] == devices[:, None]
    return jnp.max(jnp.where(per_user[:, :, None], per_tile[None, :, :], -1), axis=1)


def supplier_of(tile_class, frame_slice, frame_devs):
    return (4 * (tile_class // frame_devs) + frame_slice) * frame_devs + tile_class % frame_devs


def expand_mask(block_mask):
    query_tiles = block_mask.shape[0]
    key_tiles = block_mask.shape[1]
    wide = jnp.broadcast_to(block_mask[:, None, :, None], (query_tiles, 64, key_tiles, 64))
    return wide.reshape(query_tiles * 64, key_tiles * 64)


def head_part(matrix, offset):
    return lax.dynamic_slice_in_dim(matrix, offset, HEAD_DIM, 1)


def head_scores(query_head, key_rows, offset, mask):
    key_head = head_part(key_rows, offset)
    scores = lax.dot_general(
        query_head, key_head, (((1,), (1,)), ((), ())), preferred_element_type=jnp.float32
    ) * HEAD_DIM ** (-0.5)
    return jnp.where(mask, scores, masked_score)


FAR_SLOTS = 4
INTERPRET = False
HEAD_CHUNKS = 2


HEADS_PER_STEP = 2


def attention_kernel(
    far_key_ref, far_value_ref, query_ref, near_key_ref, near_value_ref, near_bias_ref,
    far_bias_ref, out_ref, log_ref
):
    def flat(ref, columns):
        block = ref[:, :, columns]
        return block.reshape(block.shape[0] * block.shape[1], block.shape[2])

    dims = (((1,), (1,)), ((), ()))
    scale = HEAD_DIM ** (-0.5)
    near_bias = near_bias_ref[...]
    far_bias = far_bias_ref[...]
    for step_head in range(log_ref.shape[0]):
        columns = slice(step_head * HEAD_DIM, (step_head + 1) * HEAD_DIM)
        query = flat(query_ref, columns)
        near_scores = lax.dot_general(
            query, flat(near_key_ref, columns), dims, preferred_element_type=jnp.float32
        ) * scale + near_bias
        far_scores = lax.dot_general(
            query, flat(far_key_ref, columns), dims, preferred_element_type=jnp.float32
        ) * scale + far_bias
        row_max = jnp.maximum(
            jnp.max(near_scores, axis=1, keepdims=True),
            jnp.max(far_scores, axis=1, keepdims=True),
        )
        near_exp = jnp.exp(near_scores - row_max)
        far_exp = jnp.exp(far_scores - row_max)
        total = jnp.sum(near_exp, axis=1, keepdims=True) + jnp.sum(
            far_exp, axis=1, keepdims=True
        )
        log_total = row_max + jnp.log(total)
        inverse = 1.0 / total
        near_weights = (near_exp * inverse).astype(jnp.bfloat16)
        far_weights = (far_exp * inverse).astype(jnp.bfloat16)
        mixed = jnp.dot(
            near_weights, flat(near_value_ref, columns), preferred_element_type=jnp.float32
        )
        mixed = mixed + jnp.dot(
            far_weights, flat(far_value_ref, columns), preferred_element_type=jnp.float32
        )
        out_shape = out_ref.shape
        out_ref[:, :, columns] = mixed.astype(out_ref.dtype).reshape(
            out_shape[0], out_shape[1], HEAD_DIM
        )
        log_ref[step_head] = log_total


def attend(got, unit, near_bias, far_bias):
    group_size, _, channels = got.shape
    far_rows = FAR_SLOTS * 16
    rows = group_size * unit
    heads = channels // HEAD_DIM
    per_step = HEADS_PER_STEP if heads % HEADS_PER_STEP == 0 else 1
    width = per_step * HEAD_DIM
    base = 2 * far_rows // unit
    far_spec = (group_size, far_rows, width)
    own_spec = (group_size, unit, width)
    return pl.pallas_call(
        attention_kernel,
        grid=(heads // per_step,),
        in_specs=[
            pl.BlockSpec(far_spec, lambda h: (0, 0, h)),
            pl.BlockSpec(far_spec, lambda h: (0, 1, h)),
            pl.BlockSpec(own_spec, lambda h: (0, base, h)),
            pl.BlockSpec(own_spec, lambda h: (0, base + 1, h)),
            pl.BlockSpec(own_spec, lambda h: (0, base + 2, h)),
            pl.BlockSpec((rows, rows), lambda h: (0, 0)),
            pl.BlockSpec((rows, group_size * far_rows), lambda h: (0, 0)),
        ],
        out_specs=[
            pl.BlockSpec(own_spec, lambda h: (0, 0, h)),
            pl.BlockSpec((per_step, rows, 1), lambda h: (h, 0, 0)),
        ],
        out_shape=[
            jax.ShapeDtypeStruct((group_size, unit, channels), jnp.bfloat16),
            jax.ShapeDtypeStruct((heads, rows, 1), jnp.float32),
        ],
        interpret=INTERPRET,
    )(got, got, got, got, got, near_bias, far_bias)


PACK_DESTS = 4


def pack_kernel(far_hot_ref, own_hot_ref, query_ref, key_ref, value_ref, *out_refs):
    far_hot = far_hot_ref[...]
    own_hot = own_hot_ref[...]
    dests, far_rows, local_rows = far_hot.shape
    own_rows = own_hot.shape[1]
    far_hot = far_hot.reshape(dests * far_rows, local_rows)
    own_hot = own_hot.reshape(dests * own_rows, local_rows)
    base = 2 * far_rows
    for index, out_ref in enumerate(out_refs):
        width = out_ref.shape[2]
        columns = slice(index * width, (index + 1) * width)

        def select(hot, source_ref, rows):
            picked = jnp.dot(hot, source_ref[:, columns], preferred_element_type=jnp.float32)
            return picked.astype(out_ref.dtype).reshape(dests, rows, width)

        out_ref[:, 0:far_rows, :] = select(far_hot, key_ref, far_rows)
        out_ref[:, far_rows:base, :] = select(far_hot, value_ref, far_rows)
        out_ref[:, base : base + own_rows, :] = select(own_hot, query_ref, own_rows)
        out_ref[:, base + own_rows : base + 2 * own_rows, :] = select(own_hot, key_ref, own_rows)
        out_ref[:, base + 2 * own_rows : base + 3 * own_rows, :] = select(
            own_hot, value_ref, own_rows
        )


def pack(far_rows, own_rows, query_feats, key_feats, value_feats, chunks):
    group_size, far_count = far_rows.shape
    own_count = own_rows.shape[1]
    local_rows, channels = query_feats.shape
    width = channels // chunks
    dests = PACK_DESTS if group_size % PACK_DESTS == 0 else 1
    row_iota = jnp.arange(local_rows, dtype=jnp.int32)
    far_hot = (far_rows[:, :, None] == row_iota).astype(jnp.bfloat16)
    own_hot = (own_rows[:, :, None] == row_iota).astype(jnp.bfloat16)
    total = 2 * far_count + 3 * own_count
    source_spec = pl.BlockSpec((local_rows, channels), lambda j: (0, 0))
    out_spec = pl.BlockSpec((dests, total, width), lambda j: (j, 0, 0))
    return pl.pallas_call(
        pack_kernel,
        grid=(group_size // dests,),
        in_specs=[
            pl.BlockSpec((dests, far_count, local_rows), lambda j: (j, 0, 0)),
            pl.BlockSpec((dests, own_count, local_rows), lambda j: (j, 0, 0)),
            source_spec,
            source_spec,
            source_spec,
        ],
        out_specs=[out_spec] * chunks,
        out_shape=[jax.ShapeDtypeStruct((group_size, total, width), query_feats.dtype)] * chunks,
        interpret=INTERPRET,
    )(far_hot, own_hot, query_feats, key_feats, value_feats)


def class_of(devices, frame_devs):
    return devices // frame_devs // 4 * frame_devs + devices % frame_devs


def ranked_pick(candidates, wanted, slot_count):
    rank = jnp.cumsum(wanted.astype(jnp.int32), axis=-1) - 1
    slots = jnp.arange(slot_count, dtype=jnp.int32)
    hit = wanted[..., None] & (rank[..., None] == slots)
    picked = jnp.sum(jnp.where(hit, candidates[..., None], 0), axis=-2)
    return picked, jnp.any(hit, axis=-2)


def shards(query_feats, key_feats, value_feats, owner_map, pattern):
    group_size = lax.axis_size("seq")
    device = lax.axis_index("seq")
    local_rows, channels = query_feats.shape
    strips = local_rows // (4 * WIDTH)
    blocks = WIDTH // 4
    piece_count = strips * blocks
    tile_count = owner_map.shape[0]
    own_count = tile_count // group_size
    capacity = (piece_count + group_size - 1) // group_size
    unit = capacity * 16
    frame_devs = group_size // FRAMES
    devices = jnp.arange(group_size, dtype=jnp.int32)
    local_iota = jnp.arange(piece_count, dtype=jnp.int32)
    cap_iota = jnp.arange(capacity, dtype=jnp.int32)
    slice_iota = jnp.arange(4, dtype=jnp.int32)
    token_iota = jnp.arange(16, dtype=jnp.int32)

    def piece_rows(pieces):
        strip = pieces // blocks
        column = pieces % blocks
        return (
            strip[..., None] * (4 * WIDTH)
            + (token_iota // 4) * WIDTH
            + column[..., None] * 4
            + token_iota % 4
        )

    own_rank, class_rank = owner_tables(owner_map, group_size, piece_count)
    my_class = class_of(device, frame_devs)
    my_tiles = my_class * piece_count + local_iota
    my_owner = lax.dynamic_slice_in_dim(owner_map, my_class * piece_count, piece_count)
    my_slot = lax.dynamic_slice_in_dim(class_rank, my_class * piece_count, piece_count)
    send_hit = (my_owner[None, None, :] == devices[:, None, None]) & (
        my_slot[None, None, :] == cap_iota[None, :, None]
    )
    send_index = jnp.sum(jnp.where(send_hit, local_iota[None, None, :], 0), axis=2)
    own_send_rows = piece_rows(send_index).reshape(group_size, unit)
    requests = request_table(owner_map, pattern, group_size)
    wanted = (requests >= 0) & (requests // piece_count == my_class)
    far_send_piece, _ = ranked_pick(requests % piece_count, wanted, FAR_SLOTS)
    far_send_rows = piece_rows(far_send_piece).reshape(group_size, FAR_SLOTS * 16)
    source_class = class_of(devices, frame_devs)
    class_tiles = source_class[:, None] * piece_count + local_iota[None, :]
    class_count = tile_count // piece_count
    mine = pick_rows(owner_map.reshape(class_count, piece_count), source_class) == device
    near_hit = mine[:, None, :] & (
        pick_rows(class_rank.reshape(class_count, piece_count), source_class)[:, None, :]
        == cap_iota[None, :, None]
    )
    near_tile = jnp.sum(jnp.where(near_hit, class_tiles[:, None, :], 0), axis=2)
    near_tile_rows = jnp.broadcast_to(near_tile[:, :, None], (group_size, capacity, 16)).reshape(-1)
    my_requests = lax.dynamic_index_in_dim(requests, device, axis=0, keepdims=False)
    far_wanted = (my_requests[None, :] >= 0) & (
        my_requests[None, :] // piece_count == source_class[:, None]
    )
    far_tile, far_valid = ranked_pick(
        jnp.broadcast_to(my_requests[None, :], (group_size, group_size)), far_wanted, FAR_SLOTS
    )
    far_tile = jnp.where(far_valid, far_tile, -1)
    far_tile_rows = jnp.broadcast_to(
        far_tile[:, :, None], (group_size, FAR_SLOTS, 16)
    ).reshape(-1)
    own_ids = owned_tiles(owner_map, own_rank, device, own_count)
    listed = pick_rows(pattern, own_ids)
    near_ok = jnp.any(listed[:, :, None] == near_tile_rows[None, None, :], axis=1)
    far_ok = jnp.any(listed[:, :, None] == far_tile_rows[None, None, :], axis=1)
    query_own = pick(own_rank, near_tile_rows)
    near_bias = jnp.where(jnp.take(near_ok, query_own, axis=0, mode="clip"), 0.0, masked_score)
    far_bias = jnp.where(jnp.take(far_ok, query_own, axis=0, mode="clip"), 0.0, masked_score)
    near_bias = near_bias.astype(jnp.float32)
    far_bias = far_bias.astype(jnp.float32)
    chunk_width = channels // HEAD_CHUNKS
    outputs = []
    logs = []
    packed = pack(far_send_rows, own_send_rows, query_feats, key_feats, value_feats, HEAD_CHUNKS)
    for chunk in range(HEAD_CHUNKS):
        sent = packed[chunk]
        got = lax.all_to_all(sent, "seq", split_axis=0, concat_axis=0, tiled=True)
        mixed, head_logs = attend(got, unit, near_bias, far_bias)
        returned = lax.all_to_all(mixed, "seq", split_axis=0, concat_axis=0, tiled=True)
        outputs.append(returned.reshape(-1, chunk_width))
        logs.append(head_logs[:, :, 0])
    head_logs = jnp.concatenate(logs, axis=0)
    own_class = own_ids // piece_count
    own_slot = pick(class_rank, own_ids)
    gather_rows = (
        supplier_of(own_class[:, None], slice_iota[None, :], frame_devs) * capacity
        + own_slot[:, None]
    )
    log_rows = (gather_rows[:, :, None] * 16 + token_iota).reshape(-1)
    heads = channels // HEAD_DIM
    log_sums = (
        jnp.take(head_logs, log_rows, axis=1, mode="clip")
        .reshape(heads, own_count, 64)
        .transpose(1, 0, 2)
        .reshape(1, own_count, heads * 64)
    )
    local_iota_rows = jnp.arange(local_rows, dtype=jnp.int32)
    strip = local_iota_rows // (4 * WIDTH)
    height = local_iota_rows % (4 * WIDTH) // WIDTH
    column = local_iota_rows % WIDTH
    piece = strip * blocks + column // 4
    token = height * 4 + column % 4
    back_rows = (pick(my_owner, piece) * capacity + pick(my_slot, piece)) * 16 + token
    attended = jnp.concatenate(
        [jnp.take(part, back_rows, axis=0, mode="clip") for part in outputs], axis=1
    )
    return (attended, log_sums)


def solution(mesh):
    placed = (
        P(("groups", "seq"), None),
        P(("groups", "seq"), None),
        P(("groups", "seq"), None),
        P("groups"),
        P("groups", None),
    )
    return jax.shard_map(
        shards,
        mesh=mesh,
        in_specs=placed,
        out_specs=(P(("groups", "seq"), None), P(("groups", "seq"), None, None)),
        check_vma=False,
    )
```

```python
import jax
import jax.numpy as jnp
from jax import lax
from jax.sharding import PartitionSpec as P
from jax.experimental import pallas as pl

HEADS = 20
HEAD_DIM = 128
WIDTH = 64
FRAMES = 16


masked_score = -1e30


def frame_pieces(rows_in, strips):
    channels = rows_in.shape[1]
    shaped = rows_in.reshape(strips, 4, WIDTH // 4, 4, channels)
    return shaped.transpose(0, 2, 1, 3, 4).reshape(strips * (WIDTH // 4), 16, channels)


def frame_rows(pieces, strips):
    channels = pieces.shape[2]
    shaped = pieces.reshape(strips, WIDTH // 4, 4, 4, channels)
    return shaped.transpose(0, 2, 1, 3, 4).reshape(strips * 4 * WIDTH, channels)


def owner_tables(owner_map, group_size, piece_count):
    tile_count = owner_map.shape[0]
    devices = jnp.arange(group_size, dtype=jnp.int32)
    onehot = (owner_map[:, None] == devices[None, :]).astype(jnp.int32)
    running = jnp.cumsum(onehot, axis=0)
    own_rank = jnp.sum(onehot * running, axis=1) - 1
    by_class = owner_map.reshape(tile_count // piece_count, piece_count)
    local_iota = jnp.arange(piece_count, dtype=jnp.int32)
    earlier = (by_class[:, :, None] == by_class[:, None, :]) & (
        local_iota[None, None, :] < local_iota[None, :, None]
    )
    class_rank = jnp.sum(earlier.astype(jnp.int32), axis=2).reshape(tile_count)
    return (own_rank, class_rank)


def owned_tiles(owner_map, own_rank, device, own_count):
    tile_iota = jnp.arange(owner_map.shape[0], dtype=jnp.int32)
    slot_iota = jnp.arange(own_count, dtype=jnp.int32)
    match_rows = (owner_map[None, :] == device) & (own_rank[None, :] == slot_iota[:, None])
    return jnp.sum(jnp.where(match_rows, tile_iota[None, :], 0), axis=1)


def pick(table, index):
    iota = jnp.arange(table.shape[0], dtype=jnp.int32)
    hit = index[..., None] == iota
    return jnp.sum(jnp.where(hit, table, 0), axis=-1).astype(table.dtype)


def pick_rows(table, index):
    iota = jnp.arange(table.shape[0], dtype=jnp.int32)
    hit = (index[..., None] == iota)[..., None]
    return jnp.sum(jnp.where(hit, table, 0), axis=-2).astype(table.dtype)


def request_table(owner_map, pattern, group_size):
    devices = jnp.arange(group_size, dtype=jnp.int32)
    entry_owner = pick(owner_map, pattern)
    foreign = entry_owner != owner_map[:, None]
    entry_hit = (entry_owner[:, :, None] == devices[None, None, :]) & foreign[:, :, None]
    per_tile = jnp.max(jnp.where(entry_hit, pattern[:, :, None], -1), axis=1)
    per_user = owner_map[None, :] == devices[:, None]
    return jnp.max(jnp.where(per_user[:, :, None], per_tile[None, :, :], -1), axis=1)


def supplier_of(tile_class, frame_slice, frame_devs):
    return (4 * (tile_class // frame_devs) + frame_slice) * frame_devs + tile_class % frame_devs


def expand_mask(block_mask):
    query_tiles = block_mask.shape[0]
    key_tiles = block_mask.shape[1]
    wide = jnp.broadcast_to(block_mask[:, None, :, None], (query_tiles, 64, key_tiles, 64))
    return wide.reshape(query_tiles * 64, key_tiles * 64)


def head_part(matrix, offset):
    return lax.dynamic_slice_in_dim(matrix, offset, HEAD_DIM, 1)


def head_scores(query_head, key_rows, offset, mask):
    key_head = head_part(key_rows, offset)
    scores = lax.dot_general(
        query_head, key_head, (((1,), (1,)), ((), ())), preferred_element_type=jnp.float32
    ) * HEAD_DIM ** (-0.5)
    return jnp.where(mask, scores, masked_score)


FAR_SLOTS = 4
INTERPRET = False
HEAD_CHUNKS = 2


HEADS_PER_STEP = 2


def attention_kernel(
    far_key_ref, far_value_ref, query_ref, near_key_ref, near_value_ref, near_bias_ref,
    far_bias_ref, out_ref, log_ref
):
    def flat(ref, columns):
        block = ref[:, :, columns]
        return block.reshape(block.shape[0] * block.shape[1], block.shape[2])

    dims = (((1,), (1,)), ((), ()))
    scale = HEAD_DIM ** (-0.5)
    near_bias = near_bias_ref[...]
    far_bias = far_bias_ref[...]
    for step_head in range(log_ref.shape[0]):
        columns = slice(step_head * HEAD_DIM, (step_head + 1) * HEAD_DIM)
        query = flat(query_ref, columns)
        near_scores = lax.dot_general(
            query, flat(near_key_ref, columns), dims, preferred_element_type=jnp.float32
        ) * scale + near_bias
        far_scores = lax.dot_general(
            query, flat(far_key_ref, columns), dims, preferred_element_type=jnp.float32
        ) * scale + far_bias
        row_max = jnp.maximum(
            jnp.max(near_scores, axis=1, keepdims=True),
            jnp.max(far_scores, axis=1, keepdims=True),
        )
        near_exp = jnp.exp(near_scores - row_max)
        far_exp = jnp.exp(far_scores - row_max)
        total = jnp.sum(near_exp, axis=1, keepdims=True) + jnp.sum(
            far_exp, axis=1, keepdims=True
        )
        log_total = row_max + jnp.log(total)
        inverse = 1.0 / total
        near_weights = (near_exp * inverse).astype(jnp.bfloat16)
        far_weights = (far_exp * inverse).astype(jnp.bfloat16)
        mixed = jnp.dot(
            near_weights, flat(near_value_ref, columns), preferred_element_type=jnp.float32
        )
        mixed = mixed + jnp.dot(
            far_weights, flat(far_value_ref, columns), preferred_element_type=jnp.float32
        )
        out_shape = out_ref.shape
        out_ref[:, :, columns] = mixed.astype(out_ref.dtype).reshape(
            out_shape[0], out_shape[1], HEAD_DIM
        )
        log_ref[step_head] = log_total


def attend(got, unit, near_bias, far_bias):
    group_size, _, channels = got.shape
    far_rows = FAR_SLOTS * 16
    rows = group_size * unit
    heads = channels // HEAD_DIM
    per_step = HEADS_PER_STEP if heads % HEADS_PER_STEP == 0 else 1
    width = per_step * HEAD_DIM
    base = 2 * far_rows // unit
    far_spec = (group_size, far_rows, width)
    own_spec = (group_size, unit, width)
    return pl.pallas_call(
        attention_kernel,
        grid=(heads // per_step,),
        in_specs=[
            pl.BlockSpec(far_spec, lambda h: (0, 0, h)),
            pl.BlockSpec(far_spec, lambda h: (0, 1, h)),
            pl.BlockSpec(own_spec, lambda h: (0, base, h)),
            pl.BlockSpec(own_spec, lambda h: (0, base + 1, h)),
            pl.BlockSpec(own_spec, lambda h: (0, base + 2, h)),
            pl.BlockSpec((rows, rows), lambda h: (0, 0)),
            pl.BlockSpec((rows, group_size * far_rows), lambda h: (0, 0)),
        ],
        out_specs=[
            pl.BlockSpec(own_spec, lambda h: (0, 0, h)),
            pl.BlockSpec((per_step, rows, 1), lambda h: (h, 0, 0)),
        ],
        out_shape=[
            jax.ShapeDtypeStruct((group_size, unit, channels), jnp.bfloat16),
            jax.ShapeDtypeStruct((heads, rows, 1), jnp.float32),
        ],
        interpret=INTERPRET,
    )(got, got, got, got, got, near_bias, far_bias)


PACK_DESTS = 4


def pack_kernel(far_index_ref, own_index_ref, query_ref, key_ref, value_ref, *out_refs):
    dests = out_refs[0].shape[0]
    local_rows = query_ref.shape[0]

    def one_hot(index_ref):
        count = index_ref.shape[0]
        iota = lax.broadcasted_iota(jnp.int32, (count, local_rows), 1)
        return jnp.where(index_ref[...] == iota, 1.0, 0.0).astype(jnp.bfloat16), count // dests

    far_hot, far_rows = one_hot(far_index_ref)
    own_hot, own_rows = one_hot(own_index_ref)
    base = 2 * far_rows
    for index, out_ref in enumerate(out_refs):
        width = out_ref.shape[2]
        columns = slice(index * width, (index + 1) * width)

        def select(hot, source_ref, rows):
            picked = jnp.dot(hot, source_ref[:, columns], preferred_element_type=jnp.float32)
            return picked.astype(out_ref.dtype).reshape(dests, rows, width)

        out_ref[:, 0:far_rows, :] = select(far_hot, key_ref, far_rows)
        out_ref[:, far_rows:base, :] = select(far_hot, value_ref, far_rows)
        out_ref[:, base : base + own_rows, :] = select(own_hot, query_ref, own_rows)
        out_ref[:, base + own_rows : base + 2 * own_rows, :] = select(own_hot, key_ref, own_rows)
        out_ref[:, base + 2 * own_rows : base + 3 * own_rows, :] = select(
            own_hot, value_ref, own_rows
        )


def pack(far_rows, own_rows, query_feats, key_feats, value_feats, chunks):
    group_size, far_count = far_rows.shape
    own_count = own_rows.shape[1]
    local_rows, channels = query_feats.shape
    width = channels // chunks
    dests = PACK_DESTS if group_size % PACK_DESTS == 0 else 1
    total = 2 * far_count + 3 * own_count
    source_spec = pl.BlockSpec((local_rows, channels), lambda j: (0, 0))
    out_spec = pl.BlockSpec((dests, total, width), lambda j: (j, 0, 0))
    return pl.pallas_call(
        pack_kernel,
        grid=(group_size // dests,),
        in_specs=[
            pl.BlockSpec((dests * far_count, 1), lambda j: (j, 0)),
            pl.BlockSpec((dests * own_count, 1), lambda j: (j, 0)),
            source_spec,
            source_spec,
            source_spec,
        ],
        out_specs=[out_spec] * chunks,
        out_shape=[jax.ShapeDtypeStruct((group_size, total, width), query_feats.dtype)] * chunks,
        interpret=INTERPRET,
    )(far_rows.reshape(-1, 1), own_rows.reshape(-1, 1), query_feats, key_feats, value_feats)


def class_of(devices, frame_devs):
    return devices // frame_devs // 4 * frame_devs + devices % frame_devs


def ranked_pick(candidates, wanted, slot_count):
    rank = jnp.cumsum(wanted.astype(jnp.int32), axis=-1) - 1
    slots = jnp.arange(slot_count, dtype=jnp.int32)
    hit = wanted[..., None] & (rank[..., None] == slots)
    picked = jnp.sum(jnp.where(hit, candidates[..., None], 0), axis=-2)
    return picked, jnp.any(hit, axis=-2)


def shards(query_feats, key_feats, value_feats, owner_map, pattern):
    group_size = lax.axis_size("seq")
    device = lax.axis_index("seq")
    local_rows, channels = query_feats.shape
    strips = local_rows // (4 * WIDTH)
    blocks = WIDTH // 4
    piece_count = strips * blocks
    tile_count = owner_map.shape[0]
    own_count = tile_count // group_size
    capacity = (piece_count + group_size - 1) // group_size
    unit = capacity * 16
    frame_devs = group_size // FRAMES
    devices = jnp.arange(group_size, dtype=jnp.int32)
    local_iota = jnp.arange(piece_count, dtype=jnp.int32)
    cap_iota = jnp.arange(capacity, dtype=jnp.int32)
    slice_iota = jnp.arange(4, dtype=jnp.int32)
    token_iota = jnp.arange(16, dtype=jnp.int32)

    def piece_rows(pieces):
        strip = pieces // blocks
        column = pieces % blocks
        return (
            strip[..., None] * (4 * WIDTH)
            + (token_iota // 4) * WIDTH
            + column[..., None] * 4
            + token_iota % 4
        )

    own_rank, class_rank = owner_tables(owner_map, group_size, piece_count)
    my_class = class_of(device, frame_devs)
    my_tiles = my_class * piece_count + local_iota
    my_owner = lax.dynamic_slice_in_dim(owner_map, my_class * piece_count, piece_count)
    my_slot = lax.dynamic_slice_in_dim(class_rank, my_class * piece_count, piece_count)
    send_hit = (my_owner[None, None, :] == devices[:, None, None]) & (
        my_slot[None, None, :] == cap_iota[None, :, None]
    )
    send_index = jnp.sum(jnp.where(send_hit, local_iota[None, None, :], 0), axis=2)
    own_send_rows = piece_rows(send_index).reshape(group_size, unit)
    requests = request_table(owner_map, pattern, group_size)
    wanted = (requests >= 0) & (requests // piece_count == my_class)
    far_send_piece, _ = ranked_pick(requests % piece_count, wanted, FAR_SLOTS)
    far_send_rows = piece_rows(far_send_piece).reshape(group_size, FAR_SLOTS * 16)
    source_class = class_of(devices, frame_devs)
    class_tiles = source_class[:, None] * piece_count + local_iota[None, :]
    class_count = tile_count // piece_count
    mine = pick_rows(owner_map.reshape(class_count, piece_count), source_class) == device
    near_hit = mine[:, None, :] & (
        pick_rows(class_rank.reshape(class_count, piece_count), source_class)[:, None, :]
        == cap_iota[None, :, None]
    )
    near_tile = jnp.sum(jnp.where(near_hit, class_tiles[:, None, :], 0), axis=2)
    near_tile_rows = jnp.broadcast_to(near_tile[:, :, None], (group_size, capacity, 16)).reshape(-1)
    my_requests = lax.dynamic_index_in_dim(requests, device, axis=0, keepdims=False)
    far_wanted = (my_requests[None, :] >= 0) & (
        my_requests[None, :] // piece_count == source_class[:, None]
    )
    far_tile, far_valid = ranked_pick(
        jnp.broadcast_to(my_requests[None, :], (group_size, group_size)), far_wanted, FAR_SLOTS
    )
    far_tile = jnp.where(far_valid, far_tile, -1)
    far_tile_rows = jnp.broadcast_to(
        far_tile[:, :, None], (group_size, FAR_SLOTS, 16)
    ).reshape(-1)
    own_ids = owned_tiles(owner_map, own_rank, device, own_count)
    listed = pick_rows(pattern, own_ids)
    near_ok = jnp.any(listed[:, :, None] == near_tile_rows[None, None, :], axis=1)
    far_ok = jnp.any(listed[:, :, None] == far_tile_rows[None, None, :], axis=1)
    query_own = pick(own_rank, near_tile_rows)
    near_bias = jnp.where(jnp.take(near_ok, query_own, axis=0, mode="clip"), 0.0, masked_score)
    far_bias = jnp.where(jnp.take(far_ok, query_own, axis=0, mode="clip"), 0.0, masked_score)
    near_bias = near_bias.astype(jnp.float32)
    far_bias = far_bias.astype(jnp.float32)
    chunk_width = channels // HEAD_CHUNKS
    outputs = []
    logs = []
    packed = pack(far_send_rows, own_send_rows, query_feats, key_feats, value_feats, HEAD_CHUNKS)
    for chunk in range(HEAD_CHUNKS):
        sent = packed[chunk]
        got = lax.all_to_all(sent, "seq", split_axis=0, concat_axis=0, tiled=True)
        mixed, head_logs = attend(got, unit, near_bias, far_bias)
        returned = lax.all_to_all(mixed, "seq", split_axis=0, concat_axis=0, tiled=True)
        outputs.append(returned.reshape(-1, chunk_width))
        logs.append(head_logs[:, :, 0])
    head_logs = jnp.concatenate(logs, axis=0)
    own_class = own_ids // piece_count
    own_slot = pick(class_rank, own_ids)
    gather_rows = (
        supplier_of(own_class[:, None], slice_iota[None, :], frame_devs) * capacity
        + own_slot[:, None]
    )
    log_rows = (gather_rows[:, :, None] * 16 + token_iota).reshape(-1)
    heads = channels // HEAD_DIM
    log_sums = (
        jnp.take(head_logs, log_rows, axis=1, mode="clip")
        .reshape(heads, own_count, 64)
        .transpose(1, 0, 2)
        .reshape(1, own_count, heads * 64)
    )
    local_iota_rows = jnp.arange(local_rows, dtype=jnp.int32)
    strip = local_iota_rows // (4 * WIDTH)
    height = local_iota_rows % (4 * WIDTH) // WIDTH
    column = local_iota_rows % WIDTH
    piece = strip * blocks + column // 4
    token = height * 4 + column % 4
    back_rows = (pick(my_owner, piece) * capacity + pick(my_slot, piece)) * 16 + token
    attended = jnp.concatenate(
        [jnp.take(part, back_rows, axis=0, mode="clip") for part in outputs], axis=1
    )
    return (attended, log_sums)


def solution(mesh):
    placed = (
        P(("groups", "seq"), None),
        P(("groups", "seq"), None),
        P(("groups", "seq"), None),
        P("groups"),
        P("groups", None),
    )
    return jax.shard_map(
        shards,
        mesh=mesh,
        in_specs=placed,
        out_specs=(P(("groups", "seq"), None), P(("groups", "seq"), None, None)),
        check_vma=False,
    )
```

```python
import jax
import jax.numpy as jnp
from jax import lax
from jax.sharding import PartitionSpec as P
from jax.experimental import pallas as pl

HEADS = 20
HEAD_DIM = 128
WIDTH = 64
FRAMES = 16


masked_score = -1e30


def frame_pieces(rows_in, strips):
    channels = rows_in.shape[1]
    shaped = rows_in.reshape(strips, 4, WIDTH // 4, 4, channels)
    return shaped.transpose(0, 2, 1, 3, 4).reshape(strips * (WIDTH // 4), 16, channels)


def frame_rows(pieces, strips):
    channels = pieces.shape[2]
    shaped = pieces.reshape(strips, WIDTH // 4, 4, 4, channels)
    return shaped.transpose(0, 2, 1, 3, 4).reshape(strips * 4 * WIDTH, channels)


def owner_tables(owner_map, group_size, piece_count):
    tile_count = owner_map.shape[0]
    devices = jnp.arange(group_size, dtype=jnp.int32)
    onehot = (owner_map[:, None] == devices[None, :]).astype(jnp.int32)
    running = jnp.cumsum(onehot, axis=0)
    own_rank = jnp.sum(onehot * running, axis=1) - 1
    by_class = owner_map.reshape(tile_count // piece_count, piece_count)
    local_iota = jnp.arange(piece_count, dtype=jnp.int32)
    earlier = (by_class[:, :, None] == by_class[:, None, :]) & (
        local_iota[None, None, :] < local_iota[None, :, None]
    )
    class_rank = jnp.sum(earlier.astype(jnp.int32), axis=2).reshape(tile_count)
    return (own_rank, class_rank)


def owned_tiles(owner_map, own_rank, device, own_count):
    tile_iota = jnp.arange(owner_map.shape[0], dtype=jnp.int32)
    slot_iota = jnp.arange(own_count, dtype=jnp.int32)
    match_rows = (owner_map[None, :] == device) & (own_rank[None, :] == slot_iota[:, None])
    return jnp.sum(jnp.where(match_rows, tile_iota[None, :], 0), axis=1)


def pick(table, index):
    iota = jnp.arange(table.shape[0], dtype=jnp.int32)
    hit = index[..., None] == iota
    return jnp.sum(jnp.where(hit, table, 0), axis=-1).astype(table.dtype)


def pick_rows(table, index):
    iota = jnp.arange(table.shape[0], dtype=jnp.int32)
    hit = (index[..., None] == iota)[..., None]
    return jnp.sum(jnp.where(hit, table, 0), axis=-2).astype(table.dtype)


def request_table(owner_map, pattern, group_size):
    devices = jnp.arange(group_size, dtype=jnp.int32)
    entry_owner = pick(owner_map, pattern)
    foreign = entry_owner != owner_map[:, None]
    entry_hit = (entry_owner[:, :, None] == devices[None, None, :]) & foreign[:, :, None]
    per_tile = jnp.max(jnp.where(entry_hit, pattern[:, :, None], -1), axis=1)
    per_user = owner_map[None, :] == devices[:, None]
    return jnp.max(jnp.where(per_user[:, :, None], per_tile[None, :, :], -1), axis=1)


def supplier_of(tile_class, frame_slice, frame_devs):
    return (4 * (tile_class // frame_devs) + frame_slice) * frame_devs + tile_class % frame_devs


def expand_mask(block_mask):
    query_tiles = block_mask.shape[0]
    key_tiles = block_mask.shape[1]
    wide = jnp.broadcast_to(block_mask[:, None, :, None], (query_tiles, 64, key_tiles, 64))
    return wide.reshape(query_tiles * 64, key_tiles * 64)


def head_part(matrix, offset):
    return lax.dynamic_slice_in_dim(matrix, offset, HEAD_DIM, 1)


def head_scores(query_head, key_rows, offset, mask):
    key_head = head_part(key_rows, offset)
    scores = lax.dot_general(
        query_head, key_head, (((1,), (1,)), ((), ())), preferred_element_type=jnp.float32
    ) * HEAD_DIM ** (-0.5)
    return jnp.where(mask, scores, masked_score)


FAR_SLOTS = 4
INTERPRET = False
HEAD_CHUNKS = 2


HEADS_PER_STEP = 2


def attention_kernel(
    far_key_ref, far_value_ref, query_ref, near_key_ref, near_value_ref, near_bias_ref,
    far_bias_ref, out_ref, log_ref
):
    def flat(ref, columns):
        block = ref[:, :, columns]
        return block.reshape(block.shape[0] * block.shape[1], block.shape[2])

    dims = (((1,), (1,)), ((), ()))
    scale = HEAD_DIM ** (-0.5)
    near_bias = near_bias_ref[...]
    far_bias = far_bias_ref[...]
    for step_head in range(log_ref.shape[0]):
        columns = slice(step_head * HEAD_DIM, (step_head + 1) * HEAD_DIM)
        query = flat(query_ref, columns)
        near_scores = lax.dot_general(
            query, flat(near_key_ref, columns), dims, preferred_element_type=jnp.float32
        ) * scale + near_bias
        far_scores = lax.dot_general(
            query, flat(far_key_ref, columns), dims, preferred_element_type=jnp.float32
        ) * scale + far_bias
        row_max = jnp.maximum(
            jnp.max(near_scores, axis=1, keepdims=True),
            jnp.max(far_scores, axis=1, keepdims=True),
        )
        near_exp = jnp.exp(near_scores - row_max)
        far_exp = jnp.exp(far_scores - row_max)
        total = jnp.sum(near_exp, axis=1, keepdims=True) + jnp.sum(
            far_exp, axis=1, keepdims=True
        )
        log_total = row_max + jnp.log(total)
        inverse = 1.0 / total
        near_weights = (near_exp * inverse).astype(jnp.bfloat16)
        far_weights = (far_exp * inverse).astype(jnp.bfloat16)
        mixed = jnp.dot(
            near_weights, flat(near_value_ref, columns), preferred_element_type=jnp.float32
        )
        mixed = mixed + jnp.dot(
            far_weights, flat(far_value_ref, columns), preferred_element_type=jnp.float32
        )
        out_shape = out_ref.shape
        out_ref[:, :, columns] = mixed.astype(out_ref.dtype).reshape(
            out_shape[0], out_shape[1], HEAD_DIM
        )
        log_ref[step_head] = log_total


def attend(got, unit, near_bias, far_bias):
    group_size, _, channels = got.shape
    far_rows = FAR_SLOTS * 16
    rows = group_size * unit
    heads = channels // HEAD_DIM
    per_step = HEADS_PER_STEP if heads % HEADS_PER_STEP == 0 else 1
    width = per_step * HEAD_DIM
    base = 2 * far_rows // unit
    far_spec = (group_size, far_rows, width)
    own_spec = (group_size, unit, width)
    return pl.pallas_call(
        attention_kernel,
        grid=(heads // per_step,),
        in_specs=[
            pl.BlockSpec(far_spec, lambda h: (0, 0, h)),
            pl.BlockSpec(far_spec, lambda h: (0, 1, h)),
            pl.BlockSpec(own_spec, lambda h: (0, base, h)),
            pl.BlockSpec(own_spec, lambda h: (0, base + 1, h)),
            pl.BlockSpec(own_spec, lambda h: (0, base + 2, h)),
            pl.BlockSpec((rows, rows), lambda h: (0, 0)),
            pl.BlockSpec((rows, group_size * far_rows), lambda h: (0, 0)),
        ],
        out_specs=[
            pl.BlockSpec(own_spec, lambda h: (0, 0, h)),
            pl.BlockSpec((per_step, rows, 1), lambda h: (h, 0, 0)),
        ],
        out_shape=[
            jax.ShapeDtypeStruct((group_size, unit, channels), jnp.bfloat16),
            jax.ShapeDtypeStruct((heads, rows, 1), jnp.float32),
        ],
        interpret=INTERPRET,
    )(got, got, got, got, got, near_bias, far_bias)


PACK_DESTS = 4


def pack_kernel(far_index_ref, own_index_ref, query_ref, key_ref, value_ref, *out_refs):
    dests = out_refs[0].shape[0]
    local_rows = query_ref.shape[0]

    def one_hot(index_ref):
        count = index_ref.shape[0]
        iota = lax.broadcasted_iota(jnp.int32, (count, local_rows), 1)
        return jnp.where(index_ref[...] == iota, 1.0, 0.0).astype(jnp.bfloat16), count // dests

    far_hot, far_rows = one_hot(far_index_ref)
    own_hot, own_rows = one_hot(own_index_ref)
    base = 2 * far_rows
    for index, out_ref in enumerate(out_refs):
        width = out_ref.shape[2]
        columns = slice(index * width, (index + 1) * width)

        def select(hot, source_ref, rows):
            picked = jnp.dot(hot, source_ref[:, columns], preferred_element_type=jnp.float32)
            return picked.astype(out_ref.dtype).reshape(dests, rows, width)

        out_ref[:, 0:far_rows, :] = select(far_hot, key_ref, far_rows)
        out_ref[:, far_rows:base, :] = select(far_hot, value_ref, far_rows)
        out_ref[:, base : base + own_rows, :] = select(own_hot, query_ref, own_rows)
        out_ref[:, base + own_rows : base + 2 * own_rows, :] = select(own_hot, key_ref, own_rows)
        out_ref[:, base + 2 * own_rows : base + 3 * own_rows, :] = select(
            own_hot, value_ref, own_rows
        )


def pack(far_rows, own_rows, query_feats, key_feats, value_feats, chunks):
    group_size, far_count = far_rows.shape
    own_count = own_rows.shape[1]
    local_rows, channels = query_feats.shape
    width = channels // chunks
    dests = PACK_DESTS if group_size % PACK_DESTS == 0 else 1
    total = 2 * far_count + 3 * own_count
    source_spec = pl.BlockSpec((local_rows, channels), lambda j: (0, 0))
    out_spec = pl.BlockSpec((dests, total, width), lambda j: (j, 0, 0))
    return pl.pallas_call(
        pack_kernel,
        grid=(group_size // dests,),
        in_specs=[
            pl.BlockSpec((dests * far_count, 1), lambda j: (j, 0)),
            pl.BlockSpec((dests * own_count, 1), lambda j: (j, 0)),
            source_spec,
            source_spec,
            source_spec,
        ],
        out_specs=[out_spec] * chunks,
        out_shape=[jax.ShapeDtypeStruct((group_size, total, width), query_feats.dtype)] * chunks,
        interpret=INTERPRET,
    )(far_rows.reshape(-1, 1), own_rows.reshape(-1, 1), query_feats, key_feats, value_feats)


def unpack_kernel(index_ref, part_ref, prior_ref, out_ref):
    del prior_ref
    count, rows = index_ref.shape[0], part_ref.shape[0]
    iota = lax.broadcasted_iota(jnp.int32, (count, rows), 1)
    hot = jnp.where(index_ref[...] == iota, 1.0, 0.0).astype(jnp.bfloat16)
    picked = jnp.dot(hot, part_ref[...], preferred_element_type=jnp.float32)
    out_ref[...] = picked.astype(out_ref.dtype)


def unpack(index, part, prior, column_block):
    rows, width = part.shape
    return pl.pallas_call(
        unpack_kernel,
        grid=(1,),
        in_specs=[
            pl.BlockSpec((rows, 1), lambda i: (0, 0)),
            pl.BlockSpec((rows, width), lambda i: (0, 0)),
            pl.BlockSpec((rows, width), lambda i: (0, column_block)),
        ],
        out_specs=pl.BlockSpec((rows, width), lambda i: (0, column_block)),
        out_shape=jax.ShapeDtypeStruct(prior.shape, prior.dtype),
        input_output_aliases={2: 0},
        interpret=INTERPRET,
    )(index.reshape(-1, 1), part, prior)


def class_of(devices, frame_devs):
    return devices // frame_devs // 4 * frame_devs + devices % frame_devs


def ranked_pick(candidates, wanted, slot_count):
    rank = jnp.cumsum(wanted.astype(jnp.int32), axis=-1) - 1
    slots = jnp.arange(slot_count, dtype=jnp.int32)
    hit = wanted[..., None] & (rank[..., None] == slots)
    picked = jnp.sum(jnp.where(hit, candidates[..., None], 0), axis=-2)
    return picked, jnp.any(hit, axis=-2)


def shards(query_feats, key_feats, value_feats, owner_map, pattern):
    group_size = lax.axis_size("seq")
    device = lax.axis_index("seq")
    local_rows, channels = query_feats.shape
    strips = local_rows // (4 * WIDTH)
    blocks = WIDTH // 4
    piece_count = strips * blocks
    tile_count = owner_map.shape[0]
    own_count = tile_count // group_size
    capacity = (piece_count + group_size - 1) // group_size
    unit = capacity * 16
    frame_devs = group_size // FRAMES
    devices = jnp.arange(group_size, dtype=jnp.int32)
    local_iota = jnp.arange(piece_count, dtype=jnp.int32)
    cap_iota = jnp.arange(capacity, dtype=jnp.int32)
    slice_iota = jnp.arange(4, dtype=jnp.int32)
    token_iota = jnp.arange(16, dtype=jnp.int32)

    def piece_rows(pieces):
        strip = pieces // blocks
        column = pieces % blocks
        return (
            strip[..., None] * (4 * WIDTH)
            + (token_iota // 4) * WIDTH
            + column[..., None] * 4
            + token_iota % 4
        )

    own_rank, class_rank = owner_tables(owner_map, group_size, piece_count)
    my_class = class_of(device, frame_devs)
    my_tiles = my_class * piece_count + local_iota
    my_owner = lax.dynamic_slice_in_dim(owner_map, my_class * piece_count, piece_count)
    my_slot = lax.dynamic_slice_in_dim(class_rank, my_class * piece_count, piece_count)
    send_hit = (my_owner[None, None, :] == devices[:, None, None]) & (
        my_slot[None, None, :] == cap_iota[None, :, None]
    )
    send_index = jnp.sum(jnp.where(send_hit, local_iota[None, None, :], 0), axis=2)
    own_send_rows = piece_rows(send_index).reshape(group_size, unit)
    requests = request_table(owner_map, pattern, group_size)
    wanted = (requests >= 0) & (requests // piece_count == my_class)
    far_send_piece, _ = ranked_pick(requests % piece_count, wanted, FAR_SLOTS)
    far_send_rows = piece_rows(far_send_piece).reshape(group_size, FAR_SLOTS * 16)
    source_class = class_of(devices, frame_devs)
    class_tiles = source_class[:, None] * piece_count + local_iota[None, :]
    class_count = tile_count // piece_count
    mine = pick_rows(owner_map.reshape(class_count, piece_count), source_class) == device
    near_hit = mine[:, None, :] & (
        pick_rows(class_rank.reshape(class_count, piece_count), source_class)[:, None, :]
        == cap_iota[None, :, None]
    )
    near_tile = jnp.sum(jnp.where(near_hit, class_tiles[:, None, :], 0), axis=2)
    near_tile_rows = jnp.broadcast_to(near_tile[:, :, None], (group_size, capacity, 16)).reshape(-1)
    my_requests = lax.dynamic_index_in_dim(requests, device, axis=0, keepdims=False)
    far_wanted = (my_requests[None, :] >= 0) & (
        my_requests[None, :] // piece_count == source_class[:, None]
    )
    far_tile, far_valid = ranked_pick(
        jnp.broadcast_to(my_requests[None, :], (group_size, group_size)), far_wanted, FAR_SLOTS
    )
    far_tile = jnp.where(far_valid, far_tile, -1)
    far_tile_rows = jnp.broadcast_to(
        far_tile[:, :, None], (group_size, FAR_SLOTS, 16)
    ).reshape(-1)
    own_ids = owned_tiles(owner_map, own_rank, device, own_count)
    listed = pick_rows(pattern, own_ids)
    near_ok = jnp.any(listed[:, :, None] == near_tile_rows[None, None, :], axis=1)
    far_ok = jnp.any(listed[:, :, None] == far_tile_rows[None, None, :], axis=1)
    query_own = pick(own_rank, near_tile_rows)
    near_bias = jnp.where(jnp.take(near_ok, query_own, axis=0, mode="clip"), 0.0, masked_score)
    far_bias = jnp.where(jnp.take(far_ok, query_own, axis=0, mode="clip"), 0.0, masked_score)
    near_bias = near_bias.astype(jnp.float32)
    far_bias = far_bias.astype(jnp.float32)
    chunk_width = channels // HEAD_CHUNKS
    outputs = []
    logs = []
    packed = pack(far_send_rows, own_send_rows, query_feats, key_feats, value_feats, HEAD_CHUNKS)
    for chunk in range(HEAD_CHUNKS):
        sent = packed[chunk]
        got = lax.all_to_all(sent, "seq", split_axis=0, concat_axis=0, tiled=True)
        mixed, head_logs = attend(got, unit, near_bias, far_bias)
        returned = lax.all_to_all(mixed, "seq", split_axis=0, concat_axis=0, tiled=True)
        outputs.append(returned.reshape(-1, chunk_width))
        logs.append(head_logs[:, :, 0])
    head_logs = jnp.concatenate(logs, axis=0)
    own_class = own_ids // piece_count
    own_slot = pick(class_rank, own_ids)
    gather_rows = (
        supplier_of(own_class[:, None], slice_iota[None, :], frame_devs) * capacity
        + own_slot[:, None]
    )
    log_rows = (gather_rows[:, :, None] * 16 + token_iota).reshape(-1)
    heads = channels // HEAD_DIM
    log_sums = (
        jnp.take(head_logs, log_rows, axis=1, mode="clip")
        .reshape(heads, own_count, 64)
        .transpose(1, 0, 2)
        .reshape(1, own_count, heads * 64)
    )
    local_iota_rows = jnp.arange(local_rows, dtype=jnp.int32)
    strip = local_iota_rows // (4 * WIDTH)
    height = local_iota_rows % (4 * WIDTH) // WIDTH
    column = local_iota_rows % WIDTH
    piece = strip * blocks + column // 4
    token = height * 4 + column % 4
    back_rows = (pick(my_owner, piece) * capacity + pick(my_slot, piece)) * 16 + token
    attended = jnp.zeros((local_rows, channels), jnp.bfloat16)
    for chunk, part in enumerate(outputs):
        attended = unpack(back_rows, part, attended, chunk)
    return (attended, log_sums)


def solution(mesh):
    placed = (
        P(("groups", "seq"), None),
        P(("groups", "seq"), None),
        P(("groups", "seq"), None),
        P("groups"),
        P("groups", None),
    )
    return jax.shard_map(
        shards,
        mesh=mesh,
        in_specs=placed,
        out_specs=(P(("groups", "seq"), None), P(("groups", "seq"), None, None)),
        check_vma=False,
    )
```

```python
import jax
import jax.numpy as jnp
from jax import lax
from jax.sharding import PartitionSpec as P
from jax.experimental import pallas as pl

HEADS = 20
HEAD_DIM = 128
WIDTH = 64
FRAMES = 16


masked_score = -1e30


def frame_pieces(rows_in, strips):
    channels = rows_in.shape[1]
    shaped = rows_in.reshape(strips, 4, WIDTH // 4, 4, channels)
    return shaped.transpose(0, 2, 1, 3, 4).reshape(strips * (WIDTH // 4), 16, channels)


def frame_rows(pieces, strips):
    channels = pieces.shape[2]
    shaped = pieces.reshape(strips, WIDTH // 4, 4, 4, channels)
    return shaped.transpose(0, 2, 1, 3, 4).reshape(strips * 4 * WIDTH, channels)


def owner_tables(owner_map, group_size, piece_count):
    tile_count = owner_map.shape[0]
    devices = jnp.arange(group_size, dtype=jnp.int32)
    onehot = (owner_map[:, None] == devices[None, :]).astype(jnp.int32)
    running = jnp.cumsum(onehot, axis=0)
    own_rank = jnp.sum(onehot * running, axis=1) - 1
    by_class = owner_map.reshape(tile_count // piece_count, piece_count)
    local_iota = jnp.arange(piece_count, dtype=jnp.int32)
    earlier = (by_class[:, :, None] == by_class[:, None, :]) & (
        local_iota[None, None, :] < local_iota[None, :, None]
    )
    class_rank = jnp.sum(earlier.astype(jnp.int32), axis=2).reshape(tile_count)
    return (own_rank, class_rank)


def owned_tiles(owner_map, own_rank, device, own_count):
    tile_iota = jnp.arange(owner_map.shape[0], dtype=jnp.int32)
    slot_iota = jnp.arange(own_count, dtype=jnp.int32)
    match_rows = (owner_map[None, :] == device) & (own_rank[None, :] == slot_iota[:, None])
    return jnp.sum(jnp.where(match_rows, tile_iota[None, :], 0), axis=1)


def pick(table, index):
    iota = jnp.arange(table.shape[0], dtype=jnp.int32)
    hit = index[..., None] == iota
    return jnp.sum(jnp.where(hit, table, 0), axis=-1).astype(table.dtype)


def pick_rows(table, index):
    iota = jnp.arange(table.shape[0], dtype=jnp.int32)
    hit = (index[..., None] == iota)[..., None]
    return jnp.sum(jnp.where(hit, table, 0), axis=-2).astype(table.dtype)


def request_table(owner_map, pattern, group_size):
    devices = jnp.arange(group_size, dtype=jnp.int32)
    entry_owner = pick(owner_map, pattern)
    foreign = entry_owner != owner_map[:, None]
    entry_hit = (entry_owner[:, :, None] == devices[None, None, :]) & foreign[:, :, None]
    per_tile = jnp.max(jnp.where(entry_hit, pattern[:, :, None], -1), axis=1)
    per_user = owner_map[None, :] == devices[:, None]
    return jnp.max(jnp.where(per_user[:, :, None], per_tile[None, :, :], -1), axis=1)


def supplier_of(tile_class, frame_slice, frame_devs):
    return (4 * (tile_class // frame_devs) + frame_slice) * frame_devs + tile_class % frame_devs


def expand_mask(block_mask):
    query_tiles = block_mask.shape[0]
    key_tiles = block_mask.shape[1]
    wide = jnp.broadcast_to(block_mask[:, None, :, None], (query_tiles, 64, key_tiles, 64))
    return wide.reshape(query_tiles * 64, key_tiles * 64)


def head_part(matrix, offset):
    return lax.dynamic_slice_in_dim(matrix, offset, HEAD_DIM, 1)


def head_scores(query_head, key_rows, offset, mask):
    key_head = head_part(key_rows, offset)
    scores = lax.dot_general(
        query_head, key_head, (((1,), (1,)), ((), ())), preferred_element_type=jnp.float32
    ) * HEAD_DIM ** (-0.5)
    return jnp.where(mask, scores, masked_score)


FAR_SLOTS = 4
INTERPRET = False
HEAD_CHUNKS = 2


HEADS_PER_STEP = 2


def attention_kernel(
    far_key_ref, far_value_ref, query_ref, near_key_ref, near_value_ref, near_bias_ref,
    far_bias_ref, out_ref, log_ref
):
    def flat(ref, columns):
        block = ref[:, :, columns]
        return block.reshape(block.shape[0] * block.shape[1], block.shape[2])

    dims = (((1,), (1,)), ((), ()))
    scale = HEAD_DIM ** (-0.5)
    near_bias = near_bias_ref[...]
    far_bias = far_bias_ref[...]
    for step_head in range(log_ref.shape[0]):
        columns = slice(step_head * HEAD_DIM, (step_head + 1) * HEAD_DIM)
        query = flat(query_ref, columns)
        near_scores = lax.dot_general(
            query, flat(near_key_ref, columns), dims, preferred_element_type=jnp.float32
        ) * scale + near_bias
        far_scores = lax.dot_general(
            query, flat(far_key_ref, columns), dims, preferred_element_type=jnp.float32
        ) * scale + far_bias
        row_max = jnp.maximum(
            jnp.max(near_scores, axis=1, keepdims=True),
            jnp.max(far_scores, axis=1, keepdims=True),
        )
        near_exp = jnp.exp(near_scores - row_max)
        far_exp = jnp.exp(far_scores - row_max)
        total = jnp.sum(near_exp, axis=1, keepdims=True) + jnp.sum(
            far_exp, axis=1, keepdims=True
        )
        log_total = row_max + jnp.log(total)
        inverse = 1.0 / total
        near_weights = (near_exp * inverse).astype(jnp.bfloat16)
        far_weights = (far_exp * inverse).astype(jnp.bfloat16)
        mixed = jnp.dot(
            near_weights, flat(near_value_ref, columns), preferred_element_type=jnp.float32
        )
        mixed = mixed + jnp.dot(
            far_weights, flat(far_value_ref, columns), preferred_element_type=jnp.float32
        )
        out_shape = out_ref.shape
        out_ref[:, :, columns] = mixed.astype(out_ref.dtype).reshape(
            out_shape[0], out_shape[1], HEAD_DIM
        )
        log_ref[step_head] = log_total


def attend(got, unit, near_bias, far_bias):
    group_size, _, channels = got.shape
    far_rows = FAR_SLOTS * 16
    rows = group_size * unit
    heads = channels // HEAD_DIM
    per_step = HEADS_PER_STEP if heads % HEADS_PER_STEP == 0 else 1
    width = per_step * HEAD_DIM
    base = 2 * far_rows // unit
    far_spec = (group_size, far_rows, width)
    own_spec = (group_size, unit, width)
    return pl.pallas_call(
        attention_kernel,
        grid=(heads // per_step,),
        in_specs=[
            pl.BlockSpec(far_spec, lambda h: (0, 0, h)),
            pl.BlockSpec(far_spec, lambda h: (0, 1, h)),
            pl.BlockSpec(own_spec, lambda h: (0, base, h)),
            pl.BlockSpec(own_spec, lambda h: (0, base + 1, h)),
            pl.BlockSpec(own_spec, lambda h: (0, base + 2, h)),
            pl.BlockSpec((rows, rows), lambda h: (0, 0)),
            pl.BlockSpec((rows, group_size * far_rows), lambda h: (0, 0)),
        ],
        out_specs=[
            pl.BlockSpec(own_spec, lambda h: (0, 0, h)),
            pl.BlockSpec((per_step, rows, 1), lambda h: (h, 0, 0)),
        ],
        out_shape=[
            jax.ShapeDtypeStruct((group_size, unit, channels), jnp.bfloat16),
            jax.ShapeDtypeStruct((heads, rows, 1), jnp.float32),
        ],
        interpret=INTERPRET,
    )(got, got, got, got, got, near_bias, far_bias)


PACK_DESTS = 8


def pack_kernel(far_index_ref, own_index_ref, query_ref, key_ref, value_ref, *out_refs):
    dests = out_refs[0].shape[0]
    local_rows = query_ref.shape[0]

    def one_hot(index_ref):
        count = index_ref.shape[0]
        iota = lax.broadcasted_iota(jnp.int32, (count, local_rows), 1)
        return jnp.where(index_ref[...] == iota, 1.0, 0.0).astype(jnp.bfloat16), count // dests

    far_hot, far_rows = one_hot(far_index_ref)
    own_hot, own_rows = one_hot(own_index_ref)
    base = 2 * far_rows
    for index, out_ref in enumerate(out_refs):
        width = out_ref.shape[2]
        columns = slice(index * width, (index + 1) * width)

        def select(hot, source_ref, rows):
            picked = jnp.dot(hot, source_ref[:, columns], preferred_element_type=jnp.float32)
            return picked.astype(out_ref.dtype).reshape(dests, rows, width)

        out_ref[:, 0:far_rows, :] = select(far_hot, key_ref, far_rows)
        out_ref[:, far_rows:base, :] = select(far_hot, value_ref, far_rows)
        out_ref[:, base : base + own_rows, :] = select(own_hot, query_ref, own_rows)
        out_ref[:, base + own_rows : base + 2 * own_rows, :] = select(own_hot, key_ref, own_rows)
        out_ref[:, base + 2 * own_rows : base + 3 * own_rows, :] = select(
            own_hot, value_ref, own_rows
        )


def pack(far_rows, own_rows, query_feats, key_feats, value_feats, chunks):
    group_size, far_count = far_rows.shape
    own_count = own_rows.shape[1]
    local_rows, channels = query_feats.shape
    width = channels // chunks
    dests = PACK_DESTS if group_size % PACK_DESTS == 0 else 1
    total = 2 * far_count + 3 * own_count
    source_spec = pl.BlockSpec((local_rows, channels), lambda j: (0, 0))
    out_spec = pl.BlockSpec((dests, total, width), lambda j: (j, 0, 0))
    return pl.pallas_call(
        pack_kernel,
        grid=(group_size // dests,),
        in_specs=[
            pl.BlockSpec((dests * far_count, 1), lambda j: (j, 0)),
            pl.BlockSpec((dests * own_count, 1), lambda j: (j, 0)),
            source_spec,
            source_spec,
            source_spec,
        ],
        out_specs=[out_spec] * chunks,
        out_shape=[jax.ShapeDtypeStruct((group_size, total, width), query_feats.dtype)] * chunks,
        interpret=INTERPRET,
    )(far_rows.reshape(-1, 1), own_rows.reshape(-1, 1), query_feats, key_feats, value_feats)


def unpack_kernel(index_ref, part_ref, prior_ref, out_ref):
    del prior_ref
    count, rows = index_ref.shape[0], part_ref.shape[0]
    iota = lax.broadcasted_iota(jnp.int32, (count, rows), 1)
    hot = jnp.where(index_ref[...] == iota, 1.0, 0.0).astype(jnp.bfloat16)
    picked = jnp.dot(hot, part_ref[...], preferred_element_type=jnp.float32)
    out_ref[...] = picked.astype(out_ref.dtype)


def unpack(index, part, prior, column_block):
    rows, width = part.shape
    return pl.pallas_call(
        unpack_kernel,
        grid=(1,),
        in_specs=[
            pl.BlockSpec((rows, 1), lambda i: (0, 0)),
            pl.BlockSpec((rows, width), lambda i: (0, 0)),
            pl.BlockSpec((rows, width), lambda i: (0, column_block)),
        ],
        out_specs=pl.BlockSpec((rows, width), lambda i: (0, column_block)),
        out_shape=jax.ShapeDtypeStruct(prior.shape, prior.dtype),
        input_output_aliases={2: 0},
        interpret=INTERPRET,
    )(index.reshape(-1, 1), part, prior)


def class_of(devices, frame_devs):
    return devices // frame_devs // 4 * frame_devs + devices % frame_devs


def ranked_pick(candidates, wanted, slot_count):
    rank = jnp.cumsum(wanted.astype(jnp.int32), axis=-1) - 1
    slots = jnp.arange(slot_count, dtype=jnp.int32)
    hit = wanted[..., None] & (rank[..., None] == slots)
    picked = jnp.sum(jnp.where(hit, candidates[..., None], 0), axis=-2)
    return picked, jnp.any(hit, axis=-2)


def shards(query_feats, key_feats, value_feats, owner_map, pattern):
    group_size = lax.axis_size("seq")
    device = lax.axis_index("seq")
    local_rows, channels = query_feats.shape
    strips = local_rows // (4 * WIDTH)
    blocks = WIDTH // 4
    piece_count = strips * blocks
    tile_count = owner_map.shape[0]
    own_count = tile_count // group_size
    capacity = (piece_count + group_size - 1) // group_size
    unit = capacity * 16
    frame_devs = group_size // FRAMES
    devices = jnp.arange(group_size, dtype=jnp.int32)
    local_iota = jnp.arange(piece_count, dtype=jnp.int32)
    cap_iota = jnp.arange(capacity, dtype=jnp.int32)
    slice_iota = jnp.arange(4, dtype=jnp.int32)
    token_iota = jnp.arange(16, dtype=jnp.int32)

    def piece_rows(pieces):
        strip = pieces // blocks
        column = pieces % blocks
        return (
            strip[..., None] * (4 * WIDTH)
            + (token_iota // 4) * WIDTH
            + column[..., None] * 4
            + token_iota % 4
        )

    own_rank, class_rank = owner_tables(owner_map, group_size, piece_count)
    my_class = class_of(device, frame_devs)
    my_tiles = my_class * piece_count + local_iota
    my_owner = lax.dynamic_slice_in_dim(owner_map, my_class * piece_count, piece_count)
    my_slot = lax.dynamic_slice_in_dim(class_rank, my_class * piece_count, piece_count)
    send_hit = (my_owner[None, None, :] == devices[:, None, None]) & (
        my_slot[None, None, :] == cap_iota[None, :, None]
    )
    send_index = jnp.sum(jnp.where(send_hit, local_iota[None, None, :], 0), axis=2)
    own_send_rows = piece_rows(send_index).reshape(group_size, unit)
    requests = request_table(owner_map, pattern, group_size)
    wanted = (requests >= 0) & (requests // piece_count == my_class)
    far_send_piece, _ = ranked_pick(requests % piece_count, wanted, FAR_SLOTS)
    far_send_rows = piece_rows(far_send_piece).reshape(group_size, FAR_SLOTS * 16)
    source_class = class_of(devices, frame_devs)
    class_tiles = source_class[:, None] * piece_count + local_iota[None, :]
    class_count = tile_count // piece_count
    mine = pick_rows(owner_map.reshape(class_count, piece_count), source_class) == device
    near_hit = mine[:, None, :] & (
        pick_rows(class_rank.reshape(class_count, piece_count), source_class)[:, None, :]
        == cap_iota[None, :, None]
    )
    near_tile = jnp.sum(jnp.where(near_hit, class_tiles[:, None, :], 0), axis=2)
    near_tile_rows = jnp.broadcast_to(near_tile[:, :, None], (group_size, capacity, 16)).reshape(-1)
    my_requests = lax.dynamic_index_in_dim(requests, device, axis=0, keepdims=False)
    far_wanted = (my_requests[None, :] >= 0) & (
        my_requests[None, :] // piece_count == source_class[:, None]
    )
    far_tile, far_valid = ranked_pick(
        jnp.broadcast_to(my_requests[None, :], (group_size, group_size)), far_wanted, FAR_SLOTS
    )
    far_tile = jnp.where(far_valid, far_tile, -1)
    far_tile_rows = jnp.broadcast_to(
        far_tile[:, :, None], (group_size, FAR_SLOTS, 16)
    ).reshape(-1)
    own_ids = owned_tiles(owner_map, own_rank, device, own_count)
    listed = pick_rows(pattern, own_ids)
    near_ok = jnp.any(listed[:, :, None] == near_tile_rows[None, None, :], axis=1)
    far_ok = jnp.any(listed[:, :, None] == far_tile_rows[None, None, :], axis=1)
    query_own = pick(own_rank, near_tile_rows)
    near_bias = jnp.where(jnp.take(near_ok, query_own, axis=0, mode="clip"), 0.0, masked_score)
    far_bias = jnp.where(jnp.take(far_ok, query_own, axis=0, mode="clip"), 0.0, masked_score)
    near_bias = near_bias.astype(jnp.float32)
    far_bias = far_bias.astype(jnp.float32)
    chunk_width = channels // HEAD_CHUNKS
    outputs = []
    logs = []
    packed = pack(far_send_rows, own_send_rows, query_feats, key_feats, value_feats, HEAD_CHUNKS)
    for chunk in range(HEAD_CHUNKS):
        sent = packed[chunk]
        got = lax.all_to_all(sent, "seq", split_axis=0, concat_axis=0, tiled=True)
        mixed, head_logs = attend(got, unit, near_bias, far_bias)
        returned = lax.all_to_all(mixed, "seq", split_axis=0, concat_axis=0, tiled=True)
        outputs.append(returned.reshape(-1, chunk_width))
        logs.append(head_logs[:, :, 0])
    head_logs = jnp.concatenate(logs, axis=0)
    own_class = own_ids // piece_count
    own_slot = pick(class_rank, own_ids)
    gather_rows = (
        supplier_of(own_class[:, None], slice_iota[None, :], frame_devs) * capacity
        + own_slot[:, None]
    )
    log_rows = (gather_rows[:, :, None] * 16 + token_iota).reshape(-1)
    heads = channels // HEAD_DIM
    log_sums = (
        jnp.take(head_logs, log_rows, axis=1, mode="clip")
        .reshape(heads, own_count, 64)
        .transpose(1, 0, 2)
        .reshape(1, own_count, heads * 64)
    )
    local_iota_rows = jnp.arange(local_rows, dtype=jnp.int32)
    strip = local_iota_rows // (4 * WIDTH)
    height = local_iota_rows % (4 * WIDTH) // WIDTH
    column = local_iota_rows % WIDTH
    piece = strip * blocks + column // 4
    token = height * 4 + column % 4
    back_rows = (pick(my_owner, piece) * capacity + pick(my_slot, piece)) * 16 + token
    attended = jnp.zeros((local_rows, channels), jnp.bfloat16)
    for chunk, part in enumerate(outputs):
        attended = unpack(back_rows, part, attended, chunk)
    return (attended, log_sums)


def solution(mesh):
    placed = (
        P(("groups", "seq"), None),
        P(("groups", "seq"), None),
        P(("groups", "seq"), None),
        P("groups"),
        P("groups", None),
    )
    return jax.shard_map(
        shards,
        mesh=mesh,
        in_specs=placed,
        out_specs=(P(("groups", "seq"), None), P(("groups", "seq"), None, None)),
        check_vma=False,
    )
```

```python
import jax
import jax.numpy as jnp
from jax import lax
from jax.sharding import PartitionSpec as P
from jax.experimental import pallas as pl

HEADS = 20
HEAD_DIM = 128
WIDTH = 64
FRAMES = 16


masked_score = -1e30


def frame_pieces(rows_in, strips):
    channels = rows_in.shape[1]
    shaped = rows_in.reshape(strips, 4, WIDTH // 4, 4, channels)
    return shaped.transpose(0, 2, 1, 3, 4).reshape(strips * (WIDTH // 4), 16, channels)


def frame_rows(pieces, strips):
    channels = pieces.shape[2]
    shaped = pieces.reshape(strips, WIDTH // 4, 4, 4, channels)
    return shaped.transpose(0, 2, 1, 3, 4).reshape(strips * 4 * WIDTH, channels)


def owner_tables(owner_map, group_size, piece_count):
    tile_count = owner_map.shape[0]
    devices = jnp.arange(group_size, dtype=jnp.int32)
    onehot = (owner_map[:, None] == devices[None, :]).astype(jnp.int32)
    running = jnp.cumsum(onehot, axis=0)
    own_rank = jnp.sum(onehot * running, axis=1) - 1
    by_class = owner_map.reshape(tile_count // piece_count, piece_count)
    local_iota = jnp.arange(piece_count, dtype=jnp.int32)
    earlier = (by_class[:, :, None] == by_class[:, None, :]) & (
        local_iota[None, None, :] < local_iota[None, :, None]
    )
    class_rank = jnp.sum(earlier.astype(jnp.int32), axis=2).reshape(tile_count)
    return (own_rank, class_rank)


def owned_tiles(owner_map, own_rank, device, own_count):
    tile_iota = jnp.arange(owner_map.shape[0], dtype=jnp.int32)
    slot_iota = jnp.arange(own_count, dtype=jnp.int32)
    match_rows = (owner_map[None, :] == device) & (own_rank[None, :] == slot_iota[:, None])
    return jnp.sum(jnp.where(match_rows, tile_iota[None, :], 0), axis=1)


def pick(table, index):
    iota = jnp.arange(table.shape[0], dtype=jnp.int32)
    hit = index[..., None] == iota
    return jnp.sum(jnp.where(hit, table, 0), axis=-1).astype(table.dtype)


def pick_rows(table, index):
    iota = jnp.arange(table.shape[0], dtype=jnp.int32)
    hit = (index[..., None] == iota)[..., None]
    return jnp.sum(jnp.where(hit, table, 0), axis=-2).astype(table.dtype)


def request_table(owner_map, pattern, group_size):
    devices = jnp.arange(group_size, dtype=jnp.int32)
    entry_owner = pick(owner_map, pattern)
    foreign = entry_owner != owner_map[:, None]
    entry_hit = (entry_owner[:, :, None] == devices[None, None, :]) & foreign[:, :, None]
    per_tile = jnp.max(jnp.where(entry_hit, pattern[:, :, None], -1), axis=1)
    per_user = owner_map[None, :] == devices[:, None]
    return jnp.max(jnp.where(per_user[:, :, None], per_tile[None, :, :], -1), axis=1)


def supplier_of(tile_class, frame_slice, frame_devs):
    return (4 * (tile_class // frame_devs) + frame_slice) * frame_devs + tile_class % frame_devs


def expand_mask(block_mask):
    query_tiles = block_mask.shape[0]
    key_tiles = block_mask.shape[1]
    wide = jnp.broadcast_to(block_mask[:, None, :, None], (query_tiles, 64, key_tiles, 64))
    return wide.reshape(query_tiles * 64, key_tiles * 64)


def head_part(matrix, offset):
    return lax.dynamic_slice_in_dim(matrix, offset, HEAD_DIM, 1)


def head_scores(query_head, key_rows, offset, mask):
    key_head = head_part(key_rows, offset)
    scores = lax.dot_general(
        query_head, key_head, (((1,), (1,)), ((), ())), preferred_element_type=jnp.float32
    ) * HEAD_DIM ** (-0.5)
    return jnp.where(mask, scores, masked_score)


FAR_SLOTS = 4
INTERPRET = False
HEAD_CHUNKS = 2


HEADS_PER_STEP = 2


def attention_kernel(
    far_key_ref, far_value_ref, query_ref, near_key_ref, near_value_ref, near_bias_ref,
    far_bias_ref, out_ref, log_ref
):
    def flat(ref, columns):
        block = ref[:, :, columns]
        return block.reshape(block.shape[0] * block.shape[1], block.shape[2])

    dims = (((1,), (1,)), ((), ()))
    scale = HEAD_DIM ** (-0.5)
    near_bias = near_bias_ref[...]
    far_bias = far_bias_ref[...]
    for step_head in range(log_ref.shape[0]):
        columns = slice(step_head * HEAD_DIM, (step_head + 1) * HEAD_DIM)
        query = flat(query_ref, columns)
        near_scores = lax.dot_general(
            query, flat(near_key_ref, columns), dims, preferred_element_type=jnp.float32
        ) * scale + near_bias
        far_scores = lax.dot_general(
            query, flat(far_key_ref, columns), dims, preferred_element_type=jnp.float32
        ) * scale + far_bias
        row_max = jnp.maximum(
            jnp.max(near_scores, axis=1, keepdims=True),
            jnp.max(far_scores, axis=1, keepdims=True),
        )
        near_exp = jnp.exp(near_scores - row_max)
        far_exp = jnp.exp(far_scores - row_max)
        total = jnp.sum(near_exp, axis=1, keepdims=True) + jnp.sum(
            far_exp, axis=1, keepdims=True
        )
        log_total = row_max + jnp.log(total)
        inverse = 1.0 / total
        near_weights = (near_exp * inverse).astype(jnp.bfloat16)
        far_weights = (far_exp * inverse).astype(jnp.bfloat16)
        mixed = jnp.dot(
            near_weights, flat(near_value_ref, columns), preferred_element_type=jnp.float32
        )
        mixed = mixed + jnp.dot(
            far_weights, flat(far_value_ref, columns), preferred_element_type=jnp.float32
        )
        out_shape = out_ref.shape
        out_ref[:, :, columns] = mixed.astype(out_ref.dtype).reshape(
            out_shape[0], out_shape[1], HEAD_DIM
        )
        log_ref[step_head] = log_total


def attend(got, unit, near_bias, far_bias):
    group_size, _, channels = got.shape
    far_rows = FAR_SLOTS * 16
    rows = group_size * unit
    heads = channels // HEAD_DIM
    per_step = HEADS_PER_STEP if heads % HEADS_PER_STEP == 0 else 1
    width = per_step * HEAD_DIM
    base = 2 * far_rows // unit
    far_spec = (group_size, far_rows, width)
    own_spec = (group_size, unit, width)
    return pl.pallas_call(
        attention_kernel,
        grid=(heads // per_step,),
        in_specs=[
            pl.BlockSpec(far_spec, lambda h: (0, 0, h)),
            pl.BlockSpec(far_spec, lambda h: (0, 1, h)),
            pl.BlockSpec(own_spec, lambda h: (0, base, h)),
            pl.BlockSpec(own_spec, lambda h: (0, base + 1, h)),
            pl.BlockSpec(own_spec, lambda h: (0, base + 2, h)),
            pl.BlockSpec((rows, rows), lambda h: (0, 0)),
            pl.BlockSpec((rows, group_size * far_rows), lambda h: (0, 0)),
        ],
        out_specs=[
            pl.BlockSpec(own_spec, lambda h: (0, 0, h)),
            pl.BlockSpec((per_step, rows, 1), lambda h: (h, 0, 0)),
        ],
        out_shape=[
            jax.ShapeDtypeStruct((group_size, unit, channels), jnp.bfloat16),
            jax.ShapeDtypeStruct((heads, rows, 1), jnp.float32),
        ],
        interpret=INTERPRET,
    )(got, got, got, got, got, near_bias, far_bias)


PACK_DESTS = 2


def pack_kernel(far_index_ref, own_index_ref, query_ref, key_ref, value_ref, *out_refs):
    dests = out_refs[0].shape[0]
    local_rows = query_ref.shape[0]

    def one_hot(index_ref):
        count = index_ref.shape[0]
        iota = lax.broadcasted_iota(jnp.int32, (count, local_rows), 1)
        return jnp.where(index_ref[...] == iota, 1.0, 0.0).astype(jnp.bfloat16), count // dests

    far_hot, far_rows = one_hot(far_index_ref)
    own_hot, own_rows = one_hot(own_index_ref)
    base = 2 * far_rows
    for index, out_ref in enumerate(out_refs):
        width = out_ref.shape[2]
        columns = slice(index * width, (index + 1) * width)

        def select(hot, source_ref, rows):
            picked = jnp.dot(hot, source_ref[:, columns], preferred_element_type=jnp.float32)
            return picked.astype(out_ref.dtype).reshape(dests, rows, width)

        out_ref[:, 0:far_rows, :] = select(far_hot, key_ref, far_rows)
        out_ref[:, far_rows:base, :] = select(far_hot, value_ref, far_rows)
        out_ref[:, base : base + own_rows, :] = select(own_hot, query_ref, own_rows)
        out_ref[:, base + own_rows : base + 2 * own_rows, :] = select(own_hot, key_ref, own_rows)
        out_ref[:, base + 2 * own_rows : base + 3 * own_rows, :] = select(
            own_hot, value_ref, own_rows
        )


def pack(far_rows, own_rows, query_feats, key_feats, value_feats, chunks):
    group_size, far_count = far_rows.shape
    own_count = own_rows.shape[1]
    local_rows, channels = query_feats.shape
    width = channels // chunks
    dests = PACK_DESTS if group_size % PACK_DESTS == 0 else 1
    total = 2 * far_count + 3 * own_count
    source_spec = pl.BlockSpec((local_rows, channels), lambda j: (0, 0))
    out_spec = pl.BlockSpec((dests, total, width), lambda j: (j, 0, 0))
    return pl.pallas_call(
        pack_kernel,
        grid=(group_size // dests,),
        in_specs=[
            pl.BlockSpec((dests * far_count, 1), lambda j: (j, 0)),
            pl.BlockSpec((dests * own_count, 1), lambda j: (j, 0)),
            source_spec,
            source_spec,
            source_spec,
        ],
        out_specs=[out_spec] * chunks,
        out_shape=[jax.ShapeDtypeStruct((group_size, total, width), query_feats.dtype)] * chunks,
        interpret=INTERPRET,
    )(far_rows.reshape(-1, 1), own_rows.reshape(-1, 1), query_feats, key_feats, value_feats)


def unpack_kernel(index_ref, part_ref, prior_ref, out_ref):
    del prior_ref
    count, rows = index_ref.shape[0], part_ref.shape[0]
    iota = lax.broadcasted_iota(jnp.int32, (count, rows), 1)
    hot = jnp.where(index_ref[...] == iota, 1.0, 0.0).astype(jnp.bfloat16)
    picked = jnp.dot(hot, part_ref[...], preferred_element_type=jnp.float32)
    out_ref[...] = picked.astype(out_ref.dtype)


def unpack(index, part, prior, column_block):
    rows, width = part.shape
    return pl.pallas_call(
        unpack_kernel,
        grid=(1,),
        in_specs=[
            pl.BlockSpec((rows, 1), lambda i: (0, 0)),
            pl.BlockSpec((rows, width), lambda i: (0, 0)),
            pl.BlockSpec((rows, width), lambda i: (0, column_block)),
        ],
        out_specs=pl.BlockSpec((rows, width), lambda i: (0, column_block)),
        out_shape=jax.ShapeDtypeStruct(prior.shape, prior.dtype),
        input_output_aliases={2: 0},
        interpret=INTERPRET,
    )(index.reshape(-1, 1), part, prior)


def class_of(devices, frame_devs):
    return devices // frame_devs // 4 * frame_devs + devices % frame_devs


def ranked_pick(candidates, wanted, slot_count):
    rank = jnp.cumsum(wanted.astype(jnp.int32), axis=-1) - 1
    slots = jnp.arange(slot_count, dtype=jnp.int32)
    hit = wanted[..., None] & (rank[..., None] == slots)
    picked = jnp.sum(jnp.where(hit, candidates[..., None], 0), axis=-2)
    return picked, jnp.any(hit, axis=-2)


def shards(query_feats, key_feats, value_feats, owner_map, pattern):
    group_size = lax.axis_size("seq")
    device = lax.axis_index("seq")
    local_rows, channels = query_feats.shape
    strips = local_rows // (4 * WIDTH)
    blocks = WIDTH // 4
    piece_count = strips * blocks
    tile_count = owner_map.shape[0]
    own_count = tile_count // group_size
    capacity = (piece_count + group_size - 1) // group_size
    unit = capacity * 16
    frame_devs = group_size // FRAMES
    devices = jnp.arange(group_size, dtype=jnp.int32)
    local_iota = jnp.arange(piece_count, dtype=jnp.int32)
    cap_iota = jnp.arange(capacity, dtype=jnp.int32)
    slice_iota = jnp.arange(4, dtype=jnp.int32)
    token_iota = jnp.arange(16, dtype=jnp.int32)

    def piece_rows(pieces):
        strip = pieces // blocks
        column = pieces % blocks
        return (
            strip[..., None] * (4 * WIDTH)
            + (token_iota // 4) * WIDTH
            + column[..., None] * 4
            + token_iota % 4
        )

    own_rank, class_rank = owner_tables(owner_map, group_size, piece_count)
    my_class = class_of(device, frame_devs)
    my_tiles = my_class * piece_count + local_iota
    my_owner = lax.dynamic_slice_in_dim(owner_map, my_class * piece_count, piece_count)
    my_slot = lax.dynamic_slice_in_dim(class_rank, my_class * piece_count, piece_count)
    send_hit = (my_owner[None, None, :] == devices[:, None, None]) & (
        my_slot[None, None, :] == cap_iota[None, :, None]
    )
    send_index = jnp.sum(jnp.where(send_hit, local_iota[None, None, :], 0), axis=2)
    own_send_rows = piece_rows(send_index).reshape(group_size, unit)
    requests = request_table(owner_map, pattern, group_size)
    wanted = (requests >= 0) & (requests // piece_count == my_class)
    far_send_piece, _ = ranked_pick(requests % piece_count, wanted, FAR_SLOTS)
    far_send_rows = piece_rows(far_send_piece).reshape(group_size, FAR_SLOTS * 16)
    source_class = class_of(devices, frame_devs)
    class_tiles = source_class[:, None] * piece_count + local_iota[None, :]
    class_count = tile_count // piece_count
    mine = pick_rows(owner_map.reshape(class_count, piece_count), source_class) == device
    near_hit = mine[:, None, :] & (
        pick_rows(class_rank.reshape(class_count, piece_count), source_class)[:, None, :]
        == cap_iota[None, :, None]
    )
    near_tile = jnp.sum(jnp.where(near_hit, class_tiles[:, None, :], 0), axis=2)
    near_tile_rows = jnp.broadcast_to(near_tile[:, :, None], (group_size, capacity, 16)).reshape(-1)
    my_requests = lax.dynamic_index_in_dim(requests, device, axis=0, keepdims=False)
    far_wanted = (my_requests[None, :] >= 0) & (
        my_requests[None, :] // piece_count == source_class[:, None]
    )
    far_tile, far_valid = ranked_pick(
        jnp.broadcast_to(my_requests[None, :], (group_size, group_size)), far_wanted, FAR_SLOTS
    )
    far_tile = jnp.where(far_valid, far_tile, -1)
    far_tile_rows = jnp.broadcast_to(
        far_tile[:, :, None], (group_size, FAR_SLOTS, 16)
    ).reshape(-1)
    own_ids = owned_tiles(owner_map, own_rank, device, own_count)
    listed = pick_rows(pattern, own_ids)
    near_ok = jnp.any(listed[:, :, None] == near_tile_rows[None, None, :], axis=1)
    far_ok = jnp.any(listed[:, :, None] == far_tile_rows[None, None, :], axis=1)
    query_own = pick(own_rank, near_tile_rows)
    near_bias = jnp.where(jnp.take(near_ok, query_own, axis=0, mode="clip"), 0.0, masked_score)
    far_bias = jnp.where(jnp.take(far_ok, query_own, axis=0, mode="clip"), 0.0, masked_score)
    near_bias = near_bias.astype(jnp.float32)
    far_bias = far_bias.astype(jnp.float32)
    chunk_width = channels // HEAD_CHUNKS
    outputs = []
    logs = []
    packed = pack(far_send_rows, own_send_rows, query_feats, key_feats, value_feats, HEAD_CHUNKS)
    for chunk in range(HEAD_CHUNKS):
        sent = packed[chunk]
        got = lax.all_to_all(sent, "seq", split_axis=0, concat_axis=0, tiled=True)
        mixed, head_logs = attend(got, unit, near_bias, far_bias)
        returned = lax.all_to_all(mixed, "seq", split_axis=0, concat_axis=0, tiled=True)
        outputs.append(returned.reshape(-1, chunk_width))
        logs.append(head_logs[:, :, 0])
    head_logs = jnp.concatenate(logs, axis=0)
    own_class = own_ids // piece_count
    own_slot = pick(class_rank, own_ids)
    gather_rows = (
        supplier_of(own_class[:, None], slice_iota[None, :], frame_devs) * capacity
        + own_slot[:, None]
    )
    log_rows = (gather_rows[:, :, None] * 16 + token_iota).reshape(-1)
    heads = channels // HEAD_DIM
    log_sums = (
        jnp.take(head_logs, log_rows, axis=1, mode="clip")
        .reshape(heads, own_count, 64)
        .transpose(1, 0, 2)
        .reshape(1, own_count, heads * 64)
    )
    local_iota_rows = jnp.arange(local_rows, dtype=jnp.int32)
    strip = local_iota_rows // (4 * WIDTH)
    height = local_iota_rows % (4 * WIDTH) // WIDTH
    column = local_iota_rows % WIDTH
    piece = strip * blocks + column // 4
    token = height * 4 + column % 4
    back_rows = (pick(my_owner, piece) * capacity + pick(my_slot, piece)) * 16 + token
    attended = jnp.zeros((local_rows, channels), jnp.bfloat16)
    for chunk, part in enumerate(outputs):
        attended = unpack(back_rows, part, attended, chunk)
    return (attended, log_sums)


def solution(mesh):
    placed = (
        P(("groups", "seq"), None),
        P(("groups", "seq"), None),
        P(("groups", "seq"), None),
        P("groups"),
        P("groups", None),
    )
    return jax.shard_map(
        shards,
        mesh=mesh,
        in_specs=placed,
        out_specs=(P(("groups", "seq"), None), P(("groups", "seq"), None, None)),
        check_vma=False,
    )
```
